128 devices in a mesh: leaf: 32 (over x, y, core), probe: 4 (over z).
Axes of the slice: x: 4, y: 4, z: 4, core: 2. Of those that a mesh axis runs over, the one named last changes fastest.
Arguments:
- child_updates: bfloat16 [1024, 512, 512], P('leaf'), may hold values from -0.25 to 0.25
- child_probes: bfloat16 [256, 524288], P('probe', 'leaf'), may hold values from -6 to 6
- child_dest: int32 [4096, 1], P('leaf'), may hold values from 0 to 31; in each aligned block of 128 rows (0 to 127, 128 to 255, ...) at most 8 rows name the same one
- child_rows: int32 [4096, 128], P('leaf'), may hold values from 0 to 2047
- parent_blocks: bfloat16 [2048, 128, 128], P('leaf'), may hold values from -0.5 to 0.5
- coupling: int32 [2048, 2], P('leaf'), may hold values from 0 to 15
- parent_probes: bfloat16 [256, 65536], P('probe', 'leaf'), may hold values from -6 to 6
- sketch: float32 [256, 128], P('probe'), may hold values from -0.375 to 0.375
- rank_one: int32 [32], P('leaf'), may hold values from 96 to 128, as said below
- rank_two: int32 [16], replicated, may hold values from 96 to 128, as said below
- rank_three: int32 [8], replicated, may hold values from 96 to 128, as said below
Outputs:
- basis_one: float32 [65536, 128], P(('leaf', 'probe'))
- basis_two: float32 [4096, 128], P('leaf')
- basis_three: float32 [4096, 128], P('leaf')
- top_sample: float32 [256, 4096], P('probe', 'leaf')
The draws below stay inside these ranges and needn't reach their ends.
Inputs may be any that keep to these rules, and one draw needn't show every extreme that they name: `child_dest`: among the row blocks of one front group, no parent front is named by more than 8 blocks, and some parent front is named by exactly 8. `rank_one`: one node has rank 128. `rank_two`: one node has rank 128. `rank_three`: one node has rank 128.
All inputs are finite; a program needn't handle non-finite values.
Results may differ from the reference program's by a relative error of at most 0.0065.
Values may be sent and summed in bfloat16 or wider, within the bound.
No kernel may reach another device: no remote copies, remote signals or barrier semaphores. Data moves between devices by JAX's collectives and lax.ppermute only.
A program may use at most 192 MiB of HBM per device.

```python
import math
import jax
import jax.numpy as jnp
import numpy as np
from jax import lax

PROBES = 256
RANK = 128
RB = 128
CB = 512
PF = 2048
NZB = 64
CH = 32
FRONTS = 32
PAIRS = 16
QUADS = 8
CHB = 128
CAP = 8
PB = 16
CHILDREN = 1024


def rank_draw(key, count):
    values = jax.random.randint(key, (count,), 3 * RANK // 4, RANK + 1)
    place = jax.random.randint(jax.random.fold_in(key, 7), (), 0, count)
    return values.at[place].set(RANK).astype(jnp.int32)


def draw_rank_one(key, part):
    return rank_draw(jax.random.fold_in(key, 11), FRONTS)


def draw_rank_two(key, part):
    return rank_draw(jax.random.fold_in(key, 13), PAIRS)


def draw_rank_three(key, part):
    return rank_draw(jax.random.fold_in(key, 17), QUADS)


def set_ends(values, key, least, top_value):
    extent = values.shape
    spot = [jax.random.randint(jax.random.fold_in(key, axis), (), 0, extent[axis]) for axis in range(len(extent))]
    values = values.at[tuple(spot)].set(least)
    longest = extent.index(max(extent))
    spot[longest] = (spot[longest] + 1) % extent[longest]
    return values.at[tuple(spot)].set(top_value)


def steps_of(own_key, extent, cuts, low, high):
    gain = 1.0
    for axis_at, shards_of in cuts:
        draws = jax.random.uniform(jax.random.fold_in(jax.random.fold_in(own_key, 6), axis_at), (shards_of,), jnp.float32, low / len(cuts), high / len(cuts))
        gain = gain * jnp.repeat(jnp.exp(draws), extent[axis_at] // shards_of).reshape((-1,) + (1,) * (len(extent) - 1 - axis_at))
    return gain


def routed_block(rng, own, number, rows, amount, top, limit, lean):
    sequence = jax.random.permutation(rng, amount)
    crowded, ordinary = load_shares(amount, rows * top, limit, lean, True), load_shares(amount, rows * top, limit, lean, False)
    places = jnp.arange(amount)

    def named(tallies, turn):
        used = int((tallies > 0).sum())
        fixed = max(1, used // 4)
        moved = fixed + (places - fixed + turn * (used - fixed)) % max(1, amount - fixed)
        return jnp.zeros((amount,), jnp.int32).at[sequence[jnp.where(places < fixed, places, moved)]].set(jnp.asarray(tallies, jnp.int32))

    tallies = jnp.where(number % 4 == 0, named(crowded, number // 4), named(ordinary, number - number // 4 - 1))
    mixed = jax.random.permutation(jax.random.fold_in(own, 3), amount)
    donor, sink = mixed[0:amount // 2 * 2:2], mixed[1:amount // 2 * 2:2]
    room = jnp.minimum(tallies[donor] - 1, limit - tallies[sink]) // 2
    room = jnp.where((donor == sequence[0]) | (sink == sequence[0]) | (tallies[sink] == 0), 0, jnp.maximum(room, 0))
    moved = jax.random.randint(jax.random.fold_in(own, 4), (amount // 2,), 0, 1 << 20) % (room + 1)
    tallies = tallies.at[donor].add(-moved).at[sink].add(moved)
    members = jnp.searchsorted(jnp.cumsum(tallies), jnp.arange(rows * top), side="right").astype(jnp.int32)
    grid = members.reshape(top, rows).T
    grid = grid[jax.random.permutation(jax.random.fold_in(own, 1), rows)]
    turn = jax.random.randint(jax.random.fold_in(own, 2), (rows, 1), 0, top)
    return jnp.take_along_axis(grid, (jnp.arange(top)[None, :] + turn) % top, axis=1)


def load_shares(number_of, total, limit, slope, full):
    weights = [(1 << 20) // math.isqrt(standing ** slope) + 1 for standing in range(1, number_of + 1)]
    largest = limit if full else min(limit, max(-(-total // number_of), total * weights[0] // sum(weights)))
    least = 1 if total - largest >= number_of - 1 else 0
    holding, surplus = [largest] + [least] * (number_of - 1), total - largest - least * (number_of - 1)
    while surplus > 0:
        candidates = [i for i in range(1, number_of) if holding[i] < largest] or [i for i in range(1, number_of) if holding[i] < limit]
        mass, left = sum([weights[i] for i in candidates]), surplus
        for i in candidates:
            more = min(limit - holding[i], max(1, left * weights[i] // mass), surplus)
            holding[i] = holding[i] + more
            surplus = surplus - more
    return np.array(holding)


def bell_draw(rng, extent, deviation, limit, split=(), kind=jnp.bfloat16):
    array = jax.random.normal(rng, extent, jnp.float32) * deviation
    if len(split) > 0:
        array = steps_of(rng, extent, split, -0.22, 0.18) * array
    return jnp.clip(array, min=-limit, max=limit).astype(kind)


def setup_inputs(seed: int = 0) -> dict:
    arg_keys = jax.random.split(jax.random.key(seed), 12)
    child_updates = bell_draw(arg_keys[0], (CHILDREN, CB, CB), CB ** -0.5, 0.25, ((0, 32),))
    child_probes = bell_draw(arg_keys[1], (PROBES, CHILDREN * CB), 1.0, 6.0, ((0, 4), (1, 32)))
    child_dest_keys = jax.random.split(jax.random.fold_in(arg_keys[2], 1), (FRONTS * CHB) // CHB)
    child_dest_turns = jax.random.permutation(jax.random.fold_in(arg_keys[2], 3), (FRONTS * CHB) // CHB)
    child_dest = jax.vmap(lambda own, number: routed_block(jax.random.fold_in(arg_keys[2], 2), own, number, CHB, FRONTS, 1, CAP, 2))(child_dest_keys, child_dest_turns).reshape((FRONTS * CHB, 1))
    child_rows = set_ends(jax.random.randint(arg_keys[3], (FRONTS * CHB, RB), 0, PF), jax.random.fold_in(arg_keys[3], 1), 0, PF - 1).astype(jnp.int32)
    parent_blocks = bell_draw(arg_keys[4], (FRONTS * NZB, RB, RB), RB ** -0.5, 0.5, ((0, 32),))
    coupling = set_ends(jax.random.randint(arg_keys[5], (FRONTS * NZB, 2), 0, PB), jax.random.fold_in(arg_keys[5], 1), 0, PB - 1).astype(jnp.int32)
    parent_probes = bell_draw(arg_keys[6], (PROBES, FRONTS * PF), 1.0, 6.0, ((0, 4), (1, 32)))
    sketch = bell_draw(arg_keys[7], (PROBES, RANK), PROBES ** -0.5, 0.375, ((0, 4),), jnp.float32)
    rank_one = draw_rank_one(jax.random.fold_in(arg_keys[11], 71), 0)
    rank_two = draw_rank_two(jax.random.fold_in(arg_keys[11], 71), 0)
    rank_three = draw_rank_three(jax.random.fold_in(arg_keys[11], 71), 0)
    return dict(child_updates=child_updates, child_probes=child_probes, child_dest=child_dest, child_rows=child_rows, parent_blocks=parent_blocks, coupling=coupling, parent_probes=parent_probes, sketch=sketch, rank_one=rank_one, rank_two=rank_two, rank_three=rank_three)


highest = lax.Precision.HIGHEST

def chol_basis(sketched, rank_limit):
    gram_matrix = jnp.dot(sketched.T, sketched, precision=highest)
    factor = jnp.linalg.cholesky(gram_matrix)
    orthonormal = lax.linalg.triangular_solve(factor, sketched, left_side=False, lower=True, transpose_a=True)
    columns = jnp.arange(sketched.shape[1], dtype=jnp.int32)
    return jnp.where(columns[None, :] < rank_limit, orthonormal, jnp.zeros_like(orthonormal))

def merge_level(samples, sketch, ranks):
    stacked = jnp.concatenate([samples[0::2], samples[1::2]], axis=2)
    sketched = jnp.einsum('npr,ps->nrs', stacked, sketch, precision=highest)
    merged = jax.vmap(chol_basis)(sketched, ranks)
    passed = jnp.einsum('npr,nrs->nps', stacked, merged, precision=highest)
    return (merged, passed)

def reference(child_updates, child_probes, child_dest, child_rows, parent_blocks, coupling, parent_probes, sketch, rank_one, rank_two, rank_three):
    fronts_all = rank_one.shape[0]
    updates = child_updates.reshape(fronts_all, CH, CB // RB, RB, CB)
    probes_kids = child_probes.reshape(PROBES, fronts_all, CH, CB)
    targets = child_dest.reshape(fronts_all, CHB)
    row_maps = child_rows.reshape(fronts_all, CHB, RB)

    def add_group(extended, group):
        probe_block = lax.dynamic_index_in_dim(probes_kids, group, 1, keepdims=False).astype(jnp.float32)
        update_block = lax.dynamic_index_in_dim(updates, group, 0, keepdims=False).astype(jnp.float32)
        sampled = jnp.einsum('pck,cbik->cbpi', probe_block, update_block).astype(jnp.bfloat16)
        sampled = sampled.reshape(CHB, PROBES, RB)
        target_rows = lax.dynamic_index_in_dim(targets, group, 0, keepdims=False)
        local_rows = lax.dynamic_index_in_dim(row_maps, group, 0, keepdims=False)
        global_rows = (target_rows[:, None] * PF + local_rows).reshape(-1)
        values = jnp.moveaxis(sampled, 1, 0).reshape(PROBES, CHB * RB).astype(jnp.float32)
        return (extended.at[:, global_rows].add(values), None)
    extended, _ = lax.scan(add_group, jnp.zeros((PROBES, fronts_all * PF), jnp.float32), jnp.arange(fronts_all, dtype=jnp.int32))
    blocks_all = parent_blocks.reshape(fronts_all, NZB, RB, RB)
    pattern = coupling.reshape(fronts_all, NZB, 2)
    probes_front = jnp.moveaxis(parent_probes.reshape(PROBES, fronts_all, PB, RB), 1, 0)

    def one_front(inputs):
        block_set, pattern_set, probe_set = inputs
        picked = jnp.take(probe_set, pattern_set[:, 1], axis=1).astype(jnp.float32)
        product = jnp.einsum('eik,pek->pei', block_set.astype(jnp.float32), picked)
        initial = jnp.zeros((PROBES, PB, RB), jnp.float32).at[:, pattern_set[:, 0]].add(product)
        return initial.reshape(PROBES, PF)
    initial_all = lax.map(one_front, (blocks_all, pattern, probes_front))
    sample_all = initial_all + jnp.moveaxis(extended.reshape(PROBES, fronts_all, PF), 1, 0)

    def level_one(sample_front, rank_limit):
        sketched = jnp.einsum('pr,ps->rs', sample_front, sketch, precision=highest)
        basis_front = chol_basis(sketched, rank_limit)
        return (basis_front, jnp.dot(sample_front, basis_front, precision=highest))
    basis_all, passed_one = jax.vmap(level_one)(sample_all, rank_one)
    merged_two, passed_two = merge_level(passed_one, sketch, rank_two)
    merged_three, passed_three = merge_level(passed_two, sketch, rank_three)
    basis_one = basis_all.reshape(fronts_all * PF, RANK)
    basis_two = merged_two.reshape(fronts_all * RANK, RANK)
    basis_three = jnp.repeat(merged_three.reshape(fronts_all // 2, RANK, RANK), 2, axis=0).reshape(fronts_all * RANK, RANK)
    top_sample = jnp.moveaxis(jnp.repeat(passed_three, 4, axis=0), 0, 1).reshape(PROBES, fronts_all * RANK)
    return (basis_one, basis_two, basis_three, top_sample)
```

```python
import jax
import jax.numpy as jnp
from jax import lax
from jax.sharding import PartitionSpec as P

highest = lax.Precision.HIGHEST

SLOT_CAP = 8


def partner_2(block, axis, stride):
    count = lax.axis_size(axis)
    route = []
    for low in range(count):
        high = low | 1 << stride
        if high != low and high < count:
            route += [(low, high), (high, low)]
    return lax.ppermute(block, axis, route)


def butterfly_sum(block, axis):
    count = lax.axis_size(axis)
    stride = 0
    while 1 << stride < count:
        block = block + partner_2(block, axis, stride)
        stride += 1
    return block


def gather_rows(block, axis):
    count = lax.axis_size(axis)
    index = lax.axis_index(axis)
    pieces = [block]
    for shift in range(1, count):
        route = [(j, (j + shift) % count) for j in range(count)]
        pieces.append(lax.ppermute(block, axis, route))
    stacked = jnp.stack(pieces)
    order = (index - jnp.arange(count, dtype=jnp.int32)) % count
    stacked = jnp.take(stacked, order, axis=0)
    return stacked.reshape((count * block.shape[0],) + block.shape[1:])


def basis_from_gram(sketched, gram_matrix, rank_limit):
    factor = jnp.linalg.cholesky(gram_matrix)
    orthonormal = lax.linalg.triangular_solve(
        factor, sketched, left_side=False, lower=True, transpose_a=True
    )
    columns = jnp.arange(sketched.shape[1], dtype=jnp.int32)
    return jnp.where(columns[None, :] < rank_limit, orthonormal, jnp.zeros_like(orthonormal))


def chol_basis(sketched, rank_limit):
    gram_matrix = jnp.einsum("ra,rb->ab", sketched, sketched, precision=highest)
    return basis_from_gram(sketched, gram_matrix, rank_limit)


def merge_level(own, partner, low_side, sketch_all, rank_limit):
    stacked = jnp.where(
        low_side,
        jnp.concatenate([own, partner], 1),
        jnp.concatenate([partner, own], 1),
    )
    sketched = jnp.einsum("pr,ps->rs", stacked, sketch_all, precision=highest)
    merged = chol_basis(sketched, rank_limit)
    return merged, jnp.dot(stacked, merged, precision=highest)


def on_device(
    child_updates,
    child_probes,
    child_dest,
    child_rows,
    parent_blocks,
    coupling,
    parent_probes,
    sketch,
    rank_one,
    rank_two,
    rank_three,
):
    leaf_count = lax.axis_size("leaf")
    probe_count = lax.axis_size("probe")
    leaf_index = lax.axis_index("leaf")
    probe_index = lax.axis_index("probe")
    local_probes = child_probes.shape[0]
    kid_count = child_updates.shape[0]
    kid_order = child_updates.shape[1]
    block_rows = child_rows.shape[1]
    block_count = child_rows.shape[0]
    front_rows = parent_probes.shape[1]
    rank_width = sketch.shape[1]

    updates = child_updates.reshape(kid_count, kid_order // block_rows, block_rows, kid_order)
    probe_cut = child_probes.reshape(local_probes, kid_count, kid_order)
    sampled = jnp.einsum("pck,cbik->cbpi", probe_cut, updates, preferred_element_type=jnp.float32)
    sampled = sampled.astype(jnp.bfloat16).reshape(block_count, local_probes, block_rows)

    targets = child_dest[:, 0]
    named = (targets[:, None] == jnp.arange(leaf_count, dtype=jnp.int32)[None, :]).astype(jnp.int32)
    earlier = jnp.cumsum(named, axis=0) - named
    slot = jnp.sum(earlier * named, axis=1)
    place = targets * SLOT_CAP + slot
    slot_count = leaf_count * SLOT_CAP
    source = jnp.full((slot_count,), block_count, jnp.int32).at[place].set(
        jnp.arange(block_count, dtype=jnp.int32)
    )
    padded_vals = jnp.concatenate([sampled, jnp.zeros((1, local_probes, block_rows), jnp.bfloat16)])
    padded_rows = jnp.concatenate([child_rows, jnp.zeros((1, block_rows), jnp.int32)])
    send_vals = jnp.take(padded_vals, source, axis=0)
    send_rows = jnp.take(padded_rows, source, axis=0)
    recv_vals = lax.all_to_all(send_vals, "leaf", 0, 0, tiled=True)
    recv_rows = lax.all_to_all(send_rows, "leaf", 0, 0, tiled=True)

    hot = (recv_rows[:, :, None] == jnp.arange(front_rows, dtype=jnp.int32)[None, None, :]).astype(
        jnp.bfloat16
    )
    extended = jnp.einsum("spi,sir->pr", recv_vals, hot, preferred_element_type=jnp.float32)

    pieces = parent_probes.reshape(local_probes, front_rows // block_rows, block_rows)
    picked = jnp.take(pieces, coupling[:, 1], axis=1)
    product = jnp.einsum("eik,pek->pei", parent_blocks, picked, preferred_element_type=jnp.float32)
    initial = (
        jnp.zeros(pieces.shape, jnp.float32)
        .at[:, coupling[:, 0]]
        .add(product)
        .reshape(local_probes, front_rows)
    )
    sample = initial + extended

    share_rows = front_rows // probe_count
    sketch_all = gather_rows(sketch, "probe")
    share_sample = lax.all_to_all(
        sample.reshape(local_probes, probe_count, share_rows), "probe", 1, 0, tiled=True
    ).reshape(local_probes * probe_count, share_rows)
    share_sketched = jnp.einsum("pr,ps->rs", share_sample, sketch_all, precision=highest)
    gram_one = butterfly_sum(
        jnp.einsum("ra,rb->ab", share_sketched, share_sketched, precision=highest), "probe"
    )
    own_basis = basis_from_gram(share_sketched, gram_one, rank_one[0])
    passed_one = butterfly_sum(jnp.dot(share_sample, own_basis, precision=highest), "probe")

    pair_bit = leaf_index % 2
    merged_two, passed_two = merge_level(
        passed_one, partner_2(passed_one, "leaf", 0), pair_bit == 0, sketch_all, rank_two[leaf_index // 2]
    )
    quad_bit = leaf_index // 2 % 2
    merged_three, passed_three = merge_level(
        passed_two, partner_2(passed_two, "leaf", 1), quad_bit == 0, sketch_all, rank_three[leaf_index // 4]
    )
    basis_two = lax.dynamic_slice_in_dim(merged_two, pair_bit * rank_width, rank_width, 0)
    basis_three = lax.dynamic_slice_in_dim(merged_three, quad_bit * rank_width, rank_width, 0)
    top = lax.dynamic_slice_in_dim(passed_three, probe_index * local_probes, local_probes, 0)
    return (own_basis, basis_two, basis_three, top)


def solution(mesh):
    return jax.shard_map(
        on_device,
        mesh=mesh,
        in_specs=(
            P("leaf", None, None),
            P("probe", "leaf"),
            P("leaf", None),
            P("leaf", None),
            P("leaf", None, None),
            P("leaf", None),
            P("probe", "leaf"),
            P("probe", None),
            P("leaf"),
            P(),
            P(),
        ),
        out_specs=(
            P(("leaf", "probe"), None),
            P("leaf", None),
            P("leaf", None),
            P("probe", "leaf"),
        ),
        check_vma=False,
    )
```

```python
import jax
import jax.numpy as jnp
from jax import lax
from jax.experimental import pallas as pl
from jax.experimental.pallas import tpu as pltpu
from jax.sharding import PartitionSpec as P

highest = lax.Precision.HIGHEST

SLOT_CAP = 8


def partner_2(block, axis, stride):
    count = lax.axis_size(axis)
    route = []
    for low in range(count):
        high = low | 1 << stride
        if high != low and high < count:
            route += [(low, high), (high, low)]
    return lax.ppermute(block, axis, route)


def butterfly_sum(block, axis):
    count = lax.axis_size(axis)
    stride = 0
    while 1 << stride < count:
        block = block + partner_2(block, axis, stride)
        stride += 1
    return block


def gather_rows(block, axis):
    count = lax.axis_size(axis)
    index = lax.axis_index(axis)
    pieces = [block]
    for shift in range(1, count):
        route = [(j, (j + shift) % count) for j in range(count)]
        pieces.append(lax.ppermute(block, axis, route))
    stacked = jnp.stack(pieces)
    order = (index - jnp.arange(count, dtype=jnp.int32)) % count
    stacked = jnp.take(stacked, order, axis=0)
    return stacked.reshape((count * block.shape[0],) + block.shape[1:])


def extend_add_kernel(count_ref, rows_ref, vals_ref, out_ref):
    source = pl.program_id(0)

    @pl.when(source == 0)
    def _():
        out_ref[...] = jnp.zeros_like(out_ref)

    def add_pair(pair, carry):
        targets = rows_ref[pair]
        hot = lax.broadcasted_iota(jnp.int32, (out_ref.shape[0], targets.shape[1]), 0) == targets
        out_ref[...] += jnp.dot(
            hot.astype(jnp.bfloat16), vals_ref[pair], preferred_element_type=jnp.float32
        )
        return carry

    lax.fori_loop(0, (count_ref[source] + 1) // 2, add_pair, 0)


def extend_add(recv_vals, recv_rows, sources, front_rows):
    slot_count, block_rows, probes = recv_vals.shape
    pair_count = slot_count // 2
    per_source = pair_count // sources
    counts = jnp.sum((recv_rows[:, 0] >= 0).astype(jnp.int32).reshape(sources, -1), axis=1)
    rows = recv_rows.reshape(pair_count, 1, 2 * block_rows)
    vals = recv_vals.reshape(pair_count, 2 * block_rows, probes)
    return pl.pallas_call(
        extend_add_kernel,
        grid_spec=pltpu.PrefetchScalarGridSpec(
            num_scalar_prefetch=1,
            grid=(sources,),
            in_specs=[
                pl.BlockSpec((per_source, 1, 2 * block_rows), lambda s, c: (s, 0, 0)),
                pl.BlockSpec((per_source, 2 * block_rows, probes), lambda s, c: (s, 0, 0)),
            ],
            out_specs=pl.BlockSpec((front_rows, probes), lambda s, c: (0, 0)),
        ),
        out_shape=jax.ShapeDtypeStruct((front_rows, probes), jnp.float32),
        compiler_params=pltpu.CompilerParams(dimension_semantics=("arbitrary",)),
    )(counts, rows, vals)


def basis_from_gram(sketched, gram_matrix, rank_limit):
    factor = jnp.linalg.cholesky(gram_matrix)
    orthonormal = lax.linalg.triangular_solve(
        factor, sketched, left_side=False, lower=True, transpose_a=True
    )
    columns = jnp.arange(sketched.shape[1], dtype=jnp.int32)
    return jnp.where(columns[None, :] < rank_limit, orthonormal, jnp.zeros_like(orthonormal))


def chol_basis(sketched, rank_limit):
    gram_matrix = jnp.einsum("ra,rb->ab", sketched, sketched, precision=highest)
    return basis_from_gram(sketched, gram_matrix, rank_limit)


def merge_level(own, partner, low_side, sketch_all, rank_limit):
    stacked = jnp.where(
        low_side,
        jnp.concatenate([own, partner], 1),
        jnp.concatenate([partner, own], 1),
    )
    sketched = jnp.einsum("pr,ps->rs", stacked, sketch_all, precision=highest)
    merged = chol_basis(sketched, rank_limit)
    return merged, jnp.dot(stacked, merged, precision=highest)


def on_device(
    child_updates,
    child_probes,
    child_dest,
    child_rows,
    parent_blocks,
    coupling,
    parent_probes,
    sketch,
    rank_one,
    rank_two,
    rank_three,
):
    leaf_count = lax.axis_size("leaf")
    probe_count = lax.axis_size("probe")
    leaf_index = lax.axis_index("leaf")
    probe_index = lax.axis_index("probe")
    local_probes = child_probes.shape[0]
    kid_count = child_updates.shape[0]
    kid_order = child_updates.shape[1]
    block_rows = child_rows.shape[1]
    block_count = child_rows.shape[0]
    front_rows = parent_probes.shape[1]
    rank_width = sketch.shape[1]

    updates = child_updates.reshape(kid_count, kid_order // block_rows, block_rows, kid_order)
    probe_cut = child_probes.reshape(local_probes, kid_count, kid_order)
    sampled = jnp.einsum("pck,cbik->cbip", probe_cut, updates, preferred_element_type=jnp.float32)
    sampled = sampled.astype(jnp.bfloat16).reshape(block_count, block_rows, local_probes)

    targets = child_dest[:, 0]
    named = (targets[:, None] == jnp.arange(leaf_count, dtype=jnp.int32)[None, :]).astype(jnp.int32)
    earlier = jnp.cumsum(named, axis=0) - named
    slot = jnp.sum(earlier * named, axis=1)
    place = targets * SLOT_CAP + slot
    slot_count = leaf_count * SLOT_CAP
    source = jnp.full((slot_count,), block_count, jnp.int32).at[place].set(
        jnp.arange(block_count, dtype=jnp.int32)
    )
    padded_vals = jnp.concatenate([sampled, jnp.zeros((1, block_rows, local_probes), jnp.bfloat16)])
    padded_rows = jnp.concatenate([child_rows, jnp.full((1, block_rows), -1, jnp.int32)])
    send_vals = jnp.take(padded_vals, source, axis=0)
    send_rows = jnp.take(padded_rows, source, axis=0)
    recv_vals = lax.all_to_all(send_vals, "leaf", 0, 0, tiled=True)
    recv_rows = lax.all_to_all(send_rows, "leaf", 0, 0, tiled=True)

    extended = extend_add(recv_vals, recv_rows, leaf_count, front_rows).T

    pieces = parent_probes.reshape(local_probes, front_rows // block_rows, block_rows)
    picked = jnp.take(pieces, coupling[:, 1], axis=1)
    product = jnp.einsum("eik,pek->pei", parent_blocks, picked, preferred_element_type=jnp.float32)
    initial = (
        jnp.zeros(pieces.shape, jnp.float32)
        .at[:, coupling[:, 0]]
        .add(product)
        .reshape(local_probes, front_rows)
    )
    sample = initial + extended

    share_rows = front_rows // probe_count
    sketch_all = gather_rows(sketch, "probe")
    share_sample = lax.all_to_all(
        sample.reshape(local_probes, probe_count, share_rows), "probe", 1, 0, tiled=True
    ).reshape(local_probes * probe_count, share_rows)
    share_sketched = jnp.einsum("pr,ps->rs", share_sample, sketch_all, precision=highest)
    gram_one = butterfly_sum(
        jnp.einsum("ra,rb->ab", share_sketched, share_sketched, precision=highest), "probe"
    )
    own_basis = basis_from_gram(share_sketched, gram_one, rank_one[0])
    passed_one = butterfly_sum(jnp.dot(share_sample, own_basis, precision=highest), "probe")

    pair_bit = leaf_index % 2
    merged_two, passed_two = merge_level(
        passed_one, partner_2(passed_one, "leaf", 0), pair_bit == 0, sketch_all, rank_two[leaf_index // 2]
    )
    quad_bit = leaf_index // 2 % 2
    merged_three, passed_three = merge_level(
        passed_two, partner_2(passed_two, "leaf", 1), quad_bit == 0, sketch_all, rank_three[leaf_index // 4]
    )
    basis_two = lax.dynamic_slice_in_dim(merged_two, pair_bit * rank_width, rank_width, 0)
    basis_three = lax.dynamic_slice_in_dim(merged_three, quad_bit * rank_width, rank_width, 0)
    top = lax.dynamic_slice_in_dim(passed_three, probe_index * local_probes, local_probes, 0)
    return (own_basis, basis_two, basis_three, top)


def solution(mesh):
    return jax.shard_map(
        on_device,
        mesh=mesh,
        in_specs=(
            P("leaf", None, None),
            P("probe", "leaf"),
            P("leaf", None),
            P("leaf", None),
            P("leaf", None, None),
            P("leaf", None),
            P("probe", "leaf"),
            P("probe", None),
            P("leaf"),
            P(),
            P(),
        ),
        out_specs=(
            P(("leaf", "probe"), None),
            P("leaf", None),
            P("leaf", None),
            P("probe", "leaf"),
        ),
        check_vma=False,
    )
```

```python
import jax
import jax.numpy as jnp
from jax import lax
from jax.experimental import pallas as pl
from jax.experimental.pallas import tpu as pltpu
from jax.sharding import PartitionSpec as P

highest = lax.Precision.HIGHEST

SLOT_CAP = 8


def partner_2(block, axis, stride):
    count = lax.axis_size(axis)
    route = []
    for low in range(count):
        high = low | 1 << stride
        if high != low and high < count:
            route += [(low, high), (high, low)]
    return lax.ppermute(block, axis, route)


def butterfly_sum(block, axis):
    count = lax.axis_size(axis)
    stride = 0
    while 1 << stride < count:
        block = block + partner_2(block, axis, stride)
        stride += 1
    return block


def gather_rows(block, axis):
    count = lax.axis_size(axis)
    index = lax.axis_index(axis)
    pieces = [block]
    for shift in range(1, count):
        route = [(j, (j + shift) % count) for j in range(count)]
        pieces.append(lax.ppermute(block, axis, route))
    stacked = jnp.stack(pieces)
    order = (index - jnp.arange(count, dtype=jnp.int32)) % count
    stacked = jnp.take(stacked, order, axis=0)
    return stacked.reshape((count * block.shape[0],) + block.shape[1:])


def extend_add_kernel(count_ref, rows_ref, vals_ref, out_ref):
    source = pl.program_id(0)
    lanes = rows_ref.shape[1]
    probes = vals_ref.shape[1]
    high_count = out_ref.shape[0] // probes
    group = 8

    @pl.when(source == 0)
    def _():
        out_ref[...] = jnp.zeros_like(out_ref)

    def add_group(step, carry):
        spread, hot = [], []
        for offset in range(group):
            slot = step * group + offset
            targets = rows_ref[pl.ds(slot, 1), :]
            high = targets >> 7
            low = targets & (lanes - 1)
            vals = vals_ref[slot]
            zero = jnp.zeros_like(vals)
            spread.append(
                jnp.concatenate([jnp.where(high == h, vals, zero) for h in range(high_count)], axis=0)
            )
            hot.append(
                (lax.broadcasted_iota(jnp.int32, (lanes, lanes), 0) == low).astype(jnp.bfloat16)
            )
        spread = jnp.concatenate(spread, axis=1)
        hot = jnp.concatenate(hot, axis=1)
        out_ref[...] += lax.dot_general(
            spread, hot, (((1,), (1,)), ((), ())), preferred_element_type=jnp.float32
        )
        return carry

    lax.fori_loop(0, (count_ref[source] + group - 1) // group, add_group, 0)


def extend_add(recv_vals, recv_rows, sources, front_rows):
    slot_count, probes, block_rows = recv_vals.shape
    per_source = slot_count // sources
    high_count = front_rows // block_rows
    counts = jnp.sum((recv_rows[:, 0] >= 0).astype(jnp.int32).reshape(sources, -1), axis=1)
    spread = pl.pallas_call(
        extend_add_kernel,
        grid_spec=pltpu.PrefetchScalarGridSpec(
            num_scalar_prefetch=1,
            grid=(sources,),
            in_specs=[
                pl.BlockSpec((per_source, block_rows), lambda s, c: (s, 0)),
                pl.BlockSpec((per_source, probes, block_rows), lambda s, c: (s, 0, 0)),
            ],
            out_specs=pl.BlockSpec((high_count * probes, block_rows), lambda s, c: (0, 0)),
        ),
        out_shape=jax.ShapeDtypeStruct((high_count * probes, block_rows), jnp.float32),
        compiler_params=pltpu.CompilerParams(dimension_semantics=("arbitrary",)),
    )(counts, recv_rows, recv_vals)
    spread = spread.reshape(high_count, probes, block_rows)
    return jnp.moveaxis(spread, 0, 1).reshape(probes, front_rows)


def basis_from_gram(sketched, gram_matrix, rank_limit):
    factor = jnp.linalg.cholesky(gram_matrix)
    orthonormal = lax.linalg.triangular_solve(
        factor, sketched, left_side=False, lower=True, transpose_a=True
    )
    columns = jnp.arange(sketched.shape[1], dtype=jnp.int32)
    return jnp.where(columns[None, :] < rank_limit, orthonormal, jnp.zeros_like(orthonormal))


def chol_basis(sketched, rank_limit):
    gram_matrix = jnp.einsum("ra,rb->ab", sketched, sketched, precision=highest)
    return basis_from_gram(sketched, gram_matrix, rank_limit)


def merge_level(own, partner, low_side, sketch_all, rank_limit):
    stacked = jnp.where(
        low_side,
        jnp.concatenate([own, partner], 1),
        jnp.concatenate([partner, own], 1),
    )
    sketched = jnp.einsum("pr,ps->rs", stacked, sketch_all, precision=highest)
    merged = chol_basis(sketched, rank_limit)
    return merged, jnp.dot(stacked, merged, precision=highest)


def on_device(
    child_updates,
    child_probes,
    child_dest,
    child_rows,
    parent_blocks,
    coupling,
    parent_probes,
    sketch,
    rank_one,
    rank_two,
    rank_three,
):
    leaf_count = lax.axis_size("leaf")
    probe_count = lax.axis_size("probe")
    leaf_index = lax.axis_index("leaf")
    probe_index = lax.axis_index("probe")
    local_probes = child_probes.shape[0]
    kid_count = child_updates.shape[0]
    kid_order = child_updates.shape[1]
    block_rows = child_rows.shape[1]
    block_count = child_rows.shape[0]
    front_rows = parent_probes.shape[1]
    rank_width = sketch.shape[1]

    updates = child_updates.reshape(kid_count, kid_order // block_rows, block_rows, kid_order)
    probe_cut = child_probes.reshape(local_probes, kid_count, kid_order)
    sampled = jnp.einsum("pck,cbik->cbpi", probe_cut, updates, preferred_element_type=jnp.float32)
    sampled = sampled.astype(jnp.bfloat16).reshape(block_count, local_probes, block_rows)

    targets = child_dest[:, 0]
    named = (targets[:, None] == jnp.arange(leaf_count, dtype=jnp.int32)[None, :]).astype(jnp.int32)
    earlier = jnp.cumsum(named, axis=0) - named
    slot = jnp.sum(earlier * named, axis=1)
    place = targets * SLOT_CAP + slot
    slot_count = leaf_count * SLOT_CAP
    source = jnp.full((slot_count,), block_count, jnp.int32).at[place].set(
        jnp.arange(block_count, dtype=jnp.int32)
    )
    padded_vals = jnp.concatenate([sampled, jnp.zeros((1, local_probes, block_rows), jnp.bfloat16)])
    padded_rows = jnp.concatenate([child_rows, jnp.full((1, block_rows), -1, jnp.int32)])
    send_vals = jnp.take(padded_vals, source, axis=0)
    send_rows = jnp.take(padded_rows, source, axis=0)
    recv_vals = lax.all_to_all(send_vals, "leaf", 0, 0, tiled=True)
    recv_rows = lax.all_to_all(send_rows, "leaf", 0, 0, tiled=True)

    extended = extend_add(recv_vals, recv_rows, leaf_count, front_rows)

    pieces = parent_probes.reshape(local_probes, front_rows // block_rows, block_rows)
    picked = jnp.take(pieces, coupling[:, 1], axis=1)
    product = jnp.einsum("eik,pek->pei", parent_blocks, picked, preferred_element_type=jnp.float32)
    initial = (
        jnp.zeros(pieces.shape, jnp.float32)
        .at[:, coupling[:, 0]]
        .add(product)
        .reshape(local_probes, front_rows)
    )
    sample = initial + extended

    share_rows = front_rows // probe_count
    sketch_all = gather_rows(sketch, "probe")
    share_sample = lax.all_to_all(
        sample.reshape(local_probes, probe_count, share_rows), "probe", 1, 0, tiled=True
    ).reshape(local_probes * probe_count, share_rows)
    share_sketched = jnp.einsum("pr,ps->rs", share_sample, sketch_all, precision=highest)
    gram_one = butterfly_sum(
        jnp.einsum("ra,rb->ab", share_sketched, share_sketched, precision=highest), "probe"
    )
    own_basis = basis_from_gram(share_sketched, gram_one, rank_one[0])
    passed_one = butterfly_sum(jnp.dot(share_sample, own_basis, precision=highest), "probe")

    pair_bit = leaf_index % 2
    merged_two, passed_two = merge_level(
        passed_one, partner_2(passed_one, "leaf", 0), pair_bit == 0, sketch_all, rank_two[leaf_index // 2]
    )
    quad_bit = leaf_index // 2 % 2
    merged_three, passed_three = merge_level(
        passed_two, partner_2(passed_two, "leaf", 1), quad_bit == 0, sketch_all, rank_three[leaf_index // 4]
    )
    basis_two = lax.dynamic_slice_in_dim(merged_two, pair_bit * rank_width, rank_width, 0)
    basis_three = lax.dynamic_slice_in_dim(merged_three, quad_bit * rank_width, rank_width, 0)
    top = lax.dynamic_slice_in_dim(passed_three, probe_index * local_probes, local_probes, 0)
    return (own_basis, basis_two, basis_three, top)


def solution(mesh):
    return jax.shard_map(
        on_device,
        mesh=mesh,
        in_specs=(
            P("leaf", None, None),
            P("probe", "leaf"),
            P("leaf", None),
            P("leaf", None),
            P("leaf", None, None),
            P("leaf", None),
            P("probe", "leaf"),
            P("probe", None),
            P("leaf"),
            P(),
            P(),
        ),
        out_specs=(
            P(("leaf", "probe"), None),
            P("leaf", None),
            P("leaf", None),
            P("probe", "leaf"),
        ),
        check_vma=False,
    )
```

```python
import jax
import jax.numpy as jnp
from jax import lax
from jax.experimental import pallas as pl
from jax.experimental.pallas import tpu as pltpu
from jax.sharding import PartitionSpec as P

highest = lax.Precision.HIGHEST

SLOT_CAP = 8


def partner_2(block, axis, stride):
    count = lax.axis_size(axis)
    route = []
    for low in range(count):
        high = low | 1 << stride
        if high != low and high < count:
            route += [(low, high), (high, low)]
    return lax.ppermute(block, axis, route)


def butterfly_sum(block, axis):
    count = lax.axis_size(axis)
    stride = 0
    while 1 << stride < count:
        block = block + partner_2(block, axis, stride)
        stride += 1
    return block


def gather_rows(block, axis):
    count = lax.axis_size(axis)
    index = lax.axis_index(axis)
    pieces = [block]
    for shift in range(1, count):
        route = [(j, (j + shift) % count) for j in range(count)]
        pieces.append(lax.ppermute(block, axis, route))
    stacked = jnp.stack(pieces)
    order = (index - jnp.arange(count, dtype=jnp.int32)) % count
    stacked = jnp.take(stacked, order, axis=0)
    return stacked.reshape((count * block.shape[0],) + block.shape[1:])


def extend_add_kernel(count_ref, rows_ref, vals_ref, start_ref, out_ref):
    source = pl.program_id(0)
    lanes = rows_ref.shape[1]
    probes = vals_ref.shape[1]
    high_count = out_ref.shape[0] // probes
    group = 8

    @pl.when(source == 0)
    def _():
        out_ref[...] = start_ref[...]

    def add_group(step, carry):
        spread, hot = [], []
        for offset in range(group):
            slot = step * group + offset
            targets = rows_ref[pl.ds(slot, 1), :]
            high = targets >> 7
            low = targets & (lanes - 1)
            vals = vals_ref[slot]
            zero = jnp.zeros_like(vals)
            spread.append(
                jnp.concatenate([jnp.where(high == h, vals, zero) for h in range(high_count)], axis=0)
            )
            hot.append(
                (lax.broadcasted_iota(jnp.int32, (lanes, lanes), 0) == low).astype(jnp.bfloat16)
            )
        spread = jnp.concatenate(spread, axis=1)
        hot = jnp.concatenate(hot, axis=1)
        out_ref[...] += lax.dot_general(
            spread, hot, (((1,), (1,)), ((), ())), preferred_element_type=jnp.float32
        )
        return carry

    lax.fori_loop(0, (count_ref[source] + group - 1) // group, add_group, 0)


def extend_add(recv_vals, recv_rows, start, sources, front_rows):
    slot_count, probes, block_rows = recv_vals.shape
    per_source = slot_count // sources
    high_count = front_rows // block_rows
    counts = jnp.sum((recv_rows[:, 0] >= 0).astype(jnp.int32).reshape(sources, -1), axis=1)
    start = jnp.moveaxis(start.reshape(probes, high_count, block_rows), 1, 0)
    start = start.reshape(high_count * probes, block_rows)
    spread = pl.pallas_call(
        extend_add_kernel,
        grid_spec=pltpu.PrefetchScalarGridSpec(
            num_scalar_prefetch=1,
            grid=(sources,),
            in_specs=[
                pl.BlockSpec((per_source, block_rows), lambda s, c: (s, 0)),
                pl.BlockSpec((per_source, probes, block_rows), lambda s, c: (s, 0, 0)),
                pl.BlockSpec((high_count * probes, block_rows), lambda s, c: (0, 0)),
            ],
            out_specs=pl.BlockSpec((high_count * probes, block_rows), lambda s, c: (0, 0)),
        ),
        out_shape=jax.ShapeDtypeStruct((high_count * probes, block_rows), jnp.float32),
        compiler_params=pltpu.CompilerParams(dimension_semantics=("arbitrary",)),
    )(counts, recv_rows, recv_vals, start)
    spread = spread.reshape(high_count, probes, block_rows)
    return jnp.moveaxis(spread, 0, 1).reshape(probes, front_rows)


def exchange_shares(block, axis):
    count = lax.axis_size(axis)
    index = lax.axis_index(axis)
    got = [jnp.take(block, index, axis=1)]
    for shift in range(1, count):
        route = [(j, (j + shift) % count) for j in range(count)]
        outgoing = jnp.take(block, (index + shift) % count, axis=1)
        got.append(lax.ppermute(outgoing, axis, route))
    stacked = jnp.stack(got)
    order = (index - jnp.arange(count, dtype=jnp.int32)) % count
    stacked = jnp.take(stacked, order, axis=0)
    return stacked.reshape((count * block.shape[0],) + block.shape[2:])


def basis_from_gram(sketched, gram_matrix, rank_limit):
    factor = jnp.linalg.cholesky(gram_matrix)
    orthonormal = lax.linalg.triangular_solve(
        factor, sketched, left_side=False, lower=True, transpose_a=True
    )
    columns = jnp.arange(sketched.shape[1], dtype=jnp.int32)
    return jnp.where(columns[None, :] < rank_limit, orthonormal, jnp.zeros_like(orthonormal))


def chol_basis(sketched, rank_limit):
    gram_matrix = jnp.einsum("ra,rb->ab", sketched, sketched, precision=highest)
    return basis_from_gram(sketched, gram_matrix, rank_limit)


def merge_level(own, partner, low_side, sketch_all, rank_limit):
    stacked = jnp.where(
        low_side,
        jnp.concatenate([own, partner], 1),
        jnp.concatenate([partner, own], 1),
    )
    sketched = jnp.einsum("pr,ps->rs", stacked, sketch_all, precision=highest)
    merged = chol_basis(sketched, rank_limit)
    return merged, jnp.dot(stacked, merged, precision=highest)


def on_device(
    child_updates,
    child_probes,
    child_dest,
    child_rows,
    parent_blocks,
    coupling,
    parent_probes,
    sketch,
    rank_one,
    rank_two,
    rank_three,
):
    leaf_count = lax.axis_size("leaf")
    probe_count = lax.axis_size("probe")
    leaf_index = lax.axis_index("leaf")
    probe_index = lax.axis_index("probe")
    local_probes = child_probes.shape[0]
    kid_count = child_updates.shape[0]
    kid_order = child_updates.shape[1]
    block_rows = child_rows.shape[1]
    block_count = child_rows.shape[0]
    front_rows = parent_probes.shape[1]
    rank_width = sketch.shape[1]

    updates = child_updates.reshape(kid_count, kid_order // block_rows, block_rows, kid_order)
    probe_cut = child_probes.reshape(local_probes, kid_count, kid_order)
    sampled = jnp.einsum("pck,cbik->cbpi", probe_cut, updates, preferred_element_type=jnp.float32)
    sampled = sampled.astype(jnp.bfloat16).reshape(block_count, local_probes, block_rows)

    targets = child_dest[:, 0]
    named = (targets[:, None] == jnp.arange(leaf_count, dtype=jnp.int32)[None, :]).astype(jnp.int32)
    earlier = jnp.cumsum(named, axis=0) - named
    slot = jnp.sum(earlier * named, axis=1)
    place = targets * SLOT_CAP + slot
    slot_count = leaf_count * SLOT_CAP
    source = jnp.full((slot_count,), block_count, jnp.int32).at[place].set(
        jnp.arange(block_count, dtype=jnp.int32)
    )
    filled = source < block_count
    source = jnp.minimum(source, block_count - 1)
    send_vals = jnp.where(filled[:, None, None], jnp.take(sampled, source, axis=0), jnp.bfloat16(0))
    send_rows = jnp.where(filled[:, None], jnp.take(child_rows, source, axis=0), -1)
    recv_vals = lax.all_to_all(send_vals, "leaf", 0, 0, tiled=True)
    recv_rows = lax.all_to_all(send_rows, "leaf", 0, 0, tiled=True)


    pieces = parent_probes.reshape(local_probes, front_rows // block_rows, block_rows)
    picked = jnp.take(pieces, coupling[:, 1], axis=1)
    product = jnp.einsum("eik,pek->pei", parent_blocks, picked, preferred_element_type=jnp.float32)
    initial = (
        jnp.zeros(pieces.shape, jnp.float32)
        .at[:, coupling[:, 0]]
        .add(product)
        .reshape(local_probes, front_rows)
    )
    sample = extend_add(recv_vals, recv_rows, initial, leaf_count, front_rows)

    share_rows = front_rows // probe_count
    sketch_all = gather_rows(sketch, "probe")
    share_sample = exchange_shares(sample.reshape(local_probes, probe_count, share_rows), "probe")
    share_sketched = jnp.einsum("pr,ps->rs", share_sample, sketch_all, precision=highest)
    gram_one = butterfly_sum(
        jnp.einsum("ra,rb->ab", share_sketched, share_sketched, precision=highest), "probe"
    )
    own_basis = basis_from_gram(share_sketched, gram_one, rank_one[0])
    passed_one = butterfly_sum(jnp.dot(share_sample, own_basis, precision=highest), "probe")

    pair_bit = leaf_index % 2
    merged_two, passed_two = merge_level(
        passed_one, partner_2(passed_one, "leaf", 0), pair_bit == 0, sketch_all, rank_two[leaf_index // 2]
    )
    quad_bit = leaf_index // 2 % 2
    merged_three, passed_three = merge_level(
        passed_two, partner_2(passed_two, "leaf", 1), quad_bit == 0, sketch_all, rank_three[leaf_index // 4]
    )
    basis_two = lax.dynamic_slice_in_dim(merged_two, pair_bit * rank_width, rank_width, 0)
    basis_three = lax.dynamic_slice_in_dim(merged_three, quad_bit * rank_width, rank_width, 0)
    top = lax.dynamic_slice_in_dim(passed_three, probe_index * local_probes, local_probes, 0)
    return (own_basis, basis_two, basis_three, top)


def solution(mesh):
    return jax.shard_map(
        on_device,
        mesh=mesh,
        in_specs=(
            P("leaf", None, None),
            P("probe", "leaf"),
            P("leaf", None),
            P("leaf", None),
            P("leaf", None, None),
            P("leaf", None),
            P("probe", "leaf"),
            P("probe", None),
            P("leaf"),
            P(),
            P(),
        ),
        out_specs=(
            P(("leaf", "probe"), None),
            P("leaf", None),
            P("leaf", None),
            P("probe", "leaf"),
        ),
        check_vma=False,
    )
```

```python
import functools

import jax
import jax.numpy as jnp
from jax import lax
from jax.experimental import pallas as pl
from jax.experimental.pallas import tpu as pltpu
from jax.sharding import PartitionSpec as P

highest = lax.Precision.HIGHEST

SLOT_CAP = 8


def partner_2(block, axis, stride):
    count = lax.axis_size(axis)
    route = []
    for low in range(count):
        high = low | 1 << stride
        if high != low and high < count:
            route += [(low, high), (high, low)]
    return lax.ppermute(block, axis, route)


def butterfly_sum(block, axis):
    count = lax.axis_size(axis)
    stride = 0
    while 1 << stride < count:
        block = block + partner_2(block, axis, stride)
        stride += 1
    return block


def gather_rows(block, axis):
    count = lax.axis_size(axis)
    index = lax.axis_index(axis)
    pieces = [block]
    for shift in range(1, count):
        route = [(j, (j + shift) % count) for j in range(count)]
        pieces.append(lax.ppermute(block, axis, route))
    stacked = jnp.stack(pieces)
    order = (index - jnp.arange(count, dtype=jnp.int32)) % count
    stacked = jnp.take(stacked, order, axis=0)
    return stacked.reshape((count * block.shape[0],) + block.shape[1:])


def extend_add_kernel(count_ref, load_ref, start_ref, out_ref, *, slots, probes):
    source = pl.program_id(0)
    lanes = load_ref.shape[2]
    high_count = out_ref.shape[0] // probes
    info = slots * probes

    @pl.when(source == 0)
    def _():
        out_ref[...] = start_ref[...]

    @pl.when(count_ref[source] > 0)
    def _():
        spread, hot = [], []
        for slot in range(slots):
            high = load_ref[0, pl.ds(info + slot, 1), :].astype(jnp.float32).astype(jnp.int32)
            low = load_ref[0, pl.ds(info + slots + slot, 1), :].astype(jnp.float32).astype(jnp.int32)
            vals = load_ref[0, pl.ds(slot * probes, probes), :]
            zero = jnp.zeros_like(vals)
            spread.append(
                jnp.concatenate([jnp.where(high == h, vals, zero) for h in range(high_count)], axis=0)
            )
            hot.append(
                (lax.broadcasted_iota(jnp.int32, (lanes, lanes), 0) == low).astype(jnp.bfloat16)
            )
        spread = jnp.concatenate(spread, axis=1)
        hot = jnp.concatenate(hot, axis=1)
        out_ref[...] += lax.dot_general(
            spread, hot, (((1,), (1,)), ((), ())), preferred_element_type=jnp.float32
        )


def extend_add(load, counts, start, slots, probes):
    sources, depth, lanes = load.shape
    kernel = functools.partial(extend_add_kernel, slots=slots, probes=probes)
    return pl.pallas_call(
        kernel,
        grid_spec=pltpu.PrefetchScalarGridSpec(
            num_scalar_prefetch=1,
            grid=(sources,),
            in_specs=[
                pl.BlockSpec((1, depth, lanes), lambda s, c: (s, 0, 0)),
                pl.BlockSpec(start.shape, lambda s, c: (0, 0)),
            ],
            out_specs=pl.BlockSpec(start.shape, lambda s, c: (0, 0)),
        ),
        out_shape=jax.ShapeDtypeStruct(start.shape, jnp.float32),
        compiler_params=pltpu.CompilerParams(dimension_semantics=("arbitrary",)),
    )(counts, load, start)


def exchange_shares(block, axis):
    count = lax.axis_size(axis)
    index = lax.axis_index(axis)
    got = [jnp.take(block, index, axis=1)]
    for shift in range(1, count):
        route = [(j, (j + shift) % count) for j in range(count)]
        outgoing = jnp.take(block, (index + shift) % count, axis=1)
        got.append(lax.ppermute(outgoing, axis, route))
    stacked = jnp.stack(got)
    order = (index - jnp.arange(count, dtype=jnp.int32)) % count
    stacked = jnp.take(stacked, order, axis=0)
    return stacked.reshape((count * block.shape[0],) + block.shape[2:])


def basis_from_gram(sketched, gram_matrix, rank_limit):
    factor = jnp.linalg.cholesky(gram_matrix)
    orthonormal = lax.linalg.triangular_solve(
        factor, sketched, left_side=False, lower=True, transpose_a=True
    )
    columns = jnp.arange(sketched.shape[1], dtype=jnp.int32)
    return jnp.where(columns[None, :] < rank_limit, orthonormal, jnp.zeros_like(orthonormal))


def chol_basis(sketched, rank_limit):
    gram_matrix = jnp.einsum("ra,rb->ab", sketched, sketched, precision=highest)
    return basis_from_gram(sketched, gram_matrix, rank_limit)


def merge_level(own, partner, low_side, sketch_all, rank_limit):
    stacked = jnp.where(
        low_side,
        jnp.concatenate([own, partner], 1),
        jnp.concatenate([partner, own], 1),
    )
    sketched = jnp.einsum("pr,ps->rs", stacked, sketch_all, precision=highest)
    merged = chol_basis(sketched, rank_limit)
    return merged, jnp.dot(stacked, merged, precision=highest)


def on_device(
    child_updates,
    child_probes,
    child_dest,
    child_rows,
    parent_blocks,
    coupling,
    parent_probes,
    sketch,
    rank_one,
    rank_two,
    rank_three,
):
    leaf_count = lax.axis_size("leaf")
    probe_count = lax.axis_size("probe")
    leaf_index = lax.axis_index("leaf")
    probe_index = lax.axis_index("probe")
    local_probes = child_probes.shape[0]
    kid_count = child_updates.shape[0]
    kid_order = child_updates.shape[1]
    block_rows = child_rows.shape[1]
    block_count = child_rows.shape[0]
    front_rows = parent_probes.shape[1]
    rank_width = sketch.shape[1]

    updates = child_updates.reshape(kid_count, kid_order // block_rows, block_rows, kid_order)
    probe_cut = child_probes.reshape(local_probes, kid_count, kid_order)
    sampled = jnp.einsum("pck,cbik->cbpi", probe_cut, updates, preferred_element_type=jnp.float32)
    sampled = sampled.astype(jnp.bfloat16).reshape(block_count, local_probes, block_rows)

    targets = child_dest[:, 0]
    named = (targets[:, None] == jnp.arange(leaf_count, dtype=jnp.int32)[None, :]).astype(jnp.int32)
    earlier = jnp.cumsum(named, axis=0) - named
    slot = jnp.sum(earlier * named, axis=1)
    place = targets * SLOT_CAP + slot
    slot_count = leaf_count * SLOT_CAP
    source = jnp.full((slot_count,), block_count, jnp.int32).at[place].set(
        jnp.arange(block_count, dtype=jnp.int32)
    )
    filled = source < block_count
    source = jnp.minimum(source, block_count - 1)
    high = jnp.where(filled[:, None], child_rows[source] // block_rows, -1)
    low = jnp.where(filled[:, None], child_rows[source] % block_rows, 0)
    send_vals = jnp.where(filled[:, None, None], jnp.take(sampled, source, axis=0), jnp.bfloat16(0))
    half = SLOT_CAP
    info_rows = 16
    loads = []
    for part in range(1):
        picked_slots = slice(part * half, (part + 1) * half)
        vals = send_vals.reshape(leaf_count, SLOT_CAP, local_probes, block_rows)[:, picked_slots]
        info = jnp.concatenate(
            [
                high.reshape(leaf_count, SLOT_CAP, block_rows)[:, picked_slots],
                low.reshape(leaf_count, SLOT_CAP, block_rows)[:, picked_slots],
                jnp.zeros((leaf_count, info_rows - 2 * half, block_rows), jnp.int32),
            ],
            axis=1,
        ).astype(jnp.bfloat16)
        load = jnp.concatenate(
            [vals.reshape(leaf_count, half * local_probes, block_rows), info], axis=1
        )
        loads.append(lax.all_to_all(load, "leaf", 0, 0, tiled=True))

    pieces = parent_probes.reshape(local_probes, front_rows // block_rows, block_rows)
    picked = jnp.take(pieces, coupling[:, 1], axis=1)
    product = jnp.einsum("eik,pek->pei", parent_blocks, picked, preferred_element_type=jnp.float32)
    initial = (
        jnp.zeros(pieces.shape, jnp.float32)
        .at[:, coupling[:, 0]]
        .add(product)
        .reshape(local_probes, front_rows)
    )
    high_count = front_rows // block_rows
    spread = jnp.moveaxis(initial.reshape(local_probes, high_count, block_rows), 1, 0)
    spread = spread.reshape(high_count * local_probes, block_rows)
    for load in loads:
        counts = jnp.sum(load[:, half * local_probes, :1] >= 0, axis=1).astype(jnp.int32)
        spread = extend_add(load, counts, spread, half, local_probes)
    spread = spread.reshape(high_count, local_probes, block_rows)
    sample = jnp.moveaxis(spread, 0, 1).reshape(local_probes, front_rows)

    share_rows = front_rows // probe_count
    sketch_all = gather_rows(sketch, "probe")
    share_sample = exchange_shares(sample.reshape(local_probes, probe_count, share_rows), "probe")
    share_sketched = jnp.einsum("pr,ps->rs", share_sample, sketch_all, precision=highest)
    gram_one = butterfly_sum(
        jnp.einsum("ra,rb->ab", share_sketched, share_sketched, precision=highest), "probe"
    )
    own_basis = basis_from_gram(share_sketched, gram_one, rank_one[0])
    passed_one = butterfly_sum(jnp.dot(share_sample, own_basis, precision=highest), "probe")

    pair_bit = leaf_index % 2
    merged_two, passed_two = merge_level(
        passed_one, partner_2(passed_one, "leaf", 0), pair_bit == 0, sketch_all, rank_two[leaf_index // 2]
    )
    quad_bit = leaf_index // 2 % 2
    merged_three, passed_three = merge_level(
        passed_two, partner_2(passed_two, "leaf", 1), quad_bit == 0, sketch_all, rank_three[leaf_index // 4]
    )
    basis_two = lax.dynamic_slice_in_dim(merged_two, pair_bit * rank_width, rank_width, 0)
    basis_three = lax.dynamic_slice_in_dim(merged_three, quad_bit * rank_width, rank_width, 0)
    top = lax.dynamic_slice_in_dim(passed_three, probe_index * local_probes, local_probes, 0)
    return (own_basis, basis_two, basis_three, top)


def solution(mesh):
    return jax.shard_map(
        on_device,
        mesh=mesh,
        in_specs=(
            P("leaf", None, None),
            P("probe", "leaf"),
            P("leaf", None),
            P("leaf", None),
            P("leaf", None, None),
            P("leaf", None),
            P("probe", "leaf"),
            P("probe", None),
            P("leaf"),
            P(),
            P(),
        ),
        out_specs=(
            P(("leaf", "probe"), None),
            P("leaf", None),
            P("leaf", None),
            P("probe", "leaf"),
        ),
        check_vma=False,
    )
```

```python
import functools

import jax
import jax.numpy as jnp
from jax import lax
from jax.experimental import pallas as pl
from jax.experimental.pallas import tpu as pltpu
from jax.sharding import PartitionSpec as P

highest = lax.Precision.HIGHEST

SLOT_CAP = 8


def partner_2(block, axis, stride):
    count = lax.axis_size(axis)
    route = []
    for low in range(count):
        high = low | 1 << stride
        if high != low and high < count:
            route += [(low, high), (high, low)]
    return lax.ppermute(block, axis, route)


def butterfly_sum(block, axis):
    count = lax.axis_size(axis)
    stride = 0
    while 1 << stride < count:
        block = block + partner_2(block, axis, stride)
        stride += 1
    return block


def ordered_sum(block, axis):
    count = lax.axis_size(axis)
    gathered = gather_rows(block[None], axis)
    total = gathered[0]
    for member in range(1, count):
        total = total + gathered[member]
    return total


def gather_rows(block, axis):
    count = lax.axis_size(axis)
    index = lax.axis_index(axis)
    pieces = [block]
    for shift in range(1, count):
        route = [(j, (j + shift) % count) for j in range(count)]
        pieces.append(lax.ppermute(block, axis, route))
    stacked = jnp.stack(pieces)
    order = (index - jnp.arange(count, dtype=jnp.int32)) % count
    stacked = jnp.take(stacked, order, axis=0)
    return stacked.reshape((count * block.shape[0],) + block.shape[1:])


def extend_add_kernel(count_ref, load_ref, start_ref, out_ref, *, slots, probes):
    source = pl.program_id(0)
    lanes = load_ref.shape[2]
    high_count = out_ref.shape[0] // probes
    info = slots * probes

    @pl.when(source == 0)
    def _():
        out_ref[...] = start_ref[...]

    @pl.when(count_ref[source] > 0)
    def _():
        spread, hot = [], []
        for slot in range(slots):
            high = load_ref[0, pl.ds(info + slot, 1), :].astype(jnp.float32).astype(jnp.int32)
            low = load_ref[0, pl.ds(info + slots + slot, 1), :].astype(jnp.float32).astype(jnp.int32)
            vals = load_ref[0, pl.ds(slot * probes, probes), :]
            zero = jnp.zeros_like(vals)
            spread.append(
                jnp.concatenate([jnp.where(high == h, vals, zero) for h in range(high_count)], axis=0)
            )
            hot.append(
                (lax.broadcasted_iota(jnp.int32, (lanes, lanes), 0) == low).astype(jnp.bfloat16)
            )
        spread = jnp.concatenate(spread, axis=1)
        hot = jnp.concatenate(hot, axis=1)
        out_ref[...] += lax.dot_general(
            spread, hot, (((1,), (1,)), ((), ())), preferred_element_type=jnp.float32
        )


def extend_add(load, counts, start, slots, probes):
    sources, depth, lanes = load.shape
    kernel = functools.partial(extend_add_kernel, slots=slots, probes=probes)
    return pl.pallas_call(
        kernel,
        grid_spec=pltpu.PrefetchScalarGridSpec(
            num_scalar_prefetch=1,
            grid=(sources,),
            in_specs=[
                pl.BlockSpec((1, depth, lanes), lambda s, c: (s, 0, 0)),
                pl.BlockSpec(start.shape, lambda s, c: (0, 0)),
            ],
            out_specs=pl.BlockSpec(start.shape, lambda s, c: (0, 0)),
        ),
        out_shape=jax.ShapeDtypeStruct(start.shape, jnp.float32),
        compiler_params=pltpu.CompilerParams(dimension_semantics=("arbitrary",)),
    )(counts, load, start)


def exchange_shares(block, axis):
    count = lax.axis_size(axis)
    index = lax.axis_index(axis)
    got = [jnp.take(block, index, axis=1)]
    for shift in range(1, count):
        route = [(j, (j + shift) % count) for j in range(count)]
        outgoing = jnp.take(block, (index + shift) % count, axis=1)
        got.append(lax.ppermute(outgoing, axis, route))
    stacked = jnp.stack(got)
    order = (index - jnp.arange(count, dtype=jnp.int32)) % count
    stacked = jnp.take(stacked, order, axis=0)
    return stacked.reshape((count * block.shape[0],) + block.shape[2:])


def cholesky_inverse_kernel(gram_ref, inverse_ref, work_ref, rest_ref):
    order = gram_ref.shape[0]
    sub = lax.broadcasted_iota(jnp.int32, (order, order), 0)
    lane = lax.broadcasted_iota(jnp.int32, (order, order), 1)
    sub_one = lax.broadcasted_iota(jnp.int32, (order, 1), 0)
    lane_one = lax.broadcasted_iota(jnp.int32, (1, order), 1)
    work_ref[...] = gram_ref[...]
    rest_ref[...] = jnp.where(sub == lane, 1.0, 0.0).astype(jnp.float32)

    def step(j, carry):
        work = work_ref[...]
        column = jnp.sum(jnp.where(lane == j, work, 0.0), axis=1, keepdims=True)
        pivot = jnp.sum(jnp.where(sub_one == j, column, 0.0), axis=0, keepdims=True)
        scale = 1.0 / jnp.sqrt(pivot)
        column = jnp.where(sub_one >= j, column * scale, 0.0)
        row = jnp.where(lane_one >= j, work_ref[pl.ds(j, 1), :] * scale, 0.0)
        work_ref[...] = work - column * row
        solved = rest_ref[pl.ds(j, 1), :] * scale
        inverse_ref[pl.ds(j, 1), :] = solved
        rest_ref[...] = rest_ref[...] - column * solved
        return carry

    lax.fori_loop(0, order, step, 0)


def cholesky_inverse(gram_matrix):
    order = gram_matrix.shape[0]
    symmetric = (gram_matrix + gram_matrix.T) * 0.5
    return pl.pallas_call(
        cholesky_inverse_kernel,
        out_shape=jax.ShapeDtypeStruct((order, order), jnp.float32),
        scratch_shapes=[pltpu.VMEM((order, order), jnp.float32)] * 2,
    )(symmetric)


def basis_from_gram(sketched, gram_matrix, rank_limit):
    inverse = cholesky_inverse(gram_matrix)
    orthonormal = jnp.einsum("ra,ba->rb", sketched, inverse, precision=highest)
    columns = jnp.arange(sketched.shape[1], dtype=jnp.int32)
    return jnp.where(columns[None, :] < rank_limit, orthonormal, jnp.zeros_like(orthonormal))


def chol_basis(sketched, rank_limit):
    gram_matrix = jnp.einsum("ra,rb->ab", sketched, sketched, precision=highest)
    return basis_from_gram(sketched, gram_matrix, rank_limit)


def merge_level(own, partner, low_side, sketch_all, rank_limit):
    stacked = jnp.where(
        low_side,
        jnp.concatenate([own, partner], 1),
        jnp.concatenate([partner, own], 1),
    )
    sketched = jnp.einsum("pr,ps->rs", stacked, sketch_all, precision=highest)
    merged = chol_basis(sketched, rank_limit)
    return merged, jnp.dot(stacked, merged, precision=highest)


def on_device(
    child_updates,
    child_probes,
    child_dest,
    child_rows,
    parent_blocks,
    coupling,
    parent_probes,
    sketch,
    rank_one,
    rank_two,
    rank_three,
):
    leaf_count = lax.axis_size("leaf")
    probe_count = lax.axis_size("probe")
    leaf_index = lax.axis_index("leaf")
    probe_index = lax.axis_index("probe")
    local_probes = child_probes.shape[0]
    kid_count = child_updates.shape[0]
    kid_order = child_updates.shape[1]
    block_rows = child_rows.shape[1]
    block_count = child_rows.shape[0]
    front_rows = parent_probes.shape[1]
    rank_width = sketch.shape[1]

    updates = child_updates.reshape(kid_count, kid_order // block_rows, block_rows, kid_order)
    probe_cut = child_probes.reshape(local_probes, kid_count, kid_order)
    sampled = jnp.einsum("pck,cbik->cbpi", probe_cut, updates, preferred_element_type=jnp.float32)
    sampled = sampled.astype(jnp.bfloat16).reshape(block_count, local_probes, block_rows)

    targets = child_dest[:, 0]
    named = (targets[:, None] == jnp.arange(leaf_count, dtype=jnp.int32)[None, :]).astype(jnp.int32)
    earlier = jnp.cumsum(named, axis=0) - named
    slot = jnp.sum(earlier * named, axis=1)
    place = targets * SLOT_CAP + slot
    slot_count = leaf_count * SLOT_CAP
    source = jnp.full((slot_count,), block_count, jnp.int32).at[place].set(
        jnp.arange(block_count, dtype=jnp.int32)
    )
    filled = source < block_count
    source = jnp.minimum(source, block_count - 1)
    high = jnp.where(filled[:, None], child_rows[source] // block_rows, -1)
    low = jnp.where(filled[:, None], child_rows[source] % block_rows, 0)
    send_vals = jnp.where(filled[:, None, None], jnp.take(sampled, source, axis=0), jnp.bfloat16(0))
    half = SLOT_CAP
    info_rows = 16
    loads = []
    for part in range(1):
        picked_slots = slice(part * half, (part + 1) * half)
        vals = send_vals.reshape(leaf_count, SLOT_CAP, local_probes, block_rows)[:, picked_slots]
        info = jnp.concatenate(
            [
                high.reshape(leaf_count, SLOT_CAP, block_rows)[:, picked_slots],
                low.reshape(leaf_count, SLOT_CAP, block_rows)[:, picked_slots],
                jnp.zeros((leaf_count, info_rows - 2 * half, block_rows), jnp.int32),
            ],
            axis=1,
        ).astype(jnp.bfloat16)
        load = jnp.concatenate(
            [vals.reshape(leaf_count, half * local_probes, block_rows), info], axis=1
        )
        loads.append(lax.all_to_all(load, "leaf", 0, 0, tiled=True))

    pieces = parent_probes.reshape(local_probes, front_rows // block_rows, block_rows)
    picked = jnp.take(pieces, coupling[:, 1], axis=1)
    product = jnp.einsum("eik,pek->pei", parent_blocks, picked, preferred_element_type=jnp.float32)
    initial = (
        jnp.zeros(pieces.shape, jnp.float32)
        .at[:, coupling[:, 0]]
        .add(product)
        .reshape(local_probes, front_rows)
    )
    high_count = front_rows // block_rows
    spread = jnp.moveaxis(initial.reshape(local_probes, high_count, block_rows), 1, 0)
    spread = spread.reshape(high_count * local_probes, block_rows)
    for load in loads:
        counts = jnp.sum(load[:, half * local_probes, :1] >= 0, axis=1).astype(jnp.int32)
        spread = extend_add(load, counts, spread, half, local_probes)
    spread = spread.reshape(high_count, local_probes, block_rows)
    sample = jnp.moveaxis(spread, 0, 1).reshape(local_probes, front_rows)

    share_rows = front_rows // probe_count
    sketch_all = gather_rows(sketch, "probe")
    share_sample = exchange_shares(sample.reshape(local_probes, probe_count, share_rows), "probe")
    share_sketched = jnp.einsum("pr,ps->rs", share_sample, sketch_all, precision=highest)
    gram_one = ordered_sum(
        jnp.einsum("ra,rb->ab", share_sketched, share_sketched, precision=highest), "probe"
    )
    own_basis = basis_from_gram(share_sketched, gram_one, rank_one[0])
    passed_one = ordered_sum(jnp.dot(share_sample, own_basis, precision=highest), "probe")

    pair_bit = leaf_index % 2
    merged_two, passed_two = merge_level(
        passed_one, partner_2(passed_one, "leaf", 0), pair_bit == 0, sketch_all, rank_two[leaf_index // 2]
    )
    quad_bit = leaf_index // 2 % 2
    merged_three, passed_three = merge_level(
        passed_two, partner_2(passed_two, "leaf", 1), quad_bit == 0, sketch_all, rank_three[leaf_index // 4]
    )
    basis_two = lax.dynamic_slice_in_dim(merged_two, pair_bit * rank_width, rank_width, 0)
    basis_three = lax.dynamic_slice_in_dim(merged_three, quad_bit * rank_width, rank_width, 0)
    top = lax.dynamic_slice_in_dim(passed_three, probe_index * local_probes, local_probes, 0)
    return (own_basis, basis_two, basis_three, top)


def solution(mesh):
    return jax.shard_map(
        on_device,
        mesh=mesh,
        in_specs=(
            P("leaf", None, None),
            P("probe", "leaf"),
            P("leaf", None),
            P("leaf", None),
            P("leaf", None, None),
            P("leaf", None),
            P("probe", "leaf"),
            P("probe", None),
            P("leaf"),
            P(),
            P(),
        ),
        out_specs=(
            P(("leaf", "probe"), None),
            P("leaf", None),
            P("leaf", None),
            P("probe", "leaf"),
        ),
        check_vma=False,
    )
```

```python
import functools

import jax
import jax.numpy as jnp
from jax import lax
from jax.experimental import pallas as pl
from jax.experimental.pallas import tpu as pltpu
from jax.sharding import PartitionSpec as P

highest = lax.Precision.HIGHEST

SLOT_CAP = 8


def partner_2(block, axis, stride):
    count = lax.axis_size(axis)
    route = []
    for low in range(count):
        high = low | 1 << stride
        if high != low and high < count:
            route += [(low, high), (high, low)]
    return lax.ppermute(block, axis, route)


def butterfly_sum(block, axis):
    count = lax.axis_size(axis)
    stride = 0
    while 1 << stride < count:
        block = block + partner_2(block, axis, stride)
        stride += 1
    return block


def ordered_sum(block, axis):
    count = lax.axis_size(axis)
    gathered = gather_rows(block[None], axis)
    total = gathered[0]
    for member in range(1, count):
        total = total + gathered[member]
    return total


def gather_rows(block, axis):
    count = lax.axis_size(axis)
    index = lax.axis_index(axis)
    pieces = [block]
    for shift in range(1, count):
        route = [(j, (j + shift) % count) for j in range(count)]
        pieces.append(lax.ppermute(block, axis, route))
    stacked = jnp.stack(pieces)
    order = (index - jnp.arange(count, dtype=jnp.int32)) % count
    stacked = jnp.take(stacked, order, axis=0)
    return stacked.reshape((count * block.shape[0],) + block.shape[1:])


def extend_add_kernel(count_ref, load_ref, start_ref, out_ref, *, slots, probes):
    source = pl.program_id(0)
    lanes = load_ref.shape[2]
    high_count = out_ref.shape[0] // probes
    info = slots * probes

    @pl.when(source == 0)
    def _():
        out_ref[...] = start_ref[...]

    @pl.when(count_ref[source] > 0)
    def _():
        spread, hot = [], []
        for slot in range(slots):
            high = load_ref[0, pl.ds(info + slot, 1), :].astype(jnp.float32).astype(jnp.int32)
            low = load_ref[0, pl.ds(info + slots + slot, 1), :].astype(jnp.float32).astype(jnp.int32)
            vals = load_ref[0, pl.ds(slot * probes, probes), :]
            zero = jnp.zeros_like(vals)
            spread.append(
                jnp.concatenate([jnp.where(high == h, vals, zero) for h in range(high_count)], axis=0)
            )
            hot.append(
                (lax.broadcasted_iota(jnp.int32, (lanes, lanes), 0) == low).astype(jnp.bfloat16)
            )
        spread = jnp.concatenate(spread, axis=1)
        hot = jnp.concatenate(hot, axis=1)
        out_ref[...] += lax.dot_general(
            spread, hot, (((1,), (1,)), ((), ())), preferred_element_type=jnp.float32
        )


def extend_add(load, counts, start, slots, probes):
    sources, depth, lanes = load.shape
    kernel = functools.partial(extend_add_kernel, slots=slots, probes=probes)
    return pl.pallas_call(
        kernel,
        grid_spec=pltpu.PrefetchScalarGridSpec(
            num_scalar_prefetch=1,
            grid=(sources,),
            in_specs=[
                pl.BlockSpec((1, depth, lanes), lambda s, c: (s, 0, 0)),
                pl.BlockSpec(start.shape, lambda s, c: (0, 0)),
            ],
            out_specs=pl.BlockSpec(start.shape, lambda s, c: (0, 0)),
        ),
        out_shape=jax.ShapeDtypeStruct(start.shape, jnp.float32),
        compiler_params=pltpu.CompilerParams(dimension_semantics=("arbitrary",)),
    )(counts, load, start)


def exchange_shares(block, axis):
    count = lax.axis_size(axis)
    index = lax.axis_index(axis)
    got = [jnp.take(block, index, axis=1)]
    for shift in range(1, count):
        route = [(j, (j + shift) % count) for j in range(count)]
        outgoing = jnp.take(block, (index + shift) % count, axis=1)
        got.append(lax.ppermute(outgoing, axis, route))
    stacked = jnp.stack(got)
    order = (index - jnp.arange(count, dtype=jnp.int32)) % count
    stacked = jnp.take(stacked, order, axis=0)
    return stacked.reshape((count * block.shape[0],) + block.shape[2:])


def cholesky_inverse_kernel(gram_ref, inverse_ref, work_ref, rest_ref):
    order = gram_ref.shape[0]
    tile = 8
    sub = lax.broadcasted_iota(jnp.int32, (order, order), 0)
    lane = lax.broadcasted_iota(jnp.int32, (order, order), 1)
    lane_one = lax.broadcasted_iota(jnp.int32, (1, order), 1)
    work_ref[...] = gram_ref[...]
    rest_ref[...] = jnp.where(sub == lane, 1.0, 0.0).astype(jnp.float32)
    inverse_ref[...] = jnp.zeros_like(inverse_ref)

    for first in range(0, order, tile):
        height = order - first
        tail_lane = lax.broadcasted_iota(jnp.int32, (height, order), 1)
        tail_sub = lax.broadcasted_iota(jnp.int32, (height, 1), 0) + first

        def step(j, carry, first=first, tail_lane=tail_lane, tail_sub=tail_sub):
            work = work_ref[first:, :]
            column = jnp.sum(jnp.where(tail_lane == j, work, 0.0), axis=1, keepdims=True)
            pivot = jnp.sum(jnp.where(tail_sub == j, column, 0.0), axis=0, keepdims=True)
            scale = 1.0 / jnp.sqrt(pivot)
            column = jnp.where(tail_sub >= j, column * scale, 0.0)
            row = jnp.where(lane_one >= j, work_ref[pl.ds(j, 1), :] * scale, 0.0)
            work_ref[first:, :] = work - column * row
            solved = rest_ref[pl.ds(j, 1), :] * scale
            inverse_ref[pl.ds(j, 1), :] = solved
            rest_ref[first:, :] = rest_ref[first:, :] - column * solved
            return carry

        lax.fori_loop(first, first + tile, step, 0)


def cholesky_inverse(gram_matrix):
    order = gram_matrix.shape[0]
    symmetric = (gram_matrix + gram_matrix.T) * 0.5
    return pl.pallas_call(
        cholesky_inverse_kernel,
        out_shape=jax.ShapeDtypeStruct((order, order), jnp.float32),
        scratch_shapes=[pltpu.VMEM((order, order), jnp.float32)] * 2,
    )(symmetric)


def basis_from_gram(sketched, gram_matrix, rank_limit):
    inverse = cholesky_inverse(gram_matrix)
    orthonormal = jnp.einsum("ra,ba->rb", sketched, inverse, precision=highest)
    columns = jnp.arange(sketched.shape[1], dtype=jnp.int32)
    return jnp.where(columns[None, :] < rank_limit, orthonormal, jnp.zeros_like(orthonormal))


def chol_basis(sketched, rank_limit):
    gram_matrix = jnp.einsum("ra,rb->ab", sketched, sketched, precision=highest)
    return basis_from_gram(sketched, gram_matrix, rank_limit)


def merge_level(own, partner, low_side, sketch_all, rank_limit):
    stacked = jnp.where(
        low_side,
        jnp.concatenate([own, partner], 1),
        jnp.concatenate([partner, own], 1),
    )
    sketched = jnp.einsum("pr,ps->rs", stacked, sketch_all, precision=highest)
    merged = chol_basis(sketched, rank_limit)
    return merged, jnp.dot(stacked, merged, precision=highest)


def on_device(
    child_updates,
    child_probes,
    child_dest,
    child_rows,
    parent_blocks,
    coupling,
    parent_probes,
    sketch,
    rank_one,
    rank_two,
    rank_three,
):
    leaf_count = lax.axis_size("leaf")
    probe_count = lax.axis_size("probe")
    leaf_index = lax.axis_index("leaf")
    probe_index = lax.axis_index("probe")
    local_probes = child_probes.shape[0]
    kid_count = child_updates.shape[0]
    kid_order = child_updates.shape[1]
    block_rows = child_rows.shape[1]
    block_count = child_rows.shape[0]
    front_rows = parent_probes.shape[1]
    rank_width = sketch.shape[1]

    updates = child_updates.reshape(kid_count, kid_order // block_rows, block_rows, kid_order)
    probe_cut = child_probes.reshape(local_probes, kid_count, kid_order)
    sampled = jnp.einsum("pck,cbik->cbpi", probe_cut, updates, preferred_element_type=jnp.float32)
    sampled = sampled.astype(jnp.bfloat16).reshape(block_count, local_probes, block_rows)

    targets = child_dest[:, 0]
    named = (targets[:, None] == jnp.arange(leaf_count, dtype=jnp.int32)[None, :]).astype(jnp.int32)
    earlier = jnp.cumsum(named, axis=0) - named
    slot = jnp.sum(earlier * named, axis=1)
    place = targets * SLOT_CAP + slot
    slot_count = leaf_count * SLOT_CAP
    source = jnp.full((slot_count,), block_count, jnp.int32).at[place].set(
        jnp.arange(block_count, dtype=jnp.int32)
    )
    filled = source < block_count
    source = jnp.minimum(source, block_count - 1)
    high = jnp.where(filled[:, None], child_rows[source] // block_rows, -1)
    low = jnp.where(filled[:, None], child_rows[source] % block_rows, 0)
    send_vals = jnp.where(filled[:, None, None], jnp.take(sampled, source, axis=0), jnp.bfloat16(0))
    half = SLOT_CAP
    info_rows = 16
    loads = []
    for part in range(1):
        picked_slots = slice(part * half, (part + 1) * half)
        vals = send_vals.reshape(leaf_count, SLOT_CAP, local_probes, block_rows)[:, picked_slots]
        info = jnp.concatenate(
            [
                high.reshape(leaf_count, SLOT_CAP, block_rows)[:, picked_slots],
                low.reshape(leaf_count, SLOT_CAP, block_rows)[:, picked_slots],
                jnp.zeros((leaf_count, info_rows - 2 * half, block_rows), jnp.int32),
            ],
            axis=1,
        ).astype(jnp.bfloat16)
        load = jnp.concatenate(
            [vals.reshape(leaf_count, half * local_probes, block_rows), info], axis=1
        )
        loads.append(lax.all_to_all(load, "leaf", 0, 0, tiled=True))

    pieces = parent_probes.reshape(local_probes, front_rows // block_rows, block_rows)
    picked = jnp.take(pieces, coupling[:, 1], axis=1)
    product = jnp.einsum("eik,pek->pei", parent_blocks, picked, preferred_element_type=jnp.float32)
    initial = (
        jnp.zeros(pieces.shape, jnp.float32)
        .at[:, coupling[:, 0]]
        .add(product)
        .reshape(local_probes, front_rows)
    )
    high_count = front_rows // block_rows
    spread = jnp.moveaxis(initial.reshape(local_probes, high_count, block_rows), 1, 0)
    spread = spread.reshape(high_count * local_probes, block_rows)
    for load in loads:
        counts = jnp.sum(load[:, half * local_probes, :1] >= 0, axis=1).astype(jnp.int32)
        spread = extend_add(load, counts, spread, half, local_probes)
    spread = spread.reshape(high_count, local_probes, block_rows)
    sample = jnp.moveaxis(spread, 0, 1).reshape(local_probes, front_rows)

    share_rows = front_rows // probe_count
    sketch_all = gather_rows(sketch, "probe")
    share_sample = exchange_shares(sample.reshape(local_probes, probe_count, share_rows), "probe")
    share_sketched = jnp.einsum("pr,ps->rs", share_sample, sketch_all, precision=highest)
    gram_one = ordered_sum(
        jnp.einsum("ra,rb->ab", share_sketched, share_sketched, precision=highest), "probe"
    )
    own_basis = basis_from_gram(share_sketched, gram_one, rank_one[0])
    passed_one = ordered_sum(jnp.dot(share_sample, own_basis, precision=highest), "probe")

    pair_bit = leaf_index % 2
    merged_two, passed_two = merge_level(
        passed_one, partner_2(passed_one, "leaf", 0), pair_bit == 0, sketch_all, rank_two[leaf_index // 2]
    )
    quad_bit = leaf_index // 2 % 2
    merged_three, passed_three = merge_level(
        passed_two, partner_2(passed_two, "leaf", 1), quad_bit == 0, sketch_all, rank_three[leaf_index // 4]
    )
    basis_two = lax.dynamic_slice_in_dim(merged_two, pair_bit * rank_width, rank_width, 0)
    basis_three = lax.dynamic_slice_in_dim(merged_three, quad_bit * rank_width, rank_width, 0)
    top = lax.dynamic_slice_in_dim(passed_three, probe_index * local_probes, local_probes, 0)
    return (own_basis, basis_two, basis_three, top)


def solution(mesh):
    return jax.shard_map(
        on_device,
        mesh=mesh,
        in_specs=(
            P("leaf", None, None),
            P("probe", "leaf"),
            P("leaf", None),
            P("leaf", None),
            P("leaf", None, None),
            P("leaf", None),
            P("probe", "leaf"),
            P("probe", None),
            P("leaf"),
            P(),
            P(),
        ),
        out_specs=(
            P(("leaf", "probe"), None),
            P("leaf", None),
            P("leaf", None),
            P("probe", "leaf"),
        ),
        check_vma=False,
    )
```

```python
import functools

import jax
import jax.numpy as jnp
from jax import lax
from jax.experimental import pallas as pl
from jax.experimental.pallas import tpu as pltpu
from jax.sharding import PartitionSpec as P

highest = lax.Precision.HIGHEST

SLOT_CAP = 8


def partner_2(block, axis, stride):
    count = lax.axis_size(axis)
    route = []
    for low in range(count):
        high = low | 1 << stride
        if high != low and high < count:
            route += [(low, high), (high, low)]
    return lax.ppermute(block, axis, route)


def butterfly_sum(block, axis):
    count = lax.axis_size(axis)
    stride = 0
    while 1 << stride < count:
        block = block + partner_2(block, axis, stride)
        stride += 1
    return block


def ordered_sum(block, axis):
    count = lax.axis_size(axis)
    gathered = gather_rows(block[None], axis)
    total = gathered[0]
    for member in range(1, count):
        total = total + gathered[member]
    return total


def gather_rows(block, axis):
    count = lax.axis_size(axis)
    index = lax.axis_index(axis)
    pieces = [block]
    for shift in range(1, count):
        route = [(j, (j + shift) % count) for j in range(count)]
        pieces.append(lax.ppermute(block, axis, route))
    stacked = jnp.stack(pieces)
    order = (index - jnp.arange(count, dtype=jnp.int32)) % count
    stacked = jnp.take(stacked, order, axis=0)
    return stacked.reshape((count * block.shape[0],) + block.shape[1:])


def extend_add_kernel(count_ref, load_ref, start_ref, out_ref, *, slots, probes):
    source = pl.program_id(0)
    lanes = load_ref.shape[2]
    high_count = out_ref.shape[0] // probes
    info = slots * probes

    @pl.when(source == 0)
    def _():
        out_ref[...] = start_ref[...]

    @pl.when(count_ref[source] > 0)
    def _():
        spread, hot = [], []
        for slot in range(slots):
            high = load_ref[0, pl.ds(info + slot, 1), :].astype(jnp.float32).astype(jnp.int32)
            low = load_ref[0, pl.ds(info + slots + slot, 1), :].astype(jnp.float32).astype(jnp.int32)
            vals = load_ref[0, pl.ds(slot * probes, probes), :]
            zero = jnp.zeros_like(vals)
            spread.append(
                jnp.concatenate([jnp.where(high == h, vals, zero) for h in range(high_count)], axis=0)
            )
            hot.append(
                (lax.broadcasted_iota(jnp.int32, (lanes, lanes), 0) == low).astype(jnp.bfloat16)
            )
        spread = jnp.concatenate(spread, axis=1)
        hot = jnp.concatenate(hot, axis=1)
        out_ref[...] += lax.dot_general(
            spread, hot, (((1,), (1,)), ((), ())), preferred_element_type=jnp.float32
        )


def extend_add(load, counts, start, slots, probes):
    sources, depth, lanes = load.shape
    kernel = functools.partial(extend_add_kernel, slots=slots, probes=probes)
    return pl.pallas_call(
        kernel,
        grid_spec=pltpu.PrefetchScalarGridSpec(
            num_scalar_prefetch=1,
            grid=(sources,),
            in_specs=[
                pl.BlockSpec((1, depth, lanes), lambda s, c: (s, 0, 0)),
                pl.BlockSpec(start.shape, lambda s, c: (0, 0)),
            ],
            out_specs=pl.BlockSpec(start.shape, lambda s, c: (0, 0)),
        ),
        out_shape=jax.ShapeDtypeStruct(start.shape, jnp.float32),
        compiler_params=pltpu.CompilerParams(dimension_semantics=("arbitrary",)),
    )(counts, load, start)


def exchange_shares(block, axis):
    count = lax.axis_size(axis)
    index = lax.axis_index(axis)
    got = [jnp.take(block, index, axis=1)]
    for shift in range(1, count):
        route = [(j, (j + shift) % count) for j in range(count)]
        outgoing = jnp.take(block, (index + shift) % count, axis=1)
        got.append(lax.ppermute(outgoing, axis, route))
    stacked = jnp.stack(got)
    order = (index - jnp.arange(count, dtype=jnp.int32)) % count
    stacked = jnp.take(stacked, order, axis=0)
    return stacked.reshape((count * block.shape[0],) + block.shape[2:])


def cholesky_inverse_kernel(gram_ref, inverse_ref, work_ref, rest_ref):
    order = gram_ref.shape[0]
    tile = 8
    sub = lax.broadcasted_iota(jnp.int32, (order, order), 0)
    lane = lax.broadcasted_iota(jnp.int32, (order, order), 1)
    lane_one = lax.broadcasted_iota(jnp.int32, (1, order), 1)
    work_ref[...] = gram_ref[...]
    rest_ref[...] = jnp.where(sub == lane, 1.0, 0.0).astype(jnp.float32)
    inverse_ref[...] = jnp.zeros_like(inverse_ref)

    for first in range(0, order, tile):
        height = order - first
        tail_lane = lax.broadcasted_iota(jnp.int32, (height, order), 1)
        tail_sub = lax.broadcasted_iota(jnp.int32, (height, 1), 0) + first

        def step(j, carry, first=first, tail_lane=tail_lane, tail_sub=tail_sub):
            work = work_ref[first:, :]
            pivot_row = work_ref[pl.ds(j, 1), :]
            pivot = jnp.sum(jnp.where(lane_one == j, pivot_row, 0.0), axis=1, keepdims=True)
            column = jnp.sum(jnp.where(tail_lane == j, work, 0.0), axis=1, keepdims=True)
            scale = lax.rsqrt(pivot)
            column = jnp.where(tail_sub >= j, column * scale, 0.0)
            row = jnp.where(lane_one >= j, pivot_row * scale, 0.0)
            work_ref[first:, :] = work - column * row
            solved = rest_ref[pl.ds(j, 1), :] * scale
            inverse_ref[pl.ds(j, 1), :] = solved
            rest_ref[first:, :] = rest_ref[first:, :] - column * solved
            return carry

        lax.fori_loop(first, first + tile, step, 0)


def cholesky_inverse(gram_matrix):
    order = gram_matrix.shape[0]
    symmetric = (gram_matrix + gram_matrix.T) * 0.5
    return pl.pallas_call(
        cholesky_inverse_kernel,
        out_shape=jax.ShapeDtypeStruct((order, order), jnp.float32),
        scratch_shapes=[pltpu.VMEM((order, order), jnp.float32)] * 2,
    )(symmetric)


def basis_from_gram(sketched, gram_matrix, rank_limit):
    inverse = cholesky_inverse(gram_matrix)
    orthonormal = jnp.einsum("ra,ba->rb", sketched, inverse, precision=highest)
    columns = jnp.arange(sketched.shape[1], dtype=jnp.int32)
    return jnp.where(columns[None, :] < rank_limit, orthonormal, jnp.zeros_like(orthonormal))


def chol_basis(sketched, rank_limit):
    gram_matrix = jnp.einsum("ra,rb->ab", sketched, sketched, precision=highest)
    return basis_from_gram(sketched, gram_matrix, rank_limit)


def merge_level(own, partner, low_side, sketch_all, rank_limit):
    stacked = jnp.where(
        low_side,
        jnp.concatenate([own, partner], 1),
        jnp.concatenate([partner, own], 1),
    )
    sketched = jnp.einsum("pr,ps->rs", stacked, sketch_all, precision=highest)
    merged = chol_basis(sketched, rank_limit)
    return merged, jnp.dot(stacked, merged, precision=highest)


def on_device(
    child_updates,
    child_probes,
    child_dest,
    child_rows,
    parent_blocks,
    coupling,
    parent_probes,
    sketch,
    rank_one,
    rank_two,
    rank_three,
):
    leaf_count = lax.axis_size("leaf")
    probe_count = lax.axis_size("probe")
    leaf_index = lax.axis_index("leaf")
    probe_index = lax.axis_index("probe")
    local_probes = child_probes.shape[0]
    kid_count = child_updates.shape[0]
    kid_order = child_updates.shape[1]
    block_rows = child_rows.shape[1]
    block_count = child_rows.shape[0]
    front_rows = parent_probes.shape[1]
    rank_width = sketch.shape[1]

    updates = child_updates.reshape(kid_count, kid_order // block_rows, block_rows, kid_order)
    probe_cut = child_probes.reshape(local_probes, kid_count, kid_order)
    sampled = jnp.einsum("pck,cbik->cbpi", probe_cut, updates, preferred_element_type=jnp.float32)
    sampled = sampled.astype(jnp.bfloat16).reshape(block_count, local_probes, block_rows)

    targets = child_dest[:, 0]
    named = (targets[:, None] == jnp.arange(leaf_count, dtype=jnp.int32)[None, :]).astype(jnp.int32)
    earlier = jnp.cumsum(named, axis=0) - named
    slot = jnp.sum(earlier * named, axis=1)
    place = targets * SLOT_CAP + slot
    slot_count = leaf_count * SLOT_CAP
    source = jnp.full((slot_count,), block_count, jnp.int32).at[place].set(
        jnp.arange(block_count, dtype=jnp.int32)
    )
    filled = source < block_count
    source = jnp.minimum(source, block_count - 1)
    high = jnp.where(filled[:, None], child_rows[source] // block_rows, -1)
    low = jnp.where(filled[:, None], child_rows[source] % block_rows, 0)
    send_vals = jnp.where(filled[:, None, None], jnp.take(sampled, source, axis=0), jnp.bfloat16(0))
    half = SLOT_CAP
    info_rows = 16
    loads = []
    for part in range(1):
        picked_slots = slice(part * half, (part + 1) * half)
        vals = send_vals.reshape(leaf_count, SLOT_CAP, local_probes, block_rows)[:, picked_slots]
        info = jnp.concatenate(
            [
                high.reshape(leaf_count, SLOT_CAP, block_rows)[:, picked_slots],
                low.reshape(leaf_count, SLOT_CAP, block_rows)[:, picked_slots],
                jnp.zeros((leaf_count, info_rows - 2 * half, block_rows), jnp.int32),
            ],
            axis=1,
        ).astype(jnp.bfloat16)
        load = jnp.concatenate(
            [vals.reshape(leaf_count, half * local_probes, block_rows), info], axis=1
        )
        loads.append(lax.all_to_all(load, "leaf", 0, 0, tiled=True))

    pieces = parent_probes.reshape(local_probes, front_rows // block_rows, block_rows)
    picked = jnp.take(pieces, coupling[:, 1], axis=1)
    product = jnp.einsum("eik,pek->pei", parent_blocks, picked, preferred_element_type=jnp.float32)
    initial = (
        jnp.zeros(pieces.shape, jnp.float32)
        .at[:, coupling[:, 0]]
        .add(product)
        .reshape(local_probes, front_rows)
    )
    high_count = front_rows // block_rows
    spread = jnp.moveaxis(initial.reshape(local_probes, high_count, block_rows), 1, 0)
    spread = spread.reshape(high_count * local_probes, block_rows)
    for load in loads:
        counts = jnp.sum(load[:, half * local_probes, :1] >= 0, axis=1).astype(jnp.int32)
        spread = extend_add(load, counts, spread, half, local_probes)
    spread = spread.reshape(high_count, local_probes, block_rows)
    sample = jnp.moveaxis(spread, 0, 1).reshape(local_probes, front_rows)

    share_rows = front_rows // probe_count
    sketch_all = gather_rows(sketch, "probe")
    share_sample = exchange_shares(sample.reshape(local_probes, probe_count, share_rows), "probe")
    share_sketched = jnp.einsum("pr,ps->rs", share_sample, sketch_all, precision=highest)
    gram_one = ordered_sum(
        jnp.einsum("ra,rb->ab", share_sketched, share_sketched, precision=highest), "probe"
    )
    own_basis = basis_from_gram(share_sketched, gram_one, rank_one[0])
    passed_one = ordered_sum(jnp.dot(share_sample, own_basis, precision=highest), "probe")

    pair_bit = leaf_index % 2
    merged_two, passed_two = merge_level(
        passed_one, partner_2(passed_one, "leaf", 0), pair_bit == 0, sketch_all, rank_two[leaf_index // 2]
    )
    quad_bit = leaf_index // 2 % 2
    merged_three, passed_three = merge_level(
        passed_two, partner_2(passed_two, "leaf", 1), quad_bit == 0, sketch_all, rank_three[leaf_index // 4]
    )
    basis_two = lax.dynamic_slice_in_dim(merged_two, pair_bit * rank_width, rank_width, 0)
    basis_three = lax.dynamic_slice_in_dim(merged_three, quad_bit * rank_width, rank_width, 0)
    top = lax.dynamic_slice_in_dim(passed_three, probe_index * local_probes, local_probes, 0)
    return (own_basis, basis_two, basis_three, top)


def solution(mesh):
    return jax.shard_map(
        on_device,
        mesh=mesh,
        in_specs=(
            P("leaf", None, None),
            P("probe", "leaf"),
            P("leaf", None),
            P("leaf", None),
            P("leaf", None, None),
            P("leaf", None),
            P("probe", "leaf"),
            P("probe", None),
            P("leaf"),
            P(),
            P(),
        ),
        out_specs=(
            P(("leaf", "probe"), None),
            P("leaf", None),
            P("leaf", None),
            P("probe", "leaf"),
        ),
        check_vma=False,
    )
```

```python
import functools

import jax
import jax.numpy as jnp
from jax import lax
from jax.experimental import pallas as pl
from jax.experimental.pallas import tpu as pltpu
from jax.sharding import PartitionSpec as P

highest = lax.Precision.HIGHEST

SLOT_CAP = 8


def partner_2(block, axis, stride):
    count = lax.axis_size(axis)
    route = []
    for low in range(count):
        high = low | 1 << stride
        if high != low and high < count:
            route += [(low, high), (high, low)]
    return lax.ppermute(block, axis, route)


def butterfly_sum(block, axis):
    count = lax.axis_size(axis)
    stride = 0
    while 1 << stride < count:
        block = block + partner_2(block, axis, stride)
        stride += 1
    return block


def ordered_sum(block, axis):
    count = lax.axis_size(axis)
    gathered = gather_rows(block[None], axis)
    total = gathered[0]
    for member in range(1, count):
        total = total + gathered[member]
    return total


def gather_rows(block, axis):
    count = lax.axis_size(axis)
    index = lax.axis_index(axis)
    pieces = [block]
    for shift in range(1, count):
        route = [(j, (j + shift) % count) for j in range(count)]
        pieces.append(lax.ppermute(block, axis, route))
    stacked = jnp.stack(pieces)
    order = (index - jnp.arange(count, dtype=jnp.int32)) % count
    stacked = jnp.take(stacked, order, axis=0)
    return stacked.reshape((count * block.shape[0],) + block.shape[1:])


def extend_add_kernel(count_ref, load_ref, start_ref, out_ref, *, slots, probes):
    source = pl.program_id(0)
    lanes = load_ref.shape[2]
    high_count = out_ref.shape[0] // probes
    info = slots * probes

    @pl.when(source == 0)
    def _():
        out_ref[...] = start_ref[...]

    @pl.when(count_ref[source] > 0)
    def _():
        spread, hot = [], []
        for slot in range(slots):
            high = load_ref[0, pl.ds(info + slot, 1), :].astype(jnp.float32).astype(jnp.int32)
            low = load_ref[0, pl.ds(info + slots + slot, 1), :].astype(jnp.float32).astype(jnp.int32)
            vals = load_ref[0, pl.ds(slot * probes, probes), :]
            zero = jnp.zeros_like(vals)
            spread.append(
                jnp.concatenate([jnp.where(high == h, vals, zero) for h in range(high_count)], axis=0)
            )
            hot.append(
                (lax.broadcasted_iota(jnp.int32, (lanes, lanes), 0) == low).astype(jnp.bfloat16)
            )
        spread = jnp.concatenate(spread, axis=1)
        hot = jnp.concatenate(hot, axis=1)
        out_ref[...] += lax.dot_general(
            spread, hot, (((1,), (1,)), ((), ())), preferred_element_type=jnp.float32
        )


def extend_add(load, counts, start, slots, probes):
    sources, depth, lanes = load.shape
    kernel = functools.partial(extend_add_kernel, slots=slots, probes=probes)
    return pl.pallas_call(
        kernel,
        grid_spec=pltpu.PrefetchScalarGridSpec(
            num_scalar_prefetch=1,
            grid=(sources,),
            in_specs=[
                pl.BlockSpec((1, depth, lanes), lambda s, c: (s, 0, 0)),
                pl.BlockSpec(start.shape, lambda s, c: (0, 0)),
            ],
            out_specs=pl.BlockSpec(start.shape, lambda s, c: (0, 0)),
        ),
        out_shape=jax.ShapeDtypeStruct(start.shape, jnp.float32),
        compiler_params=pltpu.CompilerParams(dimension_semantics=("arbitrary",)),
    )(counts, load, start)


def exchange_shares(block, axis):
    count = lax.axis_size(axis)
    index = lax.axis_index(axis)
    got = [jnp.take(block, index, axis=1)]
    for shift in range(1, count):
        route = [(j, (j + shift) % count) for j in range(count)]
        outgoing = jnp.take(block, (index + shift) % count, axis=1)
        got.append(lax.ppermute(outgoing, axis, route))
    stacked = jnp.stack(got)
    order = (index - jnp.arange(count, dtype=jnp.int32)) % count
    stacked = jnp.take(stacked, order, axis=0)
    return stacked.reshape((count * block.shape[0],) + block.shape[2:])


def cholesky_inverse_kernel(gram_ref, inverse_ref, work_ref, rest_ref):
    order = gram_ref.shape[0]
    tile = 8
    sub = lax.broadcasted_iota(jnp.int32, (order, order), 0)
    lane = lax.broadcasted_iota(jnp.int32, (order, order), 1)
    lane_one = lax.broadcasted_iota(jnp.int32, (1, order), 1)
    work_ref[...] = gram_ref[...]
    rest_ref[...] = jnp.where(sub == lane, 1.0, 0.0).astype(jnp.float32)
    inverse_ref[...] = jnp.zeros_like(inverse_ref)

    for first in range(0, order, tile):
        height = order - first
        tail_lane = lax.broadcasted_iota(jnp.int32, (height, order), 1)
        tail_sub = lax.broadcasted_iota(jnp.int32, (height, 1), 0) + first

        def step(j, carry, first=first, tail_lane=tail_lane, tail_sub=tail_sub):
            work = work_ref[first:, :]
            pivot_row = work_ref[pl.ds(j, 1), :]
            pivot = jnp.sum(jnp.where(lane_one == j, pivot_row, 0.0), axis=1, keepdims=True)
            column = jnp.sum(jnp.where(tail_lane == j, work, 0.0), axis=1, keepdims=True)
            scale = lax.rsqrt(pivot)
            column = jnp.where(tail_sub >= j, column * scale, 0.0)
            row = jnp.where(lane_one >= j, pivot_row * scale, 0.0)
            work_ref[first:, :] = work - column * row
            solved = rest_ref[pl.ds(j, 1), :] * scale
            inverse_ref[pl.ds(j, 1), :] = solved
            rest_ref[first:, :] = rest_ref[first:, :] - column * solved
            return carry

        lax.fori_loop(first, first + tile, step, 0, unroll=True)


def cholesky_inverse(gram_matrix):
    order = gram_matrix.shape[0]
    symmetric = (gram_matrix + gram_matrix.T) * 0.5
    return pl.pallas_call(
        cholesky_inverse_kernel,
        out_shape=jax.ShapeDtypeStruct((order, order), jnp.float32),
        scratch_shapes=[pltpu.VMEM((order, order), jnp.float32)] * 2,
    )(symmetric)


def basis_from_gram(sketched, gram_matrix, rank_limit):
    inverse = cholesky_inverse(gram_matrix)
    orthonormal = jnp.einsum("ra,ba->rb", sketched, inverse, precision=highest)
    columns = jnp.arange(sketched.shape[1], dtype=jnp.int32)
    return jnp.where(columns[None, :] < rank_limit, orthonormal, jnp.zeros_like(orthonormal))


def chol_basis(sketched, rank_limit):
    gram_matrix = jnp.einsum("ra,rb->ab", sketched, sketched, precision=highest)
    return basis_from_gram(sketched, gram_matrix, rank_limit)


def merge_level(own, partner, low_side, sketch_all, rank_limit):
    stacked = jnp.where(
        low_side,
        jnp.concatenate([own, partner], 1),
        jnp.concatenate([partner, own], 1),
    )
    sketched = jnp.einsum("pr,ps->rs", stacked, sketch_all, precision=highest)
    merged = chol_basis(sketched, rank_limit)
    return merged, jnp.dot(stacked, merged, precision=highest)


def on_device(
    child_updates,
    child_probes,
    child_dest,
    child_rows,
    parent_blocks,
    coupling,
    parent_probes,
    sketch,
    rank_one,
    rank_two,
    rank_three,
):
    leaf_count = lax.axis_size("leaf")
    probe_count = lax.axis_size("probe")
    leaf_index = lax.axis_index("leaf")
    probe_index = lax.axis_index("probe")
    local_probes = child_probes.shape[0]
    kid_count = child_updates.shape[0]
    kid_order = child_updates.shape[1]
    block_rows = child_rows.shape[1]
    block_count = child_rows.shape[0]
    front_rows = parent_probes.shape[1]
    rank_width = sketch.shape[1]

    updates = child_updates.reshape(kid_count, kid_order // block_rows, block_rows, kid_order)
    probe_cut = child_probes.reshape(local_probes, kid_count, kid_order)
    sampled = jnp.einsum("pck,cbik->cbpi", probe_cut, updates, preferred_element_type=jnp.float32)
    sampled = sampled.astype(jnp.bfloat16).reshape(block_count, local_probes, block_rows)

    targets = child_dest[:, 0]
    named = (targets[:, None] == jnp.arange(leaf_count, dtype=jnp.int32)[None, :]).astype(jnp.int32)
    earlier = jnp.cumsum(named, axis=0) - named
    slot = jnp.sum(earlier * named, axis=1)
    place = targets * SLOT_CAP + slot
    slot_count = leaf_count * SLOT_CAP
    source = jnp.full((slot_count,), block_count, jnp.int32).at[place].set(
        jnp.arange(block_count, dtype=jnp.int32)
    )
    filled = source < block_count
    source = jnp.minimum(source, block_count - 1)
    high = jnp.where(filled[:, None], child_rows[source] // block_rows, -1)
    low = jnp.where(filled[:, None], child_rows[source] % block_rows, 0)
    send_vals = jnp.where(filled[:, None, None], jnp.take(sampled, source, axis=0), jnp.bfloat16(0))
    half = SLOT_CAP
    info_rows = 16
    loads = []
    for part in range(1):
        picked_slots = slice(part * half, (part + 1) * half)
        vals = send_vals.reshape(leaf_count, SLOT_CAP, local_probes, block_rows)[:, picked_slots]
        info = jnp.concatenate(
            [
                high.reshape(leaf_count, SLOT_CAP, block_rows)[:, picked_slots],
                low.reshape(leaf_count, SLOT_CAP, block_rows)[:, picked_slots],
                jnp.zeros((leaf_count, info_rows - 2 * half, block_rows), jnp.int32),
            ],
            axis=1,
        ).astype(jnp.bfloat16)
        load = jnp.concatenate(
            [vals.reshape(leaf_count, half * local_probes, block_rows), info], axis=1
        )
        loads.append(lax.all_to_all(load, "leaf", 0, 0, tiled=True))

    pieces = parent_probes.reshape(local_probes, front_rows // block_rows, block_rows)
    picked = jnp.take(pieces, coupling[:, 1], axis=1)
    product = jnp.einsum("eik,pek->pei", parent_blocks, picked, preferred_element_type=jnp.float32)
    initial = (
        jnp.zeros(pieces.shape, jnp.float32)
        .at[:, coupling[:, 0]]
        .add(product)
        .reshape(local_probes, front_rows)
    )
    high_count = front_rows // block_rows
    spread = jnp.moveaxis(initial.reshape(local_probes, high_count, block_rows), 1, 0)
    spread = spread.reshape(high_count * local_probes, block_rows)
    for load in loads:
        counts = jnp.sum(load[:, half * local_probes, :1] >= 0, axis=1).astype(jnp.int32)
        spread = extend_add(load, counts, spread, half, local_probes)
    spread = spread.reshape(high_count, local_probes, block_rows)
    sample = jnp.moveaxis(spread, 0, 1).reshape(local_probes, front_rows)

    share_rows = front_rows // probe_count
    sketch_all = gather_rows(sketch, "probe")
    share_sample = exchange_shares(sample.reshape(local_probes, probe_count, share_rows), "probe")
    share_sketched = jnp.einsum("pr,ps->rs", share_sample, sketch_all, precision=highest)
    gram_one = ordered_sum(
        jnp.einsum("ra,rb->ab", share_sketched, share_sketched, precision=highest), "probe"
    )
    own_basis = basis_from_gram(share_sketched, gram_one, rank_one[0])
    passed_one = ordered_sum(jnp.dot(share_sample, own_basis, precision=highest), "probe")

    pair_bit = leaf_index % 2
    merged_two, passed_two = merge_level(
        passed_one, partner_2(passed_one, "leaf", 0), pair_bit == 0, sketch_all, rank_two[leaf_index // 2]
    )
    quad_bit = leaf_index // 2 % 2
    merged_three, passed_three = merge_level(
        passed_two, partner_2(passed_two, "leaf", 1), quad_bit == 0, sketch_all, rank_three[leaf_index // 4]
    )
    basis_two = lax.dynamic_slice_in_dim(merged_two, pair_bit * rank_width, rank_width, 0)
    basis_three = lax.dynamic_slice_in_dim(merged_three, quad_bit * rank_width, rank_width, 0)
    top = lax.dynamic_slice_in_dim(passed_three, probe_index * local_probes, local_probes, 0)
    return (own_basis, basis_two, basis_three, top)


def solution(mesh):
    return jax.shard_map(
        on_device,
        mesh=mesh,
        in_specs=(
            P("leaf", None, None),
            P("probe", "leaf"),
            P("leaf", None),
            P("leaf", None),
            P("leaf", None, None),
            P("leaf", None),
            P("probe", "leaf"),
            P("probe", None),
            P("leaf"),
            P(),
            P(),
        ),
        out_specs=(
            P(("leaf", "probe"), None),
            P("leaf", None),
            P("leaf", None),
            P("probe", "leaf"),
        ),
        check_vma=False,
    )
```

```python
import functools

import jax
import jax.numpy as jnp
from jax import lax
from jax.experimental import pallas as pl
from jax.experimental.pallas import tpu as pltpu
from jax.sharding import PartitionSpec as P

highest = lax.Precision.HIGHEST

SLOT_CAP = 8


def partner_2(block, axis, stride):
    count = lax.axis_size(axis)
    route = []
    for low in range(count):
        high = low | 1 << stride
        if high != low and high < count:
            route += [(low, high), (high, low)]
    return lax.ppermute(block, axis, route)


def butterfly_sum(block, axis):
    count = lax.axis_size(axis)
    stride = 0
    while 1 << stride < count:
        block = block + partner_2(block, axis, stride)
        stride += 1
    return block


def ordered_sum(block, axis):
    count = lax.axis_size(axis)
    gathered = gather_rows(block[None], axis)
    total = gathered[0]
    for member in range(1, count):
        total = total + gathered[member]
    return total


def gather_rows(block, axis):
    count = lax.axis_size(axis)
    index = lax.axis_index(axis)
    pieces = [block]
    for shift in range(1, count):
        route = [(j, (j + shift) % count) for j in range(count)]
        pieces.append(lax.ppermute(block, axis, route))
    stacked = jnp.stack(pieces)
    order = (index - jnp.arange(count, dtype=jnp.int32)) % count
    stacked = jnp.take(stacked, order, axis=0)
    return stacked.reshape((count * block.shape[0],) + block.shape[1:])


def extend_add_kernel(count_ref, load_ref, start_ref, out_ref, *, slots, probes):
    source = pl.program_id(0)
    lanes = load_ref.shape[2]
    high_count = out_ref.shape[0] // probes
    info = slots * probes

    @pl.when(source == 0)
    def _():
        out_ref[...] = start_ref[...]

    @pl.when(count_ref[source] > 0)
    def _():
        spread, hot = [], []
        for slot in range(slots):
            high = load_ref[0, pl.ds(info + slot, 1), :].astype(jnp.float32).astype(jnp.int32)
            low = load_ref[0, pl.ds(info + slots + slot, 1), :].astype(jnp.float32).astype(jnp.int32)
            vals = load_ref[0, pl.ds(slot * probes, probes), :]
            zero = jnp.zeros_like(vals)
            spread.append(
                jnp.concatenate([jnp.where(high == h, vals, zero) for h in range(high_count)], axis=0)
            )
            hot.append(
                (lax.broadcasted_iota(jnp.int32, (lanes, lanes), 0) == low).astype(jnp.bfloat16)
            )
        spread = jnp.concatenate(spread, axis=1)
        hot = jnp.concatenate(hot, axis=1)
        out_ref[...] += lax.dot_general(
            spread, hot, (((1,), (1,)), ((), ())), preferred_element_type=jnp.float32
        )


def extend_add(load, counts, start, slots, probes):
    sources, depth, lanes = load.shape
    kernel = functools.partial(extend_add_kernel, slots=slots, probes=probes)
    return pl.pallas_call(
        kernel,
        grid_spec=pltpu.PrefetchScalarGridSpec(
            num_scalar_prefetch=1,
            grid=(sources,),
            in_specs=[
                pl.BlockSpec((1, depth, lanes), lambda s, c: (s, 0, 0)),
                pl.BlockSpec(start.shape, lambda s, c: (0, 0)),
            ],
            out_specs=pl.BlockSpec(start.shape, lambda s, c: (0, 0)),
        ),
        out_shape=jax.ShapeDtypeStruct(start.shape, jnp.float32),
        compiler_params=pltpu.CompilerParams(dimension_semantics=("arbitrary",)),
    )(counts, load, start)


def exchange_shares(block, axis):
    count = lax.axis_size(axis)
    index = lax.axis_index(axis)
    got = [jnp.take(block, index, axis=1)]
    for shift in range(1, count):
        route = [(j, (j + shift) % count) for j in range(count)]
        outgoing = jnp.take(block, (index + shift) % count, axis=1)
        got.append(lax.ppermute(outgoing, axis, route))
    stacked = jnp.stack(got)
    order = (index - jnp.arange(count, dtype=jnp.int32)) % count
    stacked = jnp.take(stacked, order, axis=0)
    return stacked.reshape((count * block.shape[0],) + block.shape[2:])


def cholesky_inverse_kernel(gram_ref, inverse_ref, work_ref, rest_ref):
    order = gram_ref.shape[0]
    tile = 8
    sub = lax.broadcasted_iota(jnp.int32, (order, order), 0)
    lane = lax.broadcasted_iota(jnp.int32, (order, order), 1)
    lane_one = lax.broadcasted_iota(jnp.int32, (1, order), 1)
    work_ref[...] = gram_ref[...]
    rest_ref[...] = jnp.where(sub == lane, 1.0, 0.0).astype(jnp.float32)
    inverse_ref[...] = jnp.zeros_like(inverse_ref)

    for first in range(0, order, tile):
        height = order - first
        tail_lane = lax.broadcasted_iota(jnp.int32, (height, order), 1)
        tail_sub = lax.broadcasted_iota(jnp.int32, (height, 1), 0) + first

        def step(j, carry, first=first, tail_lane=tail_lane, tail_sub=tail_sub):
            work = work_ref[first:, :]
            pivot_row = work_ref[pl.ds(j, 1), :]
            pivot = jnp.sum(jnp.where(lane_one == j, pivot_row, 0.0), axis=1, keepdims=True)
            column = jnp.sum(jnp.where(tail_lane == j, work, 0.0), axis=1, keepdims=True)
            scale = lax.rsqrt(pivot)
            column = jnp.where(tail_sub >= j, column * scale, 0.0)
            row = jnp.where(lane_one >= j, pivot_row * scale, 0.0)
            work_ref[first:, :] = work - column * row
            solved = rest_ref[pl.ds(j, 1), :] * scale
            inverse_ref[pl.ds(j, 1), :] = solved
            rest_ref[first:, :] = rest_ref[first:, :] - column * solved
            return carry

        lax.fori_loop(first, first + tile, step, 0, unroll=True)


def cholesky_inverse(gram_matrix):
    order = gram_matrix.shape[0]
    symmetric = (gram_matrix + gram_matrix.T) * 0.5
    return pl.pallas_call(
        cholesky_inverse_kernel,
        out_shape=jax.ShapeDtypeStruct((order, order), jnp.float32),
        scratch_shapes=[pltpu.VMEM((order, order), jnp.float32)] * 2,
    )(symmetric)


def basis_from_gram(sketched, gram_matrix, rank_limit):
    inverse = cholesky_inverse(gram_matrix)
    orthonormal = jnp.einsum("ra,ba->rb", sketched, inverse, precision=highest)
    columns = jnp.arange(sketched.shape[1], dtype=jnp.int32)
    return jnp.where(columns[None, :] < rank_limit, orthonormal, jnp.zeros_like(orthonormal))


def chol_basis(sketched, rank_limit):
    gram_matrix = jnp.einsum("ra,rb->ab", sketched, sketched, precision=highest)
    return basis_from_gram(sketched, gram_matrix, rank_limit)


def merge_level(own, partner, low_side, sketch_all, rank_limit):
    stacked = jnp.where(
        low_side,
        jnp.concatenate([own, partner], 1),
        jnp.concatenate([partner, own], 1),
    )
    sketched = jnp.einsum("pr,ps->rs", stacked, sketch_all, precision=highest)
    merged = chol_basis(sketched, rank_limit)
    return merged, jnp.dot(stacked, merged, precision=highest)


def on_device(
    child_updates,
    child_probes,
    child_dest,
    child_rows,
    parent_blocks,
    coupling,
    parent_probes,
    sketch,
    rank_one,
    rank_two,
    rank_three,
):
    leaf_count = lax.axis_size("leaf")
    probe_count = lax.axis_size("probe")
    leaf_index = lax.axis_index("leaf")
    probe_index = lax.axis_index("probe")
    local_probes = child_probes.shape[0]
    kid_count = child_updates.shape[0]
    kid_order = child_updates.shape[1]
    block_rows = child_rows.shape[1]
    block_count = child_rows.shape[0]
    front_rows = parent_probes.shape[1]
    rank_width = sketch.shape[1]

    updates = child_updates.reshape(kid_count, kid_order // block_rows, block_rows, kid_order)
    probe_cut = child_probes.reshape(local_probes, kid_count, kid_order)
    sampled = jnp.einsum("pck,cbik->cbpi", probe_cut, updates, preferred_element_type=jnp.float32)
    sampled = sampled.astype(jnp.bfloat16).reshape(block_count, local_probes, block_rows)

    targets = child_dest[:, 0]
    named = (targets[:, None] == jnp.arange(leaf_count, dtype=jnp.int32)[None, :]).astype(jnp.int32)
    earlier = jnp.cumsum(named, axis=0) - named
    slot = jnp.sum(earlier * named, axis=1)
    place = targets * SLOT_CAP + slot
    slot_count = leaf_count * SLOT_CAP
    source = jnp.full((slot_count,), block_count, jnp.int32).at[place].set(
        jnp.arange(block_count, dtype=jnp.int32)
    )
    filled = source < block_count
    source = jnp.minimum(source, block_count - 1)
    high = jnp.where(filled[:, None], child_rows[source] // block_rows, -1)
    low = jnp.where(filled[:, None], child_rows[source] % block_rows, 0)
    send_vals = jnp.take(sampled, source, axis=0)
    half = SLOT_CAP
    info_rows = 16
    loads = []
    for part in range(1):
        picked_slots = slice(part * half, (part + 1) * half)
        vals = send_vals.reshape(leaf_count, SLOT_CAP, local_probes, block_rows)[:, picked_slots]
        info = jnp.concatenate(
            [
                high.reshape(leaf_count, SLOT_CAP, block_rows)[:, picked_slots],
                low.reshape(leaf_count, SLOT_CAP, block_rows)[:, picked_slots],
                jnp.zeros((leaf_count, info_rows - 2 * half, block_rows), jnp.int32),
            ],
            axis=1,
        ).astype(jnp.bfloat16)
        load = jnp.concatenate(
            [vals.reshape(leaf_count, half * local_probes, block_rows), info], axis=1
        )
        loads.append(lax.all_to_all(load, "leaf", 0, 0, tiled=True))

    pieces = parent_probes.reshape(local_probes, front_rows // block_rows, block_rows)
    picked = jnp.take(pieces, coupling[:, 1], axis=1)
    product = jnp.einsum("eik,pek->pei", parent_blocks, picked, preferred_element_type=jnp.float32)
    initial = (
        jnp.zeros(pieces.shape, jnp.float32)
        .at[:, coupling[:, 0]]
        .add(product)
        .reshape(local_probes, front_rows)
    )
    high_count = front_rows // block_rows
    spread = jnp.moveaxis(initial.reshape(local_probes, high_count, block_rows), 1, 0)
    spread = spread.reshape(high_count * local_probes, block_rows)
    for load in loads:
        counts = jnp.sum(load[:, half * local_probes, :1] >= 0, axis=1).astype(jnp.int32)
        spread = extend_add(load, counts, spread, half, local_probes)
    spread = spread.reshape(high_count, local_probes, block_rows)
    sample = jnp.moveaxis(spread, 0, 1).reshape(local_probes, front_rows)

    share_rows = front_rows // probe_count
    sketch_all = gather_rows(sketch, "probe")
    share_sample = exchange_shares(sample.reshape(local_probes, probe_count, share_rows), "probe")
    share_sketched = jnp.einsum("pr,ps->rs", share_sample, sketch_all, precision=highest)
    gram_one = ordered_sum(
        jnp.einsum("ra,rb->ab", share_sketched, share_sketched, precision=highest), "probe"
    )
    own_basis = basis_from_gram(share_sketched, gram_one, rank_one[0])
    passed_one = ordered_sum(jnp.dot(share_sample, own_basis, precision=highest), "probe")

    pair_bit = leaf_index % 2
    merged_two, passed_two = merge_level(
        passed_one, partner_2(passed_one, "leaf", 0), pair_bit == 0, sketch_all, rank_two[leaf_index // 2]
    )
    quad_bit = leaf_index // 2 % 2
    merged_three, passed_three = merge_level(
        passed_two, partner_2(passed_two, "leaf", 1), quad_bit == 0, sketch_all, rank_three[leaf_index // 4]
    )
    basis_two = lax.dynamic_slice_in_dim(merged_two, pair_bit * rank_width, rank_width, 0)
    basis_three = lax.dynamic_slice_in_dim(merged_three, quad_bit * rank_width, rank_width, 0)
    top = lax.dynamic_slice_in_dim(passed_three, probe_index * local_probes, local_probes, 0)
    return (own_basis, basis_two, basis_three, top)


def solution(mesh):
    return jax.shard_map(
        on_device,
        mesh=mesh,
        in_specs=(
            P("leaf", None, None),
            P("probe", "leaf"),
            P("leaf", None),
            P("leaf", None),
            P("leaf", None, None),
            P("leaf", None),
            P("probe", "leaf"),
            P("probe", None),
            P("leaf"),
            P(),
            P(),
        ),
        out_specs=(
            P(("leaf", "probe"), None),
            P("leaf", None),
            P("leaf", None),
            P("probe", "leaf"),
        ),
        check_vma=False,
    )
```

```python
import functools

import jax
import jax.numpy as jnp
from jax import lax
from jax.experimental import pallas as pl
from jax.experimental.pallas import tpu as pltpu
from jax.sharding import PartitionSpec as P

highest = lax.Precision.HIGHEST

SLOT_CAP = 8


def partner_2(block, axis, stride):
    count = lax.axis_size(axis)
    route = []
    for low in range(count):
        high = low | 1 << stride
        if high != low and high < count:
            route += [(low, high), (high, low)]
    return lax.ppermute(block, axis, route)


def butterfly_sum(block, axis):
    count = lax.axis_size(axis)
    stride = 0
    while 1 << stride < count:
        block = block + partner_2(block, axis, stride)
        stride += 1
    return block


def ordered_sum(block, axis):
    count = lax.axis_size(axis)
    gathered = gather_rows(block[None], axis)
    total = gathered[0]
    for member in range(1, count):
        total = total + gathered[member]
    return total


def gather_rows(block, axis):
    count = lax.axis_size(axis)
    index = lax.axis_index(axis)
    pieces = [block]
    for shift in range(1, count):
        route = [(j, (j + shift) % count) for j in range(count)]
        pieces.append(lax.ppermute(block, axis, route))
    stacked = jnp.stack(pieces)
    order = (index - jnp.arange(count, dtype=jnp.int32)) % count
    stacked = jnp.take(stacked, order, axis=0)
    return stacked.reshape((count * block.shape[0],) + block.shape[1:])


def extend_add_kernel(count_ref, load_ref, start_ref, out_ref, *, slots, probes):
    source = pl.program_id(0)
    lanes = load_ref.shape[2]
    high_count = out_ref.shape[0] // probes
    info = slots * probes

    @pl.when(source == 0)
    def _():
        out_ref[...] = start_ref[...]

    @pl.when(count_ref[source] > 0)
    def _():
        spread, hot = [], []
        for slot in range(slots):
            high = load_ref[0, pl.ds(info + slot, 1), :].astype(jnp.float32).astype(jnp.int32)
            low = load_ref[0, pl.ds(info + slots + slot, 1), :].astype(jnp.float32).astype(jnp.int32)
            vals = load_ref[0, pl.ds(slot * probes, probes), :]
            zero = jnp.zeros_like(vals)
            spread.append(
                jnp.concatenate([jnp.where(high == h, vals, zero) for h in range(high_count)], axis=0)
            )
            hot.append(
                (lax.broadcasted_iota(jnp.int32, (lanes, lanes), 0) == low).astype(jnp.bfloat16)
            )
        spread = jnp.concatenate(spread, axis=1)
        hot = jnp.concatenate(hot, axis=1)
        out_ref[...] += lax.dot_general(
            spread, hot, (((1,), (1,)), ((), ())), preferred_element_type=jnp.float32
        )


def extend_add(load, counts, start, slots, probes):
    sources, depth, lanes = load.shape
    kernel = functools.partial(extend_add_kernel, slots=slots, probes=probes)
    return pl.pallas_call(
        kernel,
        grid_spec=pltpu.PrefetchScalarGridSpec(
            num_scalar_prefetch=1,
            grid=(sources,),
            in_specs=[
                pl.BlockSpec((1, depth, lanes), lambda s, c: (s, 0, 0)),
                pl.BlockSpec(start.shape, lambda s, c: (0, 0)),
            ],
            out_specs=pl.BlockSpec(start.shape, lambda s, c: (0, 0)),
        ),
        out_shape=jax.ShapeDtypeStruct(start.shape, jnp.float32),
        compiler_params=pltpu.CompilerParams(dimension_semantics=("arbitrary",)),
    )(counts, load, start)


def exchange_shares(block, axis):
    count = lax.axis_size(axis)
    index = lax.axis_index(axis)
    got = [jnp.take(block, index, axis=1)]
    for shift in range(1, count):
        route = [(j, (j + shift) % count) for j in range(count)]
        outgoing = jnp.take(block, (index + shift) % count, axis=1)
        got.append(lax.ppermute(outgoing, axis, route))
    stacked = jnp.stack(got)
    order = (index - jnp.arange(count, dtype=jnp.int32)) % count
    stacked = jnp.take(stacked, order, axis=0)
    return stacked.reshape((count * block.shape[0],) + block.shape[2:])


def cholesky_inverse_kernel(gram_ref, inverse_ref, work_ref, rest_ref):
    order = gram_ref.shape[0]
    tile = 8
    sub = lax.broadcasted_iota(jnp.int32, (order, order), 0)
    lane = lax.broadcasted_iota(jnp.int32, (order, order), 1)
    lane_one = lax.broadcasted_iota(jnp.int32, (1, order), 1)
    work_ref[...] = gram_ref[...]
    rest_ref[...] = jnp.where(sub == lane, 1.0, 0.0).astype(jnp.float32)
    inverse_ref[...] = jnp.zeros_like(inverse_ref)

    for first in range(0, order, tile):
        height = order - first
        tail_lane = lax.broadcasted_iota(jnp.int32, (height, order), 1)
        tail_sub = lax.broadcasted_iota(jnp.int32, (height, 1), 0) + first

        def step(j, carry, first=first, tail_lane=tail_lane, tail_sub=tail_sub):
            work = work_ref[first:, :]
            pivot_row = work_ref[pl.ds(j, 1), :]
            pivot = jnp.sum(jnp.where(lane_one == j, pivot_row, 0.0), axis=1, keepdims=True)
            kept = jnp.where(lane_one >= j, pivot_row, 0.0)
            column = jnp.transpose(jnp.broadcast_to(kept, (tile, order)))[first:, 0:1]
            scale = lax.rsqrt(pivot)
            column = column * scale
            row = kept * scale
            work_ref[first:, :] = work - column * row
            solved = rest_ref[pl.ds(j, 1), :] * scale
            inverse_ref[pl.ds(j, 1), :] = solved
            rest_ref[first:, :] = rest_ref[first:, :] - column * solved
            return carry

        lax.fori_loop(first, first + tile, step, 0, unroll=True)


def cholesky_inverse(gram_matrix):
    order = gram_matrix.shape[0]
    symmetric = (gram_matrix + gram_matrix.T) * 0.5
    return pl.pallas_call(
        cholesky_inverse_kernel,
        out_shape=jax.ShapeDtypeStruct((order, order), jnp.float32),
        scratch_shapes=[pltpu.VMEM((order, order), jnp.float32)] * 2,
    )(symmetric)


def basis_from_gram(sketched, gram_matrix, rank_limit):
    inverse = cholesky_inverse(gram_matrix)
    orthonormal = jnp.einsum("ra,ba->rb", sketched, inverse, precision=highest)
    columns = jnp.arange(sketched.shape[1], dtype=jnp.int32)
    return jnp.where(columns[None, :] < rank_limit, orthonormal, jnp.zeros_like(orthonormal))


def chol_basis(sketched, rank_limit):
    gram_matrix = jnp.einsum("ra,rb->ab", sketched, sketched, precision=highest)
    return basis_from_gram(sketched, gram_matrix, rank_limit)


def merge_level(own, partner, low_side, sketch_all, rank_limit):
    stacked = jnp.where(
        low_side,
        jnp.concatenate([own, partner], 1),
        jnp.concatenate([partner, own], 1),
    )
    sketched = jnp.einsum("pr,ps->rs", stacked, sketch_all, precision=highest)
    merged = chol_basis(sketched, rank_limit)
    return merged, jnp.dot(stacked, merged, precision=highest)


def on_device(
    child_updates,
    child_probes,
    child_dest,
    child_rows,
    parent_blocks,
    coupling,
    parent_probes,
    sketch,
    rank_one,
    rank_two,
    rank_three,
):
    leaf_count = lax.axis_size("leaf")
    probe_count = lax.axis_size("probe")
    leaf_index = lax.axis_index("leaf")
    probe_index = lax.axis_index("probe")
    local_probes = child_probes.shape[0]
    kid_count = child_updates.shape[0]
    kid_order = child_updates.shape[1]
    block_rows = child_rows.shape[1]
    block_count = child_rows.shape[0]
    front_rows = parent_probes.shape[1]
    rank_width = sketch.shape[1]

    updates = child_updates.reshape(kid_count, kid_order // block_rows, block_rows, kid_order)
    probe_cut = child_probes.reshape(local_probes, kid_count, kid_order)
    sampled = jnp.einsum("pck,cbik->cbpi", probe_cut, updates, preferred_element_type=jnp.float32)
    sampled = sampled.astype(jnp.bfloat16).reshape(block_count, local_probes, block_rows)

    targets = child_dest[:, 0]
    named = (targets[:, None] == jnp.arange(leaf_count, dtype=jnp.int32)[None, :]).astype(jnp.int32)
    earlier = jnp.cumsum(named, axis=0) - named
    slot = jnp.sum(earlier * named, axis=1)
    place = targets * SLOT_CAP + slot
    slot_count = leaf_count * SLOT_CAP
    source = jnp.full((slot_count,), block_count, jnp.int32).at[place].set(
        jnp.arange(block_count, dtype=jnp.int32)
    )
    filled = source < block_count
    source = jnp.minimum(source, block_count - 1)
    high = jnp.where(filled[:, None], child_rows[source] // block_rows, -1)
    low = jnp.where(filled[:, None], child_rows[source] % block_rows, 0)
    send_vals = jnp.take(sampled, source, axis=0)
    half = SLOT_CAP
    info_rows = 16
    loads = []
    for part in range(1):
        picked_slots = slice(part * half, (part + 1) * half)
        vals = send_vals.reshape(leaf_count, SLOT_CAP, local_probes, block_rows)[:, picked_slots]
        info = jnp.concatenate(
            [
                high.reshape(leaf_count, SLOT_CAP, block_rows)[:, picked_slots],
                low.reshape(leaf_count, SLOT_CAP, block_rows)[:, picked_slots],
                jnp.zeros((leaf_count, info_rows - 2 * half, block_rows), jnp.int32),
            ],
            axis=1,
        ).astype(jnp.bfloat16)
        load = jnp.concatenate(
            [vals.reshape(leaf_count, half * local_probes, block_rows), info], axis=1
        )
        loads.append(lax.all_to_all(load, "leaf", 0, 0, tiled=True))

    pieces = parent_probes.reshape(local_probes, front_rows // block_rows, block_rows)
    picked = jnp.take(pieces, coupling[:, 1], axis=1)
    product = jnp.einsum("eik,pek->pei", parent_blocks, picked, preferred_element_type=jnp.float32)
    initial = (
        jnp.zeros(pieces.shape, jnp.float32)
        .at[:, coupling[:, 0]]
        .add(product)
        .reshape(local_probes, front_rows)
    )
    high_count = front_rows // block_rows
    spread = jnp.moveaxis(initial.reshape(local_probes, high_count, block_rows), 1, 0)
    spread = spread.reshape(high_count * local_probes, block_rows)
    for load in loads:
        counts = jnp.sum(load[:, half * local_probes, :1] >= 0, axis=1).astype(jnp.int32)
        spread = extend_add(load, counts, spread, half, local_probes)
    spread = spread.reshape(high_count, local_probes, block_rows)
    sample = jnp.moveaxis(spread, 0, 1).reshape(local_probes, front_rows)

    share_rows = front_rows // probe_count
    sketch_all = gather_rows(sketch, "probe")
    share_sample = exchange_shares(sample.reshape(local_probes, probe_count, share_rows), "probe")
    share_sketched = jnp.einsum("pr,ps->rs", share_sample, sketch_all, precision=highest)
    gram_one = ordered_sum(
        jnp.einsum("ra,rb->ab", share_sketched, share_sketched, precision=highest), "probe"
    )
    own_basis = basis_from_gram(share_sketched, gram_one, rank_one[0])
    passed_one = ordered_sum(jnp.dot(share_sample, own_basis, precision=highest), "probe")

    pair_bit = leaf_index % 2
    merged_two, passed_two = merge_level(
        passed_one, partner_2(passed_one, "leaf", 0), pair_bit == 0, sketch_all, rank_two[leaf_index // 2]
    )
    quad_bit = leaf_index // 2 % 2
    merged_three, passed_three = merge_level(
        passed_two, partner_2(passed_two, "leaf", 1), quad_bit == 0, sketch_all, rank_three[leaf_index // 4]
    )
    basis_two = lax.dynamic_slice_in_dim(merged_two, pair_bit * rank_width, rank_width, 0)
    basis_three = lax.dynamic_slice_in_dim(merged_three, quad_bit * rank_width, rank_width, 0)
    top = lax.dynamic_slice_in_dim(passed_three, probe_index * local_probes, local_probes, 0)
    return (own_basis, basis_two, basis_three, top)


def solution(mesh):
    return jax.shard_map(
        on_device,
        mesh=mesh,
        in_specs=(
            P("leaf", None, None),
            P("probe", "leaf"),
            P("leaf", None),
            P("leaf", None),
            P("leaf", None, None),
            P("leaf", None),
            P("probe", "leaf"),
            P("probe", None),
            P("leaf"),
            P(),
            P(),
        ),
        out_specs=(
            P(("leaf", "probe"), None),
            P("leaf", None),
            P("leaf", None),
            P("probe", "leaf"),
        ),
        check_vma=False,
    )
```

```python
import functools

import jax
import jax.numpy as jnp
from jax import lax
from jax.experimental import pallas as pl
from jax.experimental.pallas import tpu as pltpu
from jax.sharding import PartitionSpec as P

highest = lax.Precision.HIGHEST

SLOT_CAP = 8


def partner_2(block, axis, stride):
    count = lax.axis_size(axis)
    route = []
    for low in range(count):
        high = low | 1 << stride
        if high != low and high < count:
            route += [(low, high), (high, low)]
    return lax.ppermute(block, axis, route)


def butterfly_sum(block, axis):
    count = lax.axis_size(axis)
    stride = 0
    while 1 << stride < count:
        block = block + partner_2(block, axis, stride)
        stride += 1
    return block


def ordered_sum(block, axis):
    count = lax.axis_size(axis)
    gathered = gather_rows(block[None], axis)
    total = gathered[0]
    for member in range(1, count):
        total = total + gathered[member]
    return total


def gather_rows(block, axis):
    count = lax.axis_size(axis)
    index = lax.axis_index(axis)
    pieces = [block]
    for shift in range(1, count):
        route = [(j, (j + shift) % count) for j in range(count)]
        pieces.append(lax.ppermute(block, axis, route))
    stacked = jnp.stack(pieces)
    order = (index - jnp.arange(count, dtype=jnp.int32)) % count
    stacked = jnp.take(stacked, order, axis=0)
    return stacked.reshape((count * block.shape[0],) + block.shape[1:])


def extend_add_kernel(count_ref, load_ref, start_ref, out_ref, *, slots, probes):
    source = pl.program_id(0)
    lanes = load_ref.shape[2]
    width = out_ref.shape[1]
    high_count = out_ref.shape[0] // probes
    info = slots * probes

    @pl.when(source == 0)
    def _():
        out_ref[...] = start_ref[...]

    @pl.when(count_ref[source] > 0)
    def _():
        spread, hot = [], []
        for slot in range(slots):
            high = load_ref[0, pl.ds(info + slot, 1), :].astype(jnp.float32).astype(jnp.int32)
            low = load_ref[0, pl.ds(info + slots + slot, 1), :].astype(jnp.float32).astype(jnp.int32)
            target = high * lanes + low
            block = jnp.where(target >= 0, target // width, -1)
            offset = target % width
            vals = load_ref[0, pl.ds(slot * probes, probes), :]
            zero = jnp.zeros_like(vals)
            spread.append(
                jnp.concatenate([jnp.where(block == h, vals, zero) for h in range(high_count)], axis=0)
            )
            hot.append(
                (lax.broadcasted_iota(jnp.int32, (width, lanes), 0) == offset).astype(jnp.bfloat16)
            )
        spread = jnp.concatenate(spread, axis=1)
        hot = jnp.concatenate(hot, axis=1)
        out_ref[...] += lax.dot_general(
            spread, hot, (((1,), (1,)), ((), ())), preferred_element_type=jnp.float32
        )


def extend_add(load, counts, start, slots, probes):
    sources, depth, lanes = load.shape
    kernel = functools.partial(extend_add_kernel, slots=slots, probes=probes)
    return pl.pallas_call(
        kernel,
        grid_spec=pltpu.PrefetchScalarGridSpec(
            num_scalar_prefetch=1,
            grid=(sources,),
            in_specs=[
                pl.BlockSpec((1, depth, lanes), lambda s, c: (s, 0, 0)),
                pl.BlockSpec(start.shape, lambda s, c: (0, 0)),
            ],
            out_specs=pl.BlockSpec(start.shape, lambda s, c: (0, 0)),
        ),
        out_shape=jax.ShapeDtypeStruct(start.shape, jnp.float32),
        compiler_params=pltpu.CompilerParams(dimension_semantics=("arbitrary",)),
    )(counts, load, start)


def exchange_shares(block, axis):
    count = lax.axis_size(axis)
    index = lax.axis_index(axis)
    got = [jnp.take(block, index, axis=1)]
    for shift in range(1, count):
        route = [(j, (j + shift) % count) for j in range(count)]
        outgoing = jnp.take(block, (index + shift) % count, axis=1)
        got.append(lax.ppermute(outgoing, axis, route))
    stacked = jnp.stack(got)
    order = (index - jnp.arange(count, dtype=jnp.int32)) % count
    stacked = jnp.take(stacked, order, axis=0)
    return stacked.reshape((count * block.shape[0],) + block.shape[2:])


def cholesky_inverse_kernel(gram_ref, inverse_ref, work_ref, rest_ref):
    order = gram_ref.shape[0]
    tile = 8
    sub = lax.broadcasted_iota(jnp.int32, (order, order), 0)
    lane = lax.broadcasted_iota(jnp.int32, (order, order), 1)
    lane_one = lax.broadcasted_iota(jnp.int32, (1, order), 1)
    work_ref[...] = gram_ref[...]
    rest_ref[...] = jnp.where(sub == lane, 1.0, 0.0).astype(jnp.float32)
    inverse_ref[...] = jnp.zeros_like(inverse_ref)

    for first in range(0, order, tile):
        height = order - first
        tail_lane = lax.broadcasted_iota(jnp.int32, (height, order), 1)
        tail_sub = lax.broadcasted_iota(jnp.int32, (height, 1), 0) + first

        def step(j, carry, first=first, tail_lane=tail_lane, tail_sub=tail_sub):
            work = work_ref[first:, :]
            pivot_row = work_ref[pl.ds(j, 1), :]
            pivot = jnp.sum(jnp.where(lane_one == j, pivot_row, 0.0), axis=1, keepdims=True)
            column = jnp.sum(jnp.where(tail_lane == j, work, 0.0), axis=1, keepdims=True)
            scale = lax.rsqrt(pivot)
            column = jnp.where(tail_sub >= j, column * scale, 0.0)
            row = jnp.where(lane_one >= j, pivot_row * scale, 0.0)
            work_ref[first:, :] = work - column * row
            solved = rest_ref[pl.ds(j, 1), :] * scale
            inverse_ref[pl.ds(j, 1), :] = solved
            rest_ref[first:, :] = rest_ref[first:, :] - column * solved
            return carry

        lax.fori_loop(first, first + tile, step, 0, unroll=True)


def cholesky_inverse(gram_matrix):
    order = gram_matrix.shape[0]
    symmetric = (gram_matrix + gram_matrix.T) * 0.5
    return pl.pallas_call(
        cholesky_inverse_kernel,
        out_shape=jax.ShapeDtypeStruct((order, order), jnp.float32),
        scratch_shapes=[pltpu.VMEM((order, order), jnp.float32)] * 2,
    )(symmetric)


def basis_from_gram(sketched, gram_matrix, rank_limit):
    inverse = cholesky_inverse(gram_matrix)
    orthonormal = jnp.einsum("ra,ba->rb", sketched, inverse, precision=highest)
    columns = jnp.arange(sketched.shape[1], dtype=jnp.int32)
    return jnp.where(columns[None, :] < rank_limit, orthonormal, jnp.zeros_like(orthonormal))


def chol_basis(sketched, rank_limit):
    gram_matrix = jnp.einsum("ra,rb->ab", sketched, sketched, precision=highest)
    return basis_from_gram(sketched, gram_matrix, rank_limit)


def merge_level(own, partner, low_side, sketch_all, rank_limit):
    stacked = jnp.where(
        low_side,
        jnp.concatenate([own, partner], 1),
        jnp.concatenate([partner, own], 1),
    )
    sketched = jnp.einsum("pr,ps->rs", stacked, sketch_all, precision=highest)
    merged = chol_basis(sketched, rank_limit)
    return merged, jnp.dot(stacked, merged, precision=highest)


def on_device(
    child_updates,
    child_probes,
    child_dest,
    child_rows,
    parent_blocks,
    coupling,
    parent_probes,
    sketch,
    rank_one,
    rank_two,
    rank_three,
):
    leaf_count = lax.axis_size("leaf")
    probe_count = lax.axis_size("probe")
    leaf_index = lax.axis_index("leaf")
    probe_index = lax.axis_index("probe")
    local_probes = child_probes.shape[0]
    kid_count = child_updates.shape[0]
    kid_order = child_updates.shape[1]
    block_rows = child_rows.shape[1]
    block_count = child_rows.shape[0]
    front_rows = parent_probes.shape[1]
    rank_width = sketch.shape[1]

    updates = child_updates.reshape(kid_count, kid_order // block_rows, block_rows, kid_order)
    probe_cut = child_probes.reshape(local_probes, kid_count, kid_order)
    sampled = jnp.einsum("pck,cbik->cbpi", probe_cut, updates, preferred_element_type=jnp.float32)
    sampled = sampled.astype(jnp.bfloat16).reshape(block_count, local_probes, block_rows)

    targets = child_dest[:, 0]
    named = (targets[:, None] == jnp.arange(leaf_count, dtype=jnp.int32)[None, :]).astype(jnp.int32)
    earlier = jnp.cumsum(named, axis=0) - named
    slot = jnp.sum(earlier * named, axis=1)
    place = targets * SLOT_CAP + slot
    slot_count = leaf_count * SLOT_CAP
    source = jnp.full((slot_count,), block_count, jnp.int32).at[place].set(
        jnp.arange(block_count, dtype=jnp.int32)
    )
    filled = source < block_count
    source = jnp.minimum(source, block_count - 1)
    high = jnp.where(filled[:, None], child_rows[source] // block_rows, -1)
    low = jnp.where(filled[:, None], child_rows[source] % block_rows, 0)
    send_vals = jnp.take(sampled, source, axis=0)
    half = SLOT_CAP
    info_rows = 16
    loads = []
    for part in range(1):
        picked_slots = slice(part * half, (part + 1) * half)
        vals = send_vals.reshape(leaf_count, SLOT_CAP, local_probes, block_rows)[:, picked_slots]
        info = jnp.concatenate(
            [
                high.reshape(leaf_count, SLOT_CAP, block_rows)[:, picked_slots],
                low.reshape(leaf_count, SLOT_CAP, block_rows)[:, picked_slots],
                jnp.zeros((leaf_count, info_rows - 2 * half, block_rows), jnp.int32),
            ],
            axis=1,
        ).astype(jnp.bfloat16)
        load = jnp.concatenate(
            [vals.reshape(leaf_count, half * local_probes, block_rows), info], axis=1
        )
        loads.append(lax.all_to_all(load, "leaf", 0, 0, tiled=True))

    pieces = parent_probes.reshape(local_probes, front_rows // block_rows, block_rows)
    picked = jnp.take(pieces, coupling[:, 1], axis=1)
    product = jnp.einsum("eik,pek->pei", parent_blocks, picked, preferred_element_type=jnp.float32)
    initial = (
        jnp.zeros(pieces.shape, jnp.float32)
        .at[:, coupling[:, 0]]
        .add(product)
        .reshape(local_probes, front_rows)
    )
    width = 2 * block_rows
    high_count = front_rows // width
    spread = jnp.moveaxis(initial.reshape(local_probes, high_count, width), 1, 0)
    spread = spread.reshape(high_count * local_probes, width)
    for load in loads:
        counts = jnp.sum(load[:, half * local_probes, :1] >= 0, axis=1).astype(jnp.int32)
        spread = extend_add(load, counts, spread, half, local_probes)
    spread = spread.reshape(high_count, local_probes, width)
    sample = jnp.moveaxis(spread, 0, 1).reshape(local_probes, front_rows)

    share_rows = front_rows // probe_count
    sketch_all = gather_rows(sketch, "probe")
    share_sample = exchange_shares(sample.reshape(local_probes, probe_count, share_rows), "probe")
    share_sketched = jnp.einsum("pr,ps->rs", share_sample, sketch_all, precision=highest)
    gram_one = ordered_sum(
        jnp.einsum("ra,rb->ab", share_sketched, share_sketched, precision=highest), "probe"
    )
    own_basis = basis_from_gram(share_sketched, gram_one, rank_one[0])
    passed_one = ordered_sum(jnp.dot(share_sample, own_basis, precision=highest), "probe")

    pair_bit = leaf_index % 2
    merged_two, passed_two = merge_level(
        passed_one, partner_2(passed_one, "leaf", 0), pair_bit == 0, sketch_all, rank_two[leaf_index // 2]
    )
    quad_bit = leaf_index // 2 % 2
    merged_three, passed_three = merge_level(
        passed_two, partner_2(passed_two, "leaf", 1), quad_bit == 0, sketch_all, rank_three[leaf_index // 4]
    )
    basis_two = lax.dynamic_slice_in_dim(merged_two, pair_bit * rank_width, rank_width, 0)
    basis_three = lax.dynamic_slice_in_dim(merged_three, quad_bit * rank_width, rank_width, 0)
    top = lax.dynamic_slice_in_dim(passed_three, probe_index * local_probes, local_probes, 0)
    return (own_basis, basis_two, basis_three, top)


def solution(mesh):
    return jax.shard_map(
        on_device,
        mesh=mesh,
        in_specs=(
            P("leaf", None, None),
            P("probe", "leaf"),
            P("leaf", None),
            P("leaf", None),
            P("leaf", None, None),
            P("leaf", None),
            P("probe", "leaf"),
            P("probe", None),
            P("leaf"),
            P(),
            P(),
        ),
        out_specs=(
            P(("leaf", "probe"), None),
            P("leaf", None),
            P("leaf", None),
            P("probe", "leaf"),
        ),
        check_vma=False,
    )
```

```python
import functools

import jax
import jax.numpy as jnp
from jax import lax
from jax.experimental import pallas as pl
from jax.experimental.pallas import tpu as pltpu
from jax.sharding import PartitionSpec as P

highest = lax.Precision.HIGHEST

SLOT_CAP = 8


def partner_2(block, axis, stride):
    count = lax.axis_size(axis)
    route = []
    for low in range(count):
        high = low | 1 << stride
        if high != low and high < count:
            route += [(low, high), (high, low)]
    return lax.ppermute(block, axis, route)


def butterfly_sum(block, axis):
    count = lax.axis_size(axis)
    stride = 0
    while 1 << stride < count:
        block = block + partner_2(block, axis, stride)
        stride += 1
    return block


def ordered_sum(block, axis):
    count = lax.axis_size(axis)
    gathered = gather_rows(block[None], axis)
    total = gathered[0]
    for member in range(1, count):
        total = total + gathered[member]
    return total


def gather_rows(block, axis):
    count = lax.axis_size(axis)
    index = lax.axis_index(axis)
    pieces = [block]
    for shift in range(1, count):
        route = [(j, (j + shift) % count) for j in range(count)]
        pieces.append(lax.ppermute(block, axis, route))
    stacked = jnp.stack(pieces)
    order = (index - jnp.arange(count, dtype=jnp.int32)) % count
    stacked = jnp.take(stacked, order, axis=0)
    return stacked.reshape((count * block.shape[0],) + block.shape[1:])


def extend_add_kernel(count_ref, load_ref, start_ref, out_ref, *, slots, probes):
    source = pl.program_id(0)
    lanes = load_ref.shape[2]
    width = out_ref.shape[1]
    high_count = out_ref.shape[0] // probes
    info = slots * probes

    @pl.when(source == 0)
    def _():
        out_ref[...] = start_ref[...]

    @pl.when(count_ref[source] > 0)
    def _():
        spread, hot = [], []
        for slot in range(slots):
            high = load_ref[0, pl.ds(info + slot, 1), :].astype(jnp.float32).astype(jnp.int32)
            low = load_ref[0, pl.ds(info + slots + slot, 1), :].astype(jnp.float32).astype(jnp.int32)
            target = high * lanes + low
            block = jnp.where(target >= 0, target // width, -1)
            offset = target % width
            vals = load_ref[0, pl.ds(slot * probes, probes), :]
            zero = jnp.zeros_like(vals)
            spread.append(
                jnp.concatenate([jnp.where(block == h, vals, zero) for h in range(high_count)], axis=0)
            )
            hot.append(
                (lax.broadcasted_iota(jnp.int32, (width, lanes), 0) == offset).astype(jnp.bfloat16)
            )
        spread = jnp.concatenate(spread, axis=1)
        hot = jnp.concatenate(hot, axis=1)
        out_ref[...] += lax.dot_general(
            spread, hot, (((1,), (1,)), ((), ())), preferred_element_type=jnp.float32
        )


def extend_add(load, counts, start, slots, probes):
    sources, depth, lanes = load.shape
    kernel = functools.partial(extend_add_kernel, slots=slots, probes=probes)
    return pl.pallas_call(
        kernel,
        grid_spec=pltpu.PrefetchScalarGridSpec(
            num_scalar_prefetch=1,
            grid=(sources,),
            in_specs=[
                pl.BlockSpec((1, depth, lanes), lambda s, c: (s, 0, 0)),
                pl.BlockSpec(start.shape, lambda s, c: (0, 0)),
            ],
            out_specs=pl.BlockSpec(start.shape, lambda s, c: (0, 0)),
        ),
        out_shape=jax.ShapeDtypeStruct(start.shape, jnp.float32),
        compiler_params=pltpu.CompilerParams(dimension_semantics=("arbitrary",)),
    )(counts, load, start)


def exchange_shares(block, axis):
    count = lax.axis_size(axis)
    index = lax.axis_index(axis)
    got = [jnp.take(block, index, axis=1)]
    for shift in range(1, count):
        route = [(j, (j + shift) % count) for j in range(count)]
        outgoing = jnp.take(block, (index + shift) % count, axis=1)
        got.append(lax.ppermute(outgoing, axis, route))
    stacked = jnp.stack(got)
    order = (index - jnp.arange(count, dtype=jnp.int32)) % count
    stacked = jnp.take(stacked, order, axis=0)
    return stacked.reshape((count * block.shape[0],) + block.shape[2:])


def cholesky_inverse_kernel(gram_ref, inverse_ref, work_ref, rest_ref):
    order = gram_ref.shape[0]
    tile = 8
    sub = lax.broadcasted_iota(jnp.int32, (order, order), 0)
    lane = lax.broadcasted_iota(jnp.int32, (order, order), 1)
    lane_one = lax.broadcasted_iota(jnp.int32, (1, order), 1)
    work_ref[...] = gram_ref[...]
    rest_ref[...] = jnp.where(sub == lane, 1.0, 0.0).astype(jnp.float32)
    inverse_ref[...] = jnp.zeros_like(inverse_ref)

    for first in range(0, order, tile):
        height = order - first
        tail_lane = lax.broadcasted_iota(jnp.int32, (height, order), 1)
        tail_sub = lax.broadcasted_iota(jnp.int32, (height, 1), 0) + first

        def step(j, carry, first=first, tail_lane=tail_lane, tail_sub=tail_sub):
            work = work_ref[first:, :]
            pivot_row = work_ref[pl.ds(j, 1), :]
            pivot = jnp.sum(jnp.where(lane_one == j, pivot_row, 0.0), axis=1, keepdims=True)
            column = jnp.sum(jnp.where(tail_lane == j, work, 0.0), axis=1, keepdims=True)
            scale = lax.rsqrt(pivot)
            column = jnp.where(tail_sub >= j, column * scale, 0.0)
            row = jnp.where(lane_one >= j, pivot_row * scale, 0.0)
            work_ref[first:, :] = work - column * row
            solved = rest_ref[pl.ds(j, 1), :] * scale
            inverse_ref[pl.ds(j, 1), :] = solved
            rest_ref[first:, :] = rest_ref[first:, :] - column * solved
            return carry

        lax.fori_loop(first, first + tile, step, 0, unroll=True)


def cholesky_inverse(gram_matrix):
    order = gram_matrix.shape[0]
    symmetric = (gram_matrix + gram_matrix.T) * 0.5
    return pl.pallas_call(
        cholesky_inverse_kernel,
        out_shape=jax.ShapeDtypeStruct((order, order), jnp.float32),
        scratch_shapes=[pltpu.VMEM((order, order), jnp.float32)] * 2,
    )(symmetric)


def basis_from_gram(sketched, gram_matrix, rank_limit):
    inverse = cholesky_inverse(gram_matrix)
    orthonormal = jnp.einsum("ra,ba->rb", sketched, inverse, precision=highest)
    columns = jnp.arange(sketched.shape[1], dtype=jnp.int32)
    return jnp.where(columns[None, :] < rank_limit, orthonormal, jnp.zeros_like(orthonormal))


def chol_basis(sketched, rank_limit):
    gram_matrix = jnp.einsum("ra,rb->ab", sketched, sketched, precision=highest)
    return basis_from_gram(sketched, gram_matrix, rank_limit)


def merge_level(own, partner, low_side, sketch_all, rank_limit):
    stacked = jnp.where(
        low_side,
        jnp.concatenate([own, partner], 1),
        jnp.concatenate([partner, own], 1),
    )
    sketched = jnp.einsum("pr,ps->rs", stacked, sketch_all, precision=highest)
    merged = chol_basis(sketched, rank_limit)
    return merged, jnp.dot(stacked, merged, precision=highest)


def on_device(
    child_updates,
    child_probes,
    child_dest,
    child_rows,
    parent_blocks,
    coupling,
    parent_probes,
    sketch,
    rank_one,
    rank_two,
    rank_three,
):
    leaf_count = lax.axis_size("leaf")
    probe_count = lax.axis_size("probe")
    leaf_index = lax.axis_index("leaf")
    probe_index = lax.axis_index("probe")
    local_probes = child_probes.shape[0]
    kid_count = child_updates.shape[0]
    kid_order = child_updates.shape[1]
    block_rows = child_rows.shape[1]
    block_count = child_rows.shape[0]
    front_rows = parent_probes.shape[1]
    rank_width = sketch.shape[1]

    updates = child_updates.reshape(kid_count, kid_order // block_rows, block_rows, kid_order)
    probe_cut = child_probes.reshape(local_probes, kid_count, kid_order)
    sampled = jnp.einsum("pck,cbik->cbpi", probe_cut, updates, preferred_element_type=jnp.float32)
    sampled = sampled.astype(jnp.bfloat16).reshape(block_count, local_probes, block_rows)

    targets = child_dest[:, 0]
    named = (targets[:, None] == jnp.arange(leaf_count, dtype=jnp.int32)[None, :]).astype(jnp.int32)
    earlier = jnp.cumsum(named, axis=0) - named
    slot = jnp.sum(earlier * named, axis=1)
    place = targets * SLOT_CAP + slot
    slot_count = leaf_count * SLOT_CAP
    source = jnp.full((slot_count,), block_count, jnp.int32).at[place].set(
        jnp.arange(block_count, dtype=jnp.int32)
    )
    filled = source < block_count
    source = jnp.minimum(source, block_count - 1)
    high = jnp.where(filled[:, None], child_rows[source] // block_rows, -1)
    low = jnp.where(filled[:, None], child_rows[source] % block_rows, 0)
    send_vals = jnp.take(sampled, source, axis=0)
    half = SLOT_CAP
    info_rows = 16
    loads = []
    for part in range(1):
        picked_slots = slice(part * half, (part + 1) * half)
        vals = send_vals.reshape(leaf_count, SLOT_CAP, local_probes, block_rows)[:, picked_slots]
        info = jnp.concatenate(
            [
                high.reshape(leaf_count, SLOT_CAP, block_rows)[:, picked_slots],
                low.reshape(leaf_count, SLOT_CAP, block_rows)[:, picked_slots],
                jnp.zeros((leaf_count, info_rows - 2 * half, block_rows), jnp.int32),
            ],
            axis=1,
        ).astype(jnp.bfloat16)
        load = jnp.concatenate(
            [vals.reshape(leaf_count, half * local_probes, block_rows), info], axis=1
        )
        loads.append(lax.all_to_all(load, "leaf", 0, 0, tiled=True))

    pieces = parent_probes.reshape(local_probes, front_rows // block_rows, block_rows)
    picked = jnp.take(pieces, coupling[:, 1], axis=1)
    product = jnp.einsum("eik,pek->pei", parent_blocks, picked, preferred_element_type=jnp.float32)
    initial = (
        jnp.zeros(pieces.shape, jnp.float32)
        .at[:, coupling[:, 0]]
        .add(product)
        .reshape(local_probes, front_rows)
    )
    width = 4 * block_rows
    high_count = front_rows // width
    spread = jnp.moveaxis(initial.reshape(local_probes, high_count, width), 1, 0)
    spread = spread.reshape(high_count * local_probes, width)
    for load in loads:
        counts = jnp.sum(load[:, half * local_probes, :1] >= 0, axis=1).astype(jnp.int32)
        spread = extend_add(load, counts, spread, half, local_probes)
    spread = spread.reshape(high_count, local_probes, width)
    sample = jnp.moveaxis(spread, 0, 1).reshape(local_probes, front_rows)

    share_rows = front_rows // probe_count
    sketch_all = gather_rows(sketch, "probe")
    share_sample = exchange_shares(sample.reshape(local_probes, probe_count, share_rows), "probe")
    share_sketched = jnp.einsum("pr,ps->rs", share_sample, sketch_all, precision=highest)
    gram_one = ordered_sum(
        jnp.einsum("ra,rb->ab", share_sketched, share_sketched, precision=highest), "probe"
    )
    own_basis = basis_from_gram(share_sketched, gram_one, rank_one[0])
    passed_one = ordered_sum(jnp.dot(share_sample, own_basis, precision=highest), "probe")

    pair_bit = leaf_index % 2
    merged_two, passed_two = merge_level(
        passed_one, partner_2(passed_one, "leaf", 0), pair_bit == 0, sketch_all, rank_two[leaf_index // 2]
    )
    quad_bit = leaf_index // 2 % 2
    merged_three, passed_three = merge_level(
        passed_two, partner_2(passed_two, "leaf", 1), quad_bit == 0, sketch_all, rank_three[leaf_index // 4]
    )
    basis_two = lax.dynamic_slice_in_dim(merged_two, pair_bit * rank_width, rank_width, 0)
    basis_three = lax.dynamic_slice_in_dim(merged_three, quad_bit * rank_width, rank_width, 0)
    top = lax.dynamic_slice_in_dim(passed_three, probe_index * local_probes, local_probes, 0)
    return (own_basis, basis_two, basis_three, top)


def solution(mesh):
    return jax.shard_map(
        on_device,
        mesh=mesh,
        in_specs=(
            P("leaf", None, None),
            P("probe", "leaf"),
            P("leaf", None),
            P("leaf", None),
            P("leaf", None, None),
            P("leaf", None),
            P("probe", "leaf"),
            P("probe", None),
            P("leaf"),
            P(),
            P(),
        ),
        out_specs=(
            P(("leaf", "probe"), None),
            P("leaf", None),
            P("leaf", None),
            P("probe", "leaf"),
        ),
        check_vma=False,
    )
```

```python
import functools

import jax
import jax.numpy as jnp
from jax import lax
from jax.experimental import pallas as pl
from jax.experimental.pallas import tpu as pltpu
from jax.sharding import PartitionSpec as P

highest = lax.Precision.HIGHEST

SLOT_CAP = 8


def partner_2(block, axis, stride):
    count = lax.axis_size(axis)
    route = []
    for low in range(count):
        high = low | 1 << stride
        if high != low and high < count:
            route += [(low, high), (high, low)]
    return lax.ppermute(block, axis, route)


def butterfly_sum(block, axis):
    count = lax.axis_size(axis)
    stride = 0
    while 1 << stride < count:
        block = block + partner_2(block, axis, stride)
        stride += 1
    return block


def ordered_sum(block, axis):
    count = lax.axis_size(axis)
    gathered = gather_rows(block[None], axis)
    total = gathered[0]
    for member in range(1, count):
        total = total + gathered[member]
    return total


def gather_rows(block, axis):
    count = lax.axis_size(axis)
    index = lax.axis_index(axis)
    pieces = [block]
    for shift in range(1, count):
        route = [(j, (j + shift) % count) for j in range(count)]
        pieces.append(lax.ppermute(block, axis, route))
    stacked = jnp.stack(pieces)
    order = (index - jnp.arange(count, dtype=jnp.int32)) % count
    stacked = jnp.take(stacked, order, axis=0)
    return stacked.reshape((count * block.shape[0],) + block.shape[1:])


def extend_add_kernel(count_ref, load_ref, start_ref, out_ref, *, slots, probes):
    source = pl.program_id(0)
    lanes = load_ref.shape[2]
    width = out_ref.shape[1]
    high_count = out_ref.shape[0] // probes
    info = slots * probes

    @pl.when(source == 0)
    def _():
        out_ref[...] = start_ref[...]

    @pl.when(count_ref[source] > 0)
    def _():
        spread, hot = [], []
        for slot in range(slots):
            high = load_ref[0, pl.ds(info + slot, 1), :].astype(jnp.float32).astype(jnp.int32)
            low = load_ref[0, pl.ds(info + slots + slot, 1), :].astype(jnp.float32).astype(jnp.int32)
            target = high * lanes + low
            block = jnp.where(target >= 0, target // width, -1)
            offset = target % width
            vals = load_ref[0, pl.ds(slot * probes, probes), :]
            zero = jnp.zeros_like(vals)
            spread.append(
                jnp.concatenate([jnp.where(block == h, vals, zero) for h in range(high_count)], axis=0)
            )
            hot.append(
                (lax.broadcasted_iota(jnp.int32, (width, lanes), 0) == offset).astype(jnp.bfloat16)
            )
        spread = jnp.concatenate(spread, axis=1)
        hot = jnp.concatenate(hot, axis=1)
        out_ref[...] += lax.dot_general(
            spread, hot, (((1,), (1,)), ((), ())), preferred_element_type=jnp.float32
        )


def extend_add(load, counts, start, slots, probes):
    sources, depth, lanes = load.shape
    kernel = functools.partial(extend_add_kernel, slots=slots, probes=probes)
    return pl.pallas_call(
        kernel,
        grid_spec=pltpu.PrefetchScalarGridSpec(
            num_scalar_prefetch=1,
            grid=(sources,),
            in_specs=[
                pl.BlockSpec((1, depth, lanes), lambda s, c: (s, 0, 0)),
                pl.BlockSpec(start.shape, lambda s, c: (0, 0)),
            ],
            out_specs=pl.BlockSpec(start.shape, lambda s, c: (0, 0)),
        ),
        out_shape=jax.ShapeDtypeStruct(start.shape, jnp.float32),
        compiler_params=pltpu.CompilerParams(dimension_semantics=("arbitrary",)),
    )(counts, load, start)


def pack_kernel(source_ref, sampled_ref, info_ref, out_ref, *, slots, probes):
    dest = pl.program_id(0)
    for slot in range(slots):
        block = source_ref[dest * slots + slot]
        out_ref[0, slot * probes:(slot + 1) * probes, :] = sampled_ref[block]
    out_ref[0, slots * probes:, :] = info_ref[0]


def pack_payload(source, sampled, info, slots):
    blocks, probes, lanes = sampled.shape
    dests = info.shape[0]
    depth = slots * probes + info.shape[1]
    kernel = functools.partial(pack_kernel, slots=slots, probes=probes)
    return pl.pallas_call(
        kernel,
        grid_spec=pltpu.PrefetchScalarGridSpec(
            num_scalar_prefetch=1,
            grid=(dests,),
            in_specs=[
                pl.BlockSpec(sampled.shape, lambda d, s: (0, 0, 0)),
                pl.BlockSpec((1,) + info.shape[1:], lambda d, s: (d, 0, 0)),
            ],
            out_specs=pl.BlockSpec((1, depth, lanes), lambda d, s: (d, 0, 0)),
        ),
        out_shape=jax.ShapeDtypeStruct((dests, depth, lanes), sampled.dtype),
        compiler_params=pltpu.CompilerParams(dimension_semantics=("arbitrary",)),
    )(source, sampled, info)


def exchange_shares(block, axis):
    count = lax.axis_size(axis)
    index = lax.axis_index(axis)
    got = [jnp.take(block, index, axis=1)]
    for shift in range(1, count):
        route = [(j, (j + shift) % count) for j in range(count)]
        outgoing = jnp.take(block, (index + shift) % count, axis=1)
        got.append(lax.ppermute(outgoing, axis, route))
    stacked = jnp.stack(got)
    order = (index - jnp.arange(count, dtype=jnp.int32)) % count
    stacked = jnp.take(stacked, order, axis=0)
    return stacked.reshape((count * block.shape[0],) + block.shape[2:])


def cholesky_inverse_kernel(gram_ref, inverse_ref, work_ref, rest_ref):
    order = gram_ref.shape[0]
    tile = 8
    sub = lax.broadcasted_iota(jnp.int32, (order, order), 0)
    lane = lax.broadcasted_iota(jnp.int32, (order, order), 1)
    lane_one = lax.broadcasted_iota(jnp.int32, (1, order), 1)
    work_ref[...] = gram_ref[...]
    rest_ref[...] = jnp.where(sub == lane, 1.0, 0.0).astype(jnp.float32)
    inverse_ref[...] = jnp.zeros_like(inverse_ref)

    for first in range(0, order, tile):
        height = order - first
        tail_lane = lax.broadcasted_iota(jnp.int32, (height, order), 1)
        tail_sub = lax.broadcasted_iota(jnp.int32, (height, 1), 0) + first

        def step(j, carry, first=first, tail_lane=tail_lane, tail_sub=tail_sub):
            work = work_ref[first:, :]
            pivot_row = work_ref[pl.ds(j, 1), :]
            pivot = jnp.sum(jnp.where(lane_one == j, pivot_row, 0.0), axis=1, keepdims=True)
            column = jnp.sum(jnp.where(tail_lane == j, work, 0.0), axis=1, keepdims=True)
            scale = lax.rsqrt(pivot)
            column = jnp.where(tail_sub >= j, column * scale, 0.0)
            row = jnp.where(lane_one >= j, pivot_row * scale, 0.0)
            work_ref[first:, :] = work - column * row
            solved = rest_ref[pl.ds(j, 1), :] * scale
            inverse_ref[pl.ds(j, 1), :] = solved
            rest_ref[first:, :] = rest_ref[first:, :] - column * solved
            return carry

        lax.fori_loop(first, first + tile, step, 0, unroll=True)


def cholesky_inverse(gram_matrix):
    order = gram_matrix.shape[0]
    symmetric = (gram_matrix + gram_matrix.T) * 0.5
    return pl.pallas_call(
        cholesky_inverse_kernel,
        out_shape=jax.ShapeDtypeStruct((order, order), jnp.float32),
        scratch_shapes=[pltpu.VMEM((order, order), jnp.float32)] * 2,
    )(symmetric)


def basis_from_gram(sketched, gram_matrix, rank_limit):
    inverse = cholesky_inverse(gram_matrix)
    orthonormal = jnp.einsum("ra,ba->rb", sketched, inverse, precision=highest)
    columns = jnp.arange(sketched.shape[1], dtype=jnp.int32)
    return jnp.where(columns[None, :] < rank_limit, orthonormal, jnp.zeros_like(orthonormal))


def chol_basis(sketched, rank_limit):
    gram_matrix = jnp.einsum("ra,rb->ab", sketched, sketched, precision=highest)
    return basis_from_gram(sketched, gram_matrix, rank_limit)


def merge_level(own, partner, low_side, sketch_all, rank_limit):
    stacked = jnp.where(
        low_side,
        jnp.concatenate([own, partner], 1),
        jnp.concatenate([partner, own], 1),
    )
    sketched = jnp.einsum("pr,ps->rs", stacked, sketch_all, precision=highest)
    merged = chol_basis(sketched, rank_limit)
    return merged, jnp.dot(stacked, merged, precision=highest)


def on_device(
    child_updates,
    child_probes,
    child_dest,
    child_rows,
    parent_blocks,
    coupling,
    parent_probes,
    sketch,
    rank_one,
    rank_two,
    rank_three,
):
    leaf_count = lax.axis_size("leaf")
    probe_count = lax.axis_size("probe")
    leaf_index = lax.axis_index("leaf")
    probe_index = lax.axis_index("probe")
    local_probes = child_probes.shape[0]
    kid_count = child_updates.shape[0]
    kid_order = child_updates.shape[1]
    block_rows = child_rows.shape[1]
    block_count = child_rows.shape[0]
    front_rows = parent_probes.shape[1]
    rank_width = sketch.shape[1]

    updates = child_updates.reshape(kid_count, kid_order // block_rows, block_rows, kid_order)
    probe_cut = child_probes.reshape(local_probes, kid_count, kid_order)
    sampled = jnp.einsum("pck,cbik->cbpi", probe_cut, updates, preferred_element_type=jnp.float32)
    sampled = sampled.astype(jnp.bfloat16).reshape(block_count, local_probes, block_rows)

    targets = child_dest[:, 0]
    named = (targets[:, None] == jnp.arange(leaf_count, dtype=jnp.int32)[None, :]).astype(jnp.int32)
    earlier = jnp.cumsum(named, axis=0) - named
    slot = jnp.sum(earlier * named, axis=1)
    place = targets * SLOT_CAP + slot
    slot_count = leaf_count * SLOT_CAP
    source = jnp.full((slot_count,), block_count, jnp.int32).at[place].set(
        jnp.arange(block_count, dtype=jnp.int32)
    )
    filled = source < block_count
    source = jnp.minimum(source, block_count - 1)
    high = jnp.where(filled[:, None], child_rows[source] // block_rows, -1)
    low = jnp.where(filled[:, None], child_rows[source] % block_rows, 0)
    half = SLOT_CAP
    info_rows = 16
    loads = []
    for part in range(1):
        picked_slots = slice(part * half, (part + 1) * half)
        info = jnp.concatenate(
            [
                high.reshape(leaf_count, SLOT_CAP, block_rows)[:, picked_slots],
                low.reshape(leaf_count, SLOT_CAP, block_rows)[:, picked_slots],
                jnp.zeros((leaf_count, info_rows - 2 * half, block_rows), jnp.int32),
            ],
            axis=1,
        ).astype(jnp.bfloat16)
        load = pack_payload(source, sampled, info, half)
        loads.append(lax.all_to_all(load, "leaf", 0, 0, tiled=True))

    pieces = parent_probes.reshape(local_probes, front_rows // block_rows, block_rows)
    picked = jnp.take(pieces, coupling[:, 1], axis=1)
    product = jnp.einsum("eik,pek->pei", parent_blocks, picked, preferred_element_type=jnp.float32)
    initial = (
        jnp.zeros(pieces.shape, jnp.float32)
        .at[:, coupling[:, 0]]
        .add(product)
        .reshape(local_probes, front_rows)
    )
    width = 4 * block_rows
    high_count = front_rows // width
    spread = jnp.moveaxis(initial.reshape(local_probes, high_count, width), 1, 0)
    spread = spread.reshape(high_count * local_probes, width)
    for load in loads:
        counts = jnp.sum(load[:, half * local_probes, :1] >= 0, axis=1).astype(jnp.int32)
        spread = extend_add(load, counts, spread, half, local_probes)
    spread = spread.reshape(high_count, local_probes, width)
    sample = jnp.moveaxis(spread, 0, 1).reshape(local_probes, front_rows)

    share_rows = front_rows // probe_count
    sketch_all = gather_rows(sketch, "probe")
    share_sample = exchange_shares(sample.reshape(local_probes, probe_count, share_rows), "probe")
    share_sketched = jnp.einsum("pr,ps->rs", share_sample, sketch_all, precision=highest)
    gram_one = ordered_sum(
        jnp.einsum("ra,rb->ab", share_sketched, share_sketched, precision=highest), "probe"
    )
    own_basis = basis_from_gram(share_sketched, gram_one, rank_one[0])
    passed_one = ordered_sum(jnp.dot(share_sample, own_basis, precision=highest), "probe")

    pair_bit = leaf_index % 2
    merged_two, passed_two = merge_level(
        passed_one, partner_2(passed_one, "leaf", 0), pair_bit == 0, sketch_all, rank_two[leaf_index // 2]
    )
    quad_bit = leaf_index // 2 % 2
    merged_three, passed_three = merge_level(
        passed_two, partner_2(passed_two, "leaf", 1), quad_bit == 0, sketch_all, rank_three[leaf_index // 4]
    )
    basis_two = lax.dynamic_slice_in_dim(merged_two, pair_bit * rank_width, rank_width, 0)
    basis_three = lax.dynamic_slice_in_dim(merged_three, quad_bit * rank_width, rank_width, 0)
    top = lax.dynamic_slice_in_dim(passed_three, probe_index * local_probes, local_probes, 0)
    return (own_basis, basis_two, basis_three, top)


def solution(mesh):
    return jax.shard_map(
        on_device,
        mesh=mesh,
        in_specs=(
            P("leaf", None, None),
            P("probe", "leaf"),
            P("leaf", None),
            P("leaf", None),
            P("leaf", None, None),
            P("leaf", None),
            P("probe", "leaf"),
            P("probe", None),
            P("leaf"),
            P(),
            P(),
        ),
        out_specs=(
            P(("leaf", "probe"), None),
            P("leaf", None),
            P("leaf", None),
            P("probe", "leaf"),
        ),
        check_vma=False,
    )
```

```python
import functools

import jax
import jax.numpy as jnp
from jax import lax
from jax.experimental import pallas as pl
from jax.experimental.pallas import tpu as pltpu
from jax.sharding import PartitionSpec as P

highest = lax.Precision.HIGHEST

SLOT_CAP = 8


def partner_2(block, axis, stride):
    count = lax.axis_size(axis)
    route = []
    for low in range(count):
        high = low | 1 << stride
        if high != low and high < count:
            route += [(low, high), (high, low)]
    return lax.ppermute(block, axis, route)


def butterfly_sum(block, axis):
    count = lax.axis_size(axis)
    stride = 0
    while 1 << stride < count:
        block = block + partner_2(block, axis, stride)
        stride += 1
    return block


def ordered_sum(block, axis):
    count = lax.axis_size(axis)
    gathered = gather_rows(block[None], axis)
    total = gathered[0]
    for member in range(1, count):
        total = total + gathered[member]
    return total


def gather_rows(block, axis):
    count = lax.axis_size(axis)
    index = lax.axis_index(axis)
    pieces = [block]
    for shift in range(1, count):
        route = [(j, (j + shift) % count) for j in range(count)]
        pieces.append(lax.ppermute(block, axis, route))
    stacked = jnp.stack(pieces)
    order = (index - jnp.arange(count, dtype=jnp.int32)) % count
    stacked = jnp.take(stacked, order, axis=0)
    return stacked.reshape((count * block.shape[0],) + block.shape[1:])


def extend_add_kernel(load_ref, start_ref, out_ref, *, slots, probes):
    source = pl.program_id(0)
    lanes = load_ref.shape[2]
    width = out_ref.shape[1]
    high_count = out_ref.shape[0] // probes
    info = slots * probes

    @pl.when(source == 0)
    def _():
        out_ref[...] = start_ref[...]

    def accumulate():
        spread, hot = [], []
        for slot in range(slots):
            high = load_ref[0, pl.ds(info + slot, 1), :].astype(jnp.float32).astype(jnp.int32)
            low = load_ref[0, pl.ds(info + slots + slot, 1), :].astype(jnp.float32).astype(jnp.int32)
            target = high * lanes + low
            block = jnp.where(target >= 0, target // width, -1)
            offset = target % width
            vals = load_ref[0, pl.ds(slot * probes, probes), :]
            zero = jnp.zeros_like(vals)
            spread.append(
                jnp.concatenate([jnp.where(block == h, vals, zero) for h in range(high_count)], axis=0)
            )
            hot.append(
                (lax.broadcasted_iota(jnp.int32, (width, lanes), 0) == offset).astype(jnp.bfloat16)
            )
        spread = jnp.concatenate(spread, axis=1)
        hot = jnp.concatenate(hot, axis=1)
        out_ref[...] += lax.dot_general(
            spread, hot, (((1,), (1,)), ((), ())), preferred_element_type=jnp.float32
        )

    accumulate()


def extend_add(load, start, slots, probes):
    sources, depth, lanes = load.shape
    kernel = functools.partial(extend_add_kernel, slots=slots, probes=probes)
    return pl.pallas_call(
        kernel,
        grid=(sources,),
        in_specs=[
            pl.BlockSpec((1, depth, lanes), lambda s: (s, 0, 0)),
            pl.BlockSpec(start.shape, lambda s: (0, 0)),
        ],
        out_specs=pl.BlockSpec(start.shape, lambda s: (0, 0)),
        out_shape=jax.ShapeDtypeStruct(start.shape, jnp.float32),
        compiler_params=pltpu.CompilerParams(dimension_semantics=("arbitrary",)),
    )(load, start)


def exchange_shares(block, axis):
    count = lax.axis_size(axis)
    index = lax.axis_index(axis)
    got = [jnp.take(block, index, axis=1)]
    for shift in range(1, count):
        route = [(j, (j + shift) % count) for j in range(count)]
        outgoing = jnp.take(block, (index + shift) % count, axis=1)
        got.append(lax.ppermute(outgoing, axis, route))
    stacked = jnp.stack(got)
    order = (index - jnp.arange(count, dtype=jnp.int32)) % count
    stacked = jnp.take(stacked, order, axis=0)
    return stacked.reshape((count * block.shape[0],) + block.shape[2:])


def cholesky_inverse_kernel(gram_ref, inverse_ref, work_ref, rest_ref):
    order = gram_ref.shape[0]
    tile = 8
    sub = lax.broadcasted_iota(jnp.int32, (order, order), 0)
    lane = lax.broadcasted_iota(jnp.int32, (order, order), 1)
    lane_one = lax.broadcasted_iota(jnp.int32, (1, order), 1)
    work_ref[...] = gram_ref[...]
    rest_ref[...] = jnp.where(sub == lane, 1.0, 0.0).astype(jnp.float32)
    inverse_ref[...] = jnp.zeros_like(inverse_ref)

    for first in range(0, order, tile):
        height = order - first
        tail_lane = lax.broadcasted_iota(jnp.int32, (height, order), 1)
        tail_sub = lax.broadcasted_iota(jnp.int32, (height, 1), 0) + first

        def step(j, carry, first=first, tail_lane=tail_lane, tail_sub=tail_sub):
            work = work_ref[first:, :]
            pivot_row = work_ref[pl.ds(j, 1), :]
            pivot = jnp.sum(jnp.where(lane_one == j, pivot_row, 0.0), axis=1, keepdims=True)
            column = jnp.sum(jnp.where(tail_lane == j, work, 0.0), axis=1, keepdims=True)
            scale = lax.rsqrt(pivot)
            column = jnp.where(tail_sub >= j, column * scale, 0.0)
            row = jnp.where(lane_one >= j, pivot_row * scale, 0.0)
            work_ref[first:, :] = work - column * row
            solved = rest_ref[pl.ds(j, 1), :] * scale
            inverse_ref[pl.ds(j, 1), :] = solved
            rest_ref[first:, :] = rest_ref[first:, :] - column * solved
            return carry

        lax.fori_loop(first, first + tile, step, 0, unroll=True)


def cholesky_inverse(gram_matrix):
    order = gram_matrix.shape[0]
    symmetric = (gram_matrix + gram_matrix.T) * 0.5
    return pl.pallas_call(
        cholesky_inverse_kernel,
        out_shape=jax.ShapeDtypeStruct((order, order), jnp.float32),
        scratch_shapes=[pltpu.VMEM((order, order), jnp.float32)] * 2,
    )(symmetric)


def basis_from_gram(sketched, gram_matrix, rank_limit):
    inverse = cholesky_inverse(gram_matrix)
    orthonormal = jnp.einsum("ra,ba->rb", sketched, inverse, precision=highest)
    columns = jnp.arange(sketched.shape[1], dtype=jnp.int32)
    return jnp.where(columns[None, :] < rank_limit, orthonormal, jnp.zeros_like(orthonormal))


def chol_basis(sketched, rank_limit):
    gram_matrix = jnp.einsum("ra,rb->ab", sketched, sketched, precision=highest)
    return basis_from_gram(sketched, gram_matrix, rank_limit)


def merge_level(own, partner, low_side, sketch_all, rank_limit):
    stacked = jnp.where(
        low_side,
        jnp.concatenate([own, partner], 1),
        jnp.concatenate([partner, own], 1),
    )
    sketched = jnp.einsum("pr,ps->rs", stacked, sketch_all, precision=highest)
    merged = chol_basis(sketched, rank_limit)
    return merged, jnp.dot(stacked, merged, precision=highest)


def on_device(
    child_updates,
    child_probes,
    child_dest,
    child_rows,
    parent_blocks,
    coupling,
    parent_probes,
    sketch,
    rank_one,
    rank_two,
    rank_three,
):
    leaf_count = lax.axis_size("leaf")
    probe_count = lax.axis_size("probe")
    leaf_index = lax.axis_index("leaf")
    probe_index = lax.axis_index("probe")
    local_probes = child_probes.shape[0]
    kid_count = child_updates.shape[0]
    kid_order = child_updates.shape[1]
    block_rows = child_rows.shape[1]
    block_count = child_rows.shape[0]
    front_rows = parent_probes.shape[1]
    rank_width = sketch.shape[1]

    updates = child_updates.reshape(kid_count, kid_order // block_rows, block_rows, kid_order)
    probe_cut = child_probes.reshape(local_probes, kid_count, kid_order)
    sampled = jnp.einsum("pck,cbik->cbpi", probe_cut, updates, preferred_element_type=jnp.float32)
    sampled = sampled.astype(jnp.bfloat16).reshape(block_count, local_probes, block_rows)

    targets = child_dest[:, 0]
    named = (targets[:, None] == jnp.arange(leaf_count, dtype=jnp.int32)[None, :]).astype(jnp.int32)
    earlier = jnp.cumsum(named, axis=0) - named
    slot = jnp.sum(earlier * named, axis=1)
    place = targets * SLOT_CAP + slot
    slot_count = leaf_count * SLOT_CAP
    source = jnp.full((slot_count,), block_count, jnp.int32).at[place].set(
        jnp.arange(block_count, dtype=jnp.int32)
    )
    filled = source < block_count
    source = jnp.minimum(source, block_count - 1)
    high = jnp.where(filled[:, None], child_rows[source] // block_rows, -1)
    low = jnp.where(filled[:, None], child_rows[source] % block_rows, 0)
    send_vals = jnp.take(sampled, source, axis=0)
    half = SLOT_CAP
    info_rows = 16
    loads = []
    for part in range(1):
        picked_slots = slice(part * half, (part + 1) * half)
        vals = send_vals.reshape(leaf_count, SLOT_CAP, local_probes, block_rows)[:, picked_slots]
        info = jnp.concatenate(
            [
                high.reshape(leaf_count, SLOT_CAP, block_rows)[:, picked_slots],
                low.reshape(leaf_count, SLOT_CAP, block_rows)[:, picked_slots],
                jnp.zeros((leaf_count, info_rows - 2 * half, block_rows), jnp.int32),
            ],
            axis=1,
        ).astype(jnp.bfloat16)
        load = jnp.concatenate(
            [vals.reshape(leaf_count, half * local_probes, block_rows), info], axis=1
        )
        loads.append(lax.all_to_all(load, "leaf", 0, 0, tiled=True))

    pieces = parent_probes.reshape(local_probes, front_rows // block_rows, block_rows)
    picked = jnp.take(pieces, coupling[:, 1], axis=1)
    product = jnp.einsum("eik,pek->pei", parent_blocks, picked, preferred_element_type=jnp.float32)
    initial = (
        jnp.zeros(pieces.shape, jnp.float32)
        .at[:, coupling[:, 0]]
        .add(product)
        .reshape(local_probes, front_rows)
    )
    width = 4 * block_rows
    high_count = front_rows // width
    spread = jnp.moveaxis(initial.reshape(local_probes, high_count, width), 1, 0)
    spread = spread.reshape(high_count * local_probes, width)
    for load in loads:
        spread = extend_add(load, spread, half, local_probes)
    spread = spread.reshape(high_count, local_probes, width)
    sample = jnp.moveaxis(spread, 0, 1).reshape(local_probes, front_rows)

    share_rows = front_rows // probe_count
    sketch_all = gather_rows(sketch, "probe")
    share_sample = exchange_shares(sample.reshape(local_probes, probe_count, share_rows), "probe")
    share_sketched = jnp.einsum("pr,ps->rs", share_sample, sketch_all, precision=highest)
    gram_one = ordered_sum(
        jnp.einsum("ra,rb->ab", share_sketched, share_sketched, precision=highest), "probe"
    )
    own_basis = basis_from_gram(share_sketched, gram_one, rank_one[0])
    passed_one = ordered_sum(jnp.dot(share_sample, own_basis, precision=highest), "probe")

    pair_bit = leaf_index % 2
    merged_two, passed_two = merge_level(
        passed_one, partner_2(passed_one, "leaf", 0), pair_bit == 0, sketch_all, rank_two[leaf_index // 2]
    )
    quad_bit = leaf_index // 2 % 2
    merged_three, passed_three = merge_level(
        passed_two, partner_2(passed_two, "leaf", 1), quad_bit == 0, sketch_all, rank_three[leaf_index // 4]
    )
    basis_two = lax.dynamic_slice_in_dim(merged_two, pair_bit * rank_width, rank_width, 0)
    basis_three = lax.dynamic_slice_in_dim(merged_three, quad_bit * rank_width, rank_width, 0)
    top = lax.dynamic_slice_in_dim(passed_three, probe_index * local_probes, local_probes, 0)
    return (own_basis, basis_two, basis_three, top)


def solution(mesh):
    return jax.shard_map(
        on_device,
        mesh=mesh,
        in_specs=(
            P("leaf", None, None),
            P("probe", "leaf"),
            P("leaf", None),
            P("leaf", None),
            P("leaf", None, None),
            P("leaf", None),
            P("probe", "leaf"),
            P("probe", None),
            P("leaf"),
            P(),
            P(),
        ),
        out_specs=(
            P(("leaf", "probe"), None),
            P("leaf", None),
            P("leaf", None),
            P("probe", "leaf"),
        ),
        check_vma=False,
    )
```

```python
import functools

import jax
import jax.numpy as jnp
from jax import lax
from jax.experimental import pallas as pl
from jax.experimental.pallas import tpu as pltpu
from jax.sharding import PartitionSpec as P

highest = lax.Precision.HIGHEST

SLOT_CAP = 8


def partner_2(block, axis, stride):
    count = lax.axis_size(axis)
    route = []
    for low in range(count):
        high = low | 1 << stride
        if high != low and high < count:
            route += [(low, high), (high, low)]
    return lax.ppermute(block, axis, route)


def butterfly_sum(block, axis):
    count = lax.axis_size(axis)
    stride = 0
    while 1 << stride < count:
        block = block + partner_2(block, axis, stride)
        stride += 1
    return block


def ordered_sum(block, axis):
    count = lax.axis_size(axis)
    gathered = gather_rows(block[None], axis)
    total = gathered[0]
    for member in range(1, count):
        total = total + gathered[member]
    return total


def gather_rows(block, axis):
    count = lax.axis_size(axis)
    index = lax.axis_index(axis)
    pieces = [block]
    for shift in range(1, count):
        route = [(j, (j + shift) % count) for j in range(count)]
        pieces.append(lax.ppermute(block, axis, route))
    stacked = jnp.stack(pieces)
    order = (index - jnp.arange(count, dtype=jnp.int32)) % count
    stacked = jnp.take(stacked, order, axis=0)
    return stacked.reshape((count * block.shape[0],) + block.shape[1:])


def extend_add_kernel(load_ref, start_ref, out_ref, *, slots, probes):
    source = pl.program_id(0)
    lanes = load_ref.shape[2]
    width = out_ref.shape[1]
    high_count = out_ref.shape[0] // probes
    info = slots * probes

    @pl.when(source == 0)
    def _():
        out_ref[...] = start_ref[...]

    def accumulate():
        spread, hot = [], []
        for slot in range(slots):
            high = load_ref[0, pl.ds(info + slot, 1), :].astype(jnp.float32).astype(jnp.int32)
            low = load_ref[0, pl.ds(info + slots + slot, 1), :].astype(jnp.float32).astype(jnp.int32)
            target = high * lanes + low
            block = jnp.where(target >= 0, target // width, -1)
            offset = target % width
            vals = load_ref[0, pl.ds(slot * probes, probes), :]
            zero = jnp.zeros_like(vals)
            spread.append(
                jnp.concatenate([jnp.where(block == h, vals, zero) for h in range(high_count)], axis=0)
            )
            hot.append(
                (lax.broadcasted_iota(jnp.int32, (width, lanes), 0) == offset).astype(jnp.bfloat16)
            )
        spread = jnp.concatenate(spread, axis=1)
        hot = jnp.concatenate(hot, axis=1)
        out_ref[...] += lax.dot_general(
            spread, hot, (((1,), (1,)), ((), ())), preferred_element_type=jnp.float32
        )

    accumulate()


def extend_add(load, start, slots, probes):
    sources, depth, lanes = load.shape
    kernel = functools.partial(extend_add_kernel, slots=slots, probes=probes)
    return pl.pallas_call(
        kernel,
        grid=(sources,),
        in_specs=[
            pl.BlockSpec((1, depth, lanes), lambda s: (s, 0, 0)),
            pl.BlockSpec(start.shape, lambda s: (0, 0)),
        ],
        out_specs=pl.BlockSpec(start.shape, lambda s: (0, 0)),
        out_shape=jax.ShapeDtypeStruct(start.shape, jnp.float32),
        compiler_params=pltpu.CompilerParams(dimension_semantics=("arbitrary",)),
    )(load, start)


def exchange_shares(block, axis):
    count = lax.axis_size(axis)
    index = lax.axis_index(axis)
    got = [jnp.take(block, index, axis=1)]
    for shift in range(1, count):
        route = [(j, (j + shift) % count) for j in range(count)]
        outgoing = jnp.take(block, (index + shift) % count, axis=1)
        got.append(lax.ppermute(outgoing, axis, route))
    stacked = jnp.stack(got)
    order = (index - jnp.arange(count, dtype=jnp.int32)) % count
    stacked = jnp.take(stacked, order, axis=0)
    return stacked.reshape((count * block.shape[0],) + block.shape[2:])


def cholesky_inverse_kernel(gram_ref, inverse_ref, work_ref, rest_ref):
    order = gram_ref.shape[0]
    tile = 16
    sub = lax.broadcasted_iota(jnp.int32, (order, order), 0)
    lane = lax.broadcasted_iota(jnp.int32, (order, order), 1)
    lane_one = lax.broadcasted_iota(jnp.int32, (1, order), 1)
    work_ref[...] = gram_ref[...]
    rest_ref[...] = jnp.where(sub == lane, 1.0, 0.0).astype(jnp.float32)
    inverse_ref[...] = jnp.zeros_like(inverse_ref)

    for first in range(0, order, tile):
        height = order - first
        tail_lane = lax.broadcasted_iota(jnp.int32, (height, order), 1)
        tail_sub = lax.broadcasted_iota(jnp.int32, (height, 1), 0) + first

        def step(j, carry, first=first, tail_lane=tail_lane, tail_sub=tail_sub):
            work = work_ref[first:, :]
            pivot_row = work_ref[pl.ds(j, 1), :]
            pivot = jnp.sum(jnp.where(lane_one == j, pivot_row, 0.0), axis=1, keepdims=True)
            column = jnp.sum(jnp.where(tail_lane == j, work, 0.0), axis=1, keepdims=True)
            scale = lax.rsqrt(pivot)
            column = jnp.where(tail_sub >= j, column * scale, 0.0)
            row = jnp.where(lane_one >= j, pivot_row * scale, 0.0)
            work_ref[first:, :] = work - column * row
            solved = rest_ref[pl.ds(j, 1), :] * scale
            inverse_ref[pl.ds(j, 1), :] = solved
            rest_ref[first:, :] = rest_ref[first:, :] - column * solved
            return carry

        lax.fori_loop(first, first + tile, step, 0, unroll=True)


def cholesky_inverse(gram_matrix):
    order = gram_matrix.shape[0]
    symmetric = (gram_matrix + gram_matrix.T) * 0.5
    return pl.pallas_call(
        cholesky_inverse_kernel,
        out_shape=jax.ShapeDtypeStruct((order, order), jnp.float32),
        scratch_shapes=[pltpu.VMEM((order, order), jnp.float32)] * 2,
    )(symmetric)


def basis_from_gram(sketched, gram_matrix, rank_limit):
    inverse = cholesky_inverse(gram_matrix)
    orthonormal = jnp.einsum("ra,ba->rb", sketched, inverse, precision=highest)
    columns = jnp.arange(sketched.shape[1], dtype=jnp.int32)
    return jnp.where(columns[None, :] < rank_limit, orthonormal, jnp.zeros_like(orthonormal))


def chol_basis(sketched, rank_limit):
    gram_matrix = jnp.einsum("ra,rb->ab", sketched, sketched, precision=highest)
    return basis_from_gram(sketched, gram_matrix, rank_limit)


def merge_level(own, partner, low_side, sketch_all, rank_limit):
    stacked = jnp.where(
        low_side,
        jnp.concatenate([own, partner], 1),
        jnp.concatenate([partner, own], 1),
    )
    sketched = jnp.einsum("pr,ps->rs", stacked, sketch_all, precision=highest)
    merged = chol_basis(sketched, rank_limit)
    return merged, jnp.dot(stacked, merged, precision=highest)


def on_device(
    child_updates,
    child_probes,
    child_dest,
    child_rows,
    parent_blocks,
    coupling,
    parent_probes,
    sketch,
    rank_one,
    rank_two,
    rank_three,
):
    leaf_count = lax.axis_size("leaf")
    probe_count = lax.axis_size("probe")
    leaf_index = lax.axis_index("leaf")
    probe_index = lax.axis_index("probe")
    local_probes = child_probes.shape[0]
    kid_count = child_updates.shape[0]
    kid_order = child_updates.shape[1]
    block_rows = child_rows.shape[1]
    block_count = child_rows.shape[0]
    front_rows = parent_probes.shape[1]
    rank_width = sketch.shape[1]

    updates = child_updates.reshape(kid_count, kid_order // block_rows, block_rows, kid_order)
    probe_cut = child_probes.reshape(local_probes, kid_count, kid_order)
    sampled = jnp.einsum("pck,cbik->cbpi", probe_cut, updates, preferred_element_type=jnp.float32)
    sampled = sampled.astype(jnp.bfloat16).reshape(block_count, local_probes, block_rows)

    targets = child_dest[:, 0]
    named = (targets[:, None] == jnp.arange(leaf_count, dtype=jnp.int32)[None, :]).astype(jnp.int32)
    earlier = jnp.cumsum(named, axis=0) - named
    slot = jnp.sum(earlier * named, axis=1)
    place = targets * SLOT_CAP + slot
    slot_count = leaf_count * SLOT_CAP
    source = jnp.full((slot_count,), block_count, jnp.int32).at[place].set(
        jnp.arange(block_count, dtype=jnp.int32)
    )
    filled = source < block_count
    source = jnp.minimum(source, block_count - 1)
    high = jnp.where(filled[:, None], child_rows[source] // block_rows, -1)
    low = jnp.where(filled[:, None], child_rows[source] % block_rows, 0)
    send_vals = jnp.take(sampled, source, axis=0)
    half = SLOT_CAP
    info_rows = 16
    loads = []
    for part in range(1):
        picked_slots = slice(part * half, (part + 1) * half)
        vals = send_vals.reshape(leaf_count, SLOT_CAP, local_probes, block_rows)[:, picked_slots]
        info = jnp.concatenate(
            [
                high.reshape(leaf_count, SLOT_CAP, block_rows)[:, picked_slots],
                low.reshape(leaf_count, SLOT_CAP, block_rows)[:, picked_slots],
                jnp.zeros((leaf_count, info_rows - 2 * half, block_rows), jnp.int32),
            ],
            axis=1,
        ).astype(jnp.bfloat16)
        load = jnp.concatenate(
            [vals.reshape(leaf_count, half * local_probes, block_rows), info], axis=1
        )
        loads.append(lax.all_to_all(load, "leaf", 0, 0, tiled=True))

    pieces = parent_probes.reshape(local_probes, front_rows // block_rows, block_rows)
    picked = jnp.take(pieces, coupling[:, 1], axis=1)
    product = jnp.einsum("eik,pek->pei", parent_blocks, picked, preferred_element_type=jnp.float32)
    initial = (
        jnp.zeros(pieces.shape, jnp.float32)
        .at[:, coupling[:, 0]]
        .add(product)
        .reshape(local_probes, front_rows)
    )
    width = 4 * block_rows
    high_count = front_rows // width
    spread = jnp.moveaxis(initial.reshape(local_probes, high_count, width), 1, 0)
    spread = spread.reshape(high_count * local_probes, width)
    for load in loads:
        spread = extend_add(load, spread, half, local_probes)
    spread = spread.reshape(high_count, local_probes, width)
    sample = jnp.moveaxis(spread, 0, 1).reshape(local_probes, front_rows)

    share_rows = front_rows // probe_count
    sketch_all = gather_rows(sketch, "probe")
    share_sample = exchange_shares(sample.reshape(local_probes, probe_count, share_rows), "probe")
    share_sketched = jnp.einsum("pr,ps->rs", share_sample, sketch_all, precision=highest)
    gram_one = ordered_sum(
        jnp.einsum("ra,rb->ab", share_sketched, share_sketched, precision=highest), "probe"
    )
    own_basis = basis_from_gram(share_sketched, gram_one, rank_one[0])
    passed_one = ordered_sum(jnp.dot(share_sample, own_basis, precision=highest), "probe")

    pair_bit = leaf_index % 2
    merged_two, passed_two = merge_level(
        passed_one, partner_2(passed_one, "leaf", 0), pair_bit == 0, sketch_all, rank_two[leaf_index // 2]
    )
    quad_bit = leaf_index // 2 % 2
    merged_three, passed_three = merge_level(
        passed_two, partner_2(passed_two, "leaf", 1), quad_bit == 0, sketch_all, rank_three[leaf_index // 4]
    )
    basis_two = lax.dynamic_slice_in_dim(merged_two, pair_bit * rank_width, rank_width, 0)
    basis_three = lax.dynamic_slice_in_dim(merged_three, quad_bit * rank_width, rank_width, 0)
    top = lax.dynamic_slice_in_dim(passed_three, probe_index * local_probes, local_probes, 0)
    return (own_basis, basis_two, basis_three, top)


def solution(mesh):
    return jax.shard_map(
        on_device,
        mesh=mesh,
        in_specs=(
            P("leaf", None, None),
            P("probe", "leaf"),
            P("leaf", None),
            P("leaf", None),
            P("leaf", None, None),
            P("leaf", None),
            P("probe", "leaf"),
            P("probe", None),
            P("leaf"),
            P(),
            P(),
        ),
        out_specs=(
            P(("leaf", "probe"), None),
            P("leaf", None),
            P("leaf", None),
            P("probe", "leaf"),
        ),
        check_vma=False,
    )
```
